32 devices in a mesh: grp: 2 (over y), lat: 4 (over z), lon: 4 (over x, core).
Axes of the slice: x: 2, y: 2, z: 4, core: 2. Of those that a mesh axis runs over, the one named last changes fastest.
Arguments:
- inputs: bfloat16 [2, 16, 256, 256], P('grp', 'lat', 'lon'), parts along dimension 0, may hold values from -6 to 6
- cotangent: bfloat16 [2, 16, 256, 256], P('grp', 'lat', 'lon'), parts along dimension 0, may hold values from -6 to 6
- weight: bfloat16 [9, 256, 256], replicated, may hold values from -0.125 to 0.125
- src_rows: int32 [16, 12], replicated, may hold values from 0 to 15, as said below
- lon_start: int32 [16, 12], replicated, may hold values from -16 to 16, as said below
- lon_span: int32 [16, 12], replicated, may hold values from 1 to 256, as said below
- basis_idx: int32 [16, 12], replicated, may hold values from 0 to 8, as said below
- quad_weight: float32 [16, 12], replicated, may hold values from -4 to 4
Outputs:
- response: float32 [2, 16, 256, 256], P('grp', 'lat', 'lon'), parts along dimension 0
- grad_input: float32 [2, 16, 256, 256], P('grp', 'lat', 'lon'), parts along dimension 0
- grad_weight: float32 [18, 256, 256], P('grp', 'lat', 'lon'), parts along dimension 0
The draws below stay inside these ranges and needn't reach their ends.
There are 2 independent parts, one for each index of `grp`. The reference program is written for one: setup_inputs(seed, part) draws one part's arguments, and reference() takes and returns one part's arrays. A program takes and returns all parts, laid end to end along the dimension named above; an argument that names none is the same for every part. Nothing has to cross between parts.
Inputs may be any that keep to these rules, and one draw needn't show every extreme that they name: `src_rows`: each entry's input row lies within 2 rows of its output row; every row has entries reaching exactly 2 rows up and down, clipped at the grid's edges. `lon_start`: for an entry with span 256 the start is 0; otherwise the range lies within 16 longitudes of the output longitude on either side. `lon_span`: either 256 (a full circle, only in the first and last 2 rows) or at most 33. `basis_idx`: every basis function appears in every row.
All inputs are finite; a program needn't handle non-finite values.
Results may differ from the reference program's by a relative error of at most 0.01.
Values may be sent and summed in bfloat16 or wider, within the bound.
No kernel may reach another device: no remote copies, remote signals or barrier semaphores. Data moves between devices by JAX's collectives and lax.ppermute only.
A program may use at most 64 MiB of HBM per device.

```python
import jax
import jax.numpy as jnp
from jax import lax

MEMBERS = 1
CH = 256
BASIS = 9
SLOTS = 12
REACH = 2
RIM = 16
POLAR = 2
LAT_ROWS = 16
LON_CELLS = 256


def stencil_tables(key):
    root_key = jax.random.fold_in(key, 7)
    k_step, k_span, k_shift, k_basis = jax.random.split(root_key, 4)
    row_ids = jnp.arange(LAT_ROWS, dtype=jnp.int32)[:, None]
    slot_ids = jnp.arange(SLOTS, dtype=jnp.int32)[None, :]
    shape = (LAT_ROWS, SLOTS)
    steps = jax.random.randint(k_step, shape, -REACH, REACH + 1)
    steps = jnp.where(slot_ids == 2, -REACH, jnp.where(slot_ids == 3, REACH, steps))
    sources = jnp.clip(row_ids + steps, 0, LAT_ROWS - 1).astype(jnp.int32)
    spans = jax.random.randint(k_span, shape, 1, 2 * RIM + 2)
    spans = jnp.where(slot_ids == 1, 2 * RIM + 1, spans)
    spans = jnp.where(slot_ids == 4, 1, spans)
    shifts = jax.random.randint(k_shift, shape, 0, 2 * RIM + 1)
    shifts = jnp.where(slot_ids == 4, 2 * RIM, shifts)
    starts = -RIM + shifts % (2 * RIM + 2 - spans)
    polar = (row_ids < POLAR) | (row_ids >= LAT_ROWS - POLAR)
    full_cycle = polar & (slot_ids % 3 == 0)
    spans = jnp.where(full_cycle, LON_CELLS, spans).astype(jnp.int32)
    starts = jnp.where(full_cycle, 0, starts).astype(jnp.int32)
    drawn_basis = jax.random.randint(k_basis, shape, 0, BASIS)
    bases = jnp.where(slot_ids < BASIS, slot_ids + 0 * row_ids, drawn_basis).astype(jnp.int32)
    return (sources, starts, spans, bases)


def draw_src_rows(key, part):
    return stencil_tables(key)[0]


def draw_lon_start(key, part):
    return stencil_tables(key)[1]


def draw_lon_span(key, part):
    return stencil_tables(key)[2]


def draw_basis_idx(key, part):
    return stencil_tables(key)[3]


def raised(drawn, rng, source, target, blocks, factor):
    def block_of(position):
        return (jnp.arange(drawn.shape[position]) // (drawn.shape[position] // blocks)).reshape((-1,) + (1,) * (drawn.ndim - 1 - position))

    first = jax.random.permutation(rng, blocks)[block_of(target)]
    far = (block_of(target) + blocks // 2) % blocks
    return jnp.where((block_of(source) == first) | (block_of(source) == far), factor * drawn, drawn)


def steps_of(rng, dims, shards, least, high):
    factor_of = 1.0
    for axis_at, blocks in shards:
        heights = jax.random.uniform(jax.random.fold_in(jax.random.fold_in(rng, 6), axis_at), (blocks,), jnp.float32, least / len(shards), high / len(shards))
        factor_of = factor_of * jnp.repeat(jnp.exp(heights), dims[axis_at] // blocks).reshape((-1,) + (1,) * (len(dims) - 1 - axis_at))
    return factor_of


def scatter_about(own_key, dims, width, reach, cuts=(), kind=jnp.bfloat16):
    level = steps_of(own_key, dims, cuts, -0.22, 0.18) if cuts else 1.0
    array = jax.random.normal(own_key, dims, jnp.float32) * width * level
    return jnp.minimum(jnp.maximum(array, -reach), reach).astype(kind)


def bell_draw_with(own_key, dims, scale, bound, shards, heavy, kind=jnp.bfloat16):
    array = scale * jax.random.normal(own_key, dims, jnp.float32)
    if shards:
        array = array * steps_of(own_key, dims, shards, -0.22, 0.18)
    return jnp.clip(raised(array, jax.random.fold_in(own_key, 3), *heavy), -bound, bound).astype(kind)


def setup_inputs(seed: int = 0, part: int = 0) -> dict:
    splits = jax.random.split(jax.random.key(seed), 9)
    part_splits = jax.random.split(jax.random.fold_in(splits[8], part), 9)
    inputs = bell_draw_with(part_splits[0], (MEMBERS, LAT_ROWS, LON_CELLS, CH), 1.0, 6.0, ((1, 4), (2, 4)), (1, 3, 4, 2.0))
    cotangent = scatter_about(part_splits[1], (MEMBERS, LAT_ROWS, LON_CELLS, CH), 1.0, 6.0, ((1, 4), (2, 4)))
    weight = scatter_about(splits[2], (BASIS, CH, CH), (BASIS * CH) ** -0.5, 0.125)
    src_rows = draw_src_rows(jax.random.fold_in(splits[8], 71), part)
    lon_start = draw_lon_start(jax.random.fold_in(splits[8], 71), part)
    lon_span = draw_lon_span(jax.random.fold_in(splits[8], 71), part)
    basis_idx = draw_basis_idx(jax.random.fold_in(splits[8], 71), part)
    quad_weight = scatter_about(splits[7], (LAT_ROWS, SLOTS), 1.0, 4.0, (), jnp.float32)
    return dict(inputs=inputs, cotangent=cotangent, weight=weight, src_rows=src_rows, lon_start=lon_start, lon_span=lon_span, basis_idx=basis_idx, quad_weight=quad_weight)


def prefix_table(grid_rows):
    doubled = jnp.concatenate([grid_rows, grid_rows], axis=2).astype(jnp.float32)
    summed = jnp.cumsum(doubled, axis=2)
    return jnp.concatenate([jnp.zeros_like(summed[:, :, :1]), summed], axis=2)

def reference(inputs, cotangent, weight, src_rows, lon_start, lon_span, basis_idx, quad_weight):
    members, height, lon_total, channels = inputs.shape
    weighting = quad_weight / jnp.sqrt(lon_span.astype(jnp.float32))
    basis_ids = jnp.arange(BASIS, dtype=jnp.int32)
    mixing_all = weighting[:, :, None] * (basis_idx[:, :, None] == basis_ids[None, None, :]).astype(jnp.float32)
    w_fwd = weight.reshape(BASIS * channels, channels)
    w_back = jnp.transpose(weight, (0, 2, 1)).reshape(BASIS * channels, channels)
    columns = jnp.arange(lon_total, dtype=jnp.int32)
    slot_ids = jnp.arange(SLOTS, dtype=jnp.int32)

    def forward_row(carried, out_row):
        sources = src_rows[out_row]
        starts = lon_start[out_row]
        spans = lon_span[out_row]
        picked = jnp.take(inputs, sources, axis=1)
        table = prefix_table(picked)
        begin = (columns[None, :] + starts[:, None]) % lon_total
        boxed = table[:, slot_ids[:, None], begin + spans[:, None], :] - table[:, slot_ids[:, None], begin, :]
        filtered = jnp.einsum('bswc,sk->bwkc', boxed, mixing_all[out_row]).astype(jnp.bfloat16)
        flattened = filtered.reshape(members * lon_total, BASIS * channels)
        response_row = jnp.dot(flattened, w_fwd, preferred_element_type=jnp.float32)
        grad_rows = cotangent[:, out_row].reshape(members * lon_total, channels)
        carried = carried + jnp.dot(flattened.T, grad_rows, preferred_element_type=jnp.float32)
        return (carried, response_row.reshape(members, lon_total, channels))
    start_grad = jnp.zeros((BASIS * channels, channels), jnp.float32)
    summed_grad, response_rows = lax.scan(forward_row, start_grad, jnp.arange(height, dtype=jnp.int32))
    response = jnp.moveaxis(response_rows, 0, 1)
    grad_weight = (summed_grad / jnp.sqrt(jnp.float32(members * height * lon_total))).reshape(BASIS, channels, channels)
    pad_pair = ((REACH, REACH), (0, 0))
    padded_grad = jnp.pad(cotangent, ((0, 0), (REACH, REACH), (0, 0), (0, 0)))
    padded_src = jnp.pad(src_rows, pad_pair, constant_values=-1)
    padded_start = jnp.pad(lon_start, pad_pair, constant_values=0)
    padded_span = jnp.pad(lon_span, pad_pair, constant_values=1)
    padded_mixing = jnp.pad(mixing_all, ((REACH, REACH), (0, 0), (0, 0)))
    window_rows = 2 * REACH + 1
    ext_ids = jnp.arange(window_rows, dtype=jnp.int32)[:, None, None]

    def backward_row(src_row):
        grad_rows = lax.dynamic_slice_in_dim(padded_grad, src_row, window_rows, 1)
        sources = lax.dynamic_slice_in_dim(padded_src, src_row, window_rows, 0)
        starts = lax.dynamic_slice_in_dim(padded_start, src_row, window_rows, 0)
        spans = lax.dynamic_slice_in_dim(padded_span, src_row, window_rows, 0)
        mixing_rows = lax.dynamic_slice_in_dim(padded_mixing, src_row, window_rows, 0)
        table = prefix_table(grad_rows)
        begin = (columns[None, None, :] - starts[:, :, None] - spans[:, :, None] + 1) % lon_total
        boxed = table[:, ext_ids, begin + spans[:, :, None], :] - table[:, ext_ids, begin, :]
        mixing = mixing_rows * (sources == src_row).astype(jnp.float32)[:, :, None]
        back = jnp.einsum('beswc,esk->bwkc', boxed, mixing).astype(jnp.bfloat16)
        flattened = back.reshape(members * lon_total, BASIS * channels)
        grad_row = jnp.dot(flattened, w_back, preferred_element_type=jnp.float32)
        return grad_row.reshape(members, lon_total, channels)
    grad_input = jnp.moveaxis(lax.map(backward_row, jnp.arange(height, dtype=jnp.int32)), 0, 1)
    return (response, grad_input, grad_weight)
```

```python
import jax
import jax.numpy as jnp
from jax import lax
from jax.sharding import PartitionSpec as P

BASIS = 9
REACH = 2
RIM = 16
HIGH = lax.Precision.HIGHEST


def with_halo(block, sides, width, periodic):
    for axis, dim in sides:
        count = lax.axis_size(axis)
        forward = [(i, i + 1) for i in range(count - 1)]
        if periodic:
            forward.append((count - 1, 0))
        backward = [(target, source) for source, target in forward]
        low = lax.ppermute(
            lax.slice_in_dim(block, block.shape[dim] - width, None, axis=dim), axis, forward
        )
        high = lax.ppermute(lax.slice_in_dim(block, 0, width, axis=dim), axis, backward)
        block = jnp.concatenate([low, block, high], axis=dim)
    return block


def extend(grid_field):
    grid_field = with_halo(grid_field, (("lat", 1),), REACH, False)
    return with_halo(grid_field, (("lon", 2),), RIM, True)


def cycle_totals(widened, lon_count):
    interior = lax.slice_in_dim(widened, RIM, RIM + lon_count, axis=2)
    return lax.psum(jnp.sum(interior, axis=2, dtype=jnp.float32), "lon")


def split_dot(spec, coef, field):
    high = coef.astype(jnp.bfloat16)
    low = (coef - high.astype(jnp.float32)).astype(jnp.bfloat16)
    first = jnp.einsum(spec, high, field, preferred_element_type=jnp.float32)
    return first + jnp.einsum(spec, low, field, preferred_element_type=jnp.float32)


def on_device(inputs, cotangent, weight, src_rows, lon_start, lon_span, basis_idx, quad_weight):
    members, row_count, lon_count, channels = inputs.shape
    lon_total = lon_count * lax.axis_size("lon")
    height = row_count * lax.axis_size("lat")
    first_row = lax.axis_index("lat") * row_count
    extent = lon_count + 2 * RIM
    window = row_count + 2 * REACH
    weighting = quad_weight / jnp.sqrt(lon_span.astype(jnp.float32))
    basis_ids = jnp.arange(BASIS, dtype=jnp.int32)
    win_ids = jnp.arange(window, dtype=jnp.int32)
    wide_cols = jnp.arange(extent, dtype=jnp.int32)[:, None] - RIM
    own_cols = jnp.arange(lon_count, dtype=jnp.int32)[None, :]
    offsets = wide_cols - own_cols

    widened = extend(inputs)
    grad_wide = extend(cotangent)
    totals = cycle_totals(widened, lon_count)
    grad_totals = cycle_totals(grad_wide, lon_count)

    def rows_of(table, begin, count):
        return lax.dynamic_slice_in_dim(table, begin, count, 0)

    f_src = rows_of(src_rows, first_row, row_count)
    f_start = rows_of(lon_start, first_row, row_count)[:, :, None, None]
    f_span = rows_of(lon_span, first_row, row_count)
    f_basis = rows_of(basis_idx, first_row, row_count)
    f_scale = rows_of(weighting, first_row, row_count)
    f_full = f_span == lon_total
    f_band = (
        (offsets >= f_start)
        & (offsets < f_start + f_span[:, :, None, None])
        & ~f_full[:, :, None, None]
    ).astype(jnp.float32)
    f_mix = f_scale[:, :, None] * (f_basis[:, :, None] == basis_ids).astype(jnp.float32)
    f_sel = ((f_src - first_row + REACH)[:, :, None] == win_ids).astype(jnp.float32)
    f_mixsel = f_mix[:, :, None, :] * f_sel[:, :, :, None]
    f_coef = jnp.einsum("rshk,rsvw->rkhvw", f_mixsel, f_band, precision=HIGH)
    f_cycle = jnp.einsum("rshk,rs->rkh", f_mixsel, f_full.astype(jnp.float32), precision=HIGH)
    filt = split_dot("rkhvw,bhvc->brwkc", f_coef, widened)
    filt = filt + jnp.einsum("rkh,bhc->brkc", f_cycle, totals, precision=HIGH)[:, :, None]
    filtered = filt.astype(jnp.bfloat16)
    flattened = filtered.reshape(members, row_count, lon_count, BASIS * channels)
    w_fwd = weight.reshape(BASIS * channels, channels)
    response = jnp.einsum("brwq,qo->brwo", flattened, w_fwd, preferred_element_type=jnp.float32)

    pad_pair = ((REACH, REACH), (0, 0))
    begin = first_row
    b_src = rows_of(jnp.pad(src_rows, pad_pair, constant_values=-1), begin, window)
    b_start = rows_of(jnp.pad(lon_start, pad_pair, constant_values=0), begin, window)
    b_span = rows_of(jnp.pad(lon_span, pad_pair, constant_values=1), begin, window)
    b_basis = rows_of(jnp.pad(basis_idx, pad_pair, constant_values=0), begin, window)
    b_scale = rows_of(jnp.pad(weighting, pad_pair, constant_values=0.0), begin, window)
    b_full = b_span == lon_total
    back_offsets = -offsets
    b_band = (
        (back_offsets >= b_start[:, :, None, None])
        & (back_offsets < (b_start + b_span)[:, :, None, None])
        & ~b_full[:, :, None, None]
    ).astype(jnp.float32)
    targets = first_row + jnp.arange(row_count, dtype=jnp.int32)
    b_hit = (b_src[None, :, :] == targets[:, None, None]).astype(jnp.float32)
    b_pick = (b_basis[:, :, None] == basis_ids).astype(jnp.float32)
    b_mix = (b_scale[None, :, :] * b_hit)[:, :, :, None] * b_pick[None]
    b_coef = jnp.einsum("phsk,hsvw->pkhvw", b_mix, b_band, precision=HIGH)
    b_cycle = jnp.einsum("phsk,hs->pkh", b_mix, b_full.astype(jnp.float32), precision=HIGH)
    back = split_dot("pkhvw,bhvo->bpwko", b_coef, grad_wide)
    back = back + jnp.einsum("pkh,bho->bpko", b_cycle, grad_totals, precision=HIGH)[:, :, None]
    back_filtered = back.astype(jnp.bfloat16).reshape(
        members, row_count, lon_count, BASIS * channels
    )
    w_back = jnp.transpose(weight, (0, 2, 1)).reshape(BASIS * channels, channels)
    grad_input = jnp.einsum(
        "bpwq,qc->bpwc", back_filtered, w_back, preferred_element_type=jnp.float32
    )
    partial_value = jnp.einsum(
        "brwq,brwo->qo", flattened, cotangent, preferred_element_type=jnp.float32
    )
    partial_value = partial_value.reshape(BASIS, channels, channels)
    reduced = lax.psum_scatter(partial_value, "lon", scatter_dimension=2, tiled=True)
    reduced = lax.psum_scatter(reduced, "lat", scatter_dimension=1, tiled=True)
    grad_weight = reduced / jnp.sqrt(jnp.float32(members * height * lon_total))
    return (response, grad_input, grad_weight)


def solution(mesh):
    placed = (
        P("grp", "lat", "lon", None),
        P("grp", "lat", "lon", None),
        P(),
        P(),
        P(),
        P(),
        P(),
        P(),
    )
    return jax.shard_map(
        on_device,
        mesh=mesh,
        in_specs=placed,
        out_specs=(
            P("grp", "lat", "lon", None),
            P("grp", "lat", "lon", None),
            P("grp", "lat", "lon"),
        ),
        check_vma=False,
    )
```

```python
import functools

import jax
import jax.numpy as jnp
from jax import lax
from jax.experimental import pallas as pl
from jax.experimental.pallas import tpu as pltpu
from jax.sharding import PartitionSpec as P

BASIS = 9
REACH = 2
RIM = 16


def with_halo(block, sides, width, periodic):
    for axis, dim in sides:
        count = lax.axis_size(axis)
        forward = [(i, i + 1) for i in range(count - 1)]
        if periodic:
            forward.append((count - 1, 0))
        backward = [(target, source) for source, target in forward]
        low = lax.ppermute(
            lax.slice_in_dim(block, block.shape[dim] - width, None, axis=dim), axis, forward
        )
        high = lax.ppermute(lax.slice_in_dim(block, 0, width, axis=dim), axis, backward)
        block = jnp.concatenate([low, block, high], axis=dim)
    return block


def extend(grid_field, padded):
    grid_field = with_halo(grid_field, (("lat", 1),), REACH, False)
    grid_field = with_halo(grid_field, (("lon", 2),), RIM, True)
    extra = padded - grid_field.shape[2]
    return jnp.pad(grid_field, ((0, 0), (0, 0), (0, extra), (0, 0)))


def cycle_totals(widened, lon_count):
    interior = lax.slice_in_dim(widened, RIM, RIM + lon_count, axis=2)
    return lax.psum(jnp.sum(interior, axis=2, dtype=jnp.float32), "lon")


def filter_kernel(
    rows_ref, start_ref, span_ref, basis_ref, scale_ref, field_ref, total_ref, out_ref, acc_ref,
    *, slots, window_rows, lon_count, lon_total, backward,
):
    r = pl.program_id(1)
    padded = field_ref.shape[2]
    channels = field_ref.shape[3]
    acc_ref[...] = jnp.zeros(acc_ref.shape, jnp.float32)
    out_col = lax.broadcasted_iota(jnp.int32, (lon_count, padded), 0)
    in_col = lax.broadcasted_iota(jnp.int32, (lon_count, padded), 1) - RIM
    offset = out_col - in_col if backward else in_col - out_col

    def add_slot(row, table_row, slot, scale):
        start = start_ref[table_row, slot]
        span = span_ref[table_row, slot]
        basis = basis_ref[table_row, slot]
        narrow = span < lon_total
        band = ((offset >= start) & (offset < start + span) & narrow).astype(jnp.bfloat16)
        boxed = jnp.dot(band, field_ref[0, row], preferred_element_type=jnp.float32)
        full = jnp.where(narrow, 0.0, 1.0).astype(jnp.float32)
        boxed = boxed + full * total_ref[0, row]
        acc_ref[basis] = acc_ref[basis] + scale * boxed

    if backward:
        for e in range(window_rows):
            row = r + e
            for slot in range(slots):
                scale = scale_ref[r, row * slots + slot]

                @pl.when(scale != 0.0)
                def _():
                    add_slot(row, row, slot, scale)
    else:
        for slot in range(slots):
            add_slot(rows_ref[r, slot], r, slot, scale_ref[r, slot])

    for k in range(BASIS):
        out_ref[0, 0, :, k * channels:(k + 1) * channels] = acc_ref[k].astype(jnp.bfloat16)


def run_filter(tables, field, totals, lon_count, lon_total, backward):
    members, window, padded, channels = field.shape
    row_count = window - 2 * REACH
    slots = tables[1].shape[1]
    smem = pl.BlockSpec(memory_space=pltpu.SMEM)
    kernel = functools.partial(
        filter_kernel,
        slots=slots,
        window_rows=2 * REACH + 1,
        lon_count=lon_count,
        lon_total=lon_total,
        backward=backward,
    )
    return pl.pallas_call(
        kernel,
        grid=(members, row_count),
        in_specs=[smem] * 5
        + [
            pl.BlockSpec((1, window, padded, channels), lambda b, r: (b, 0, 0, 0)),
            pl.BlockSpec((1, window, 1, channels), lambda b, r: (b, 0, 0, 0)),
        ],
        out_specs=pl.BlockSpec(
            (1, 1, lon_count, BASIS * channels), lambda b, r: (b, r, 0, 0)
        ),
        out_shape=jax.ShapeDtypeStruct(
            (members, row_count, lon_count, BASIS * channels), jnp.bfloat16
        ),
        scratch_shapes=[pltpu.VMEM((BASIS, lon_count, channels), jnp.float32)],
    )(*tables, field, totals[:, :, None, :])


def on_device(inputs, cotangent, weight, src_rows, lon_start, lon_span, basis_idx, quad_weight):
    members, row_count, lon_count, channels = inputs.shape
    lon_total = lon_count * lax.axis_size("lon")
    height = row_count * lax.axis_size("lat")
    first_row = lax.axis_index("lat") * row_count
    window = row_count + 2 * REACH
    padded = -(-(lon_count + 2 * RIM) // 128) * 128
    weighting = quad_weight / jnp.sqrt(lon_span.astype(jnp.float32))

    widened = extend(inputs, padded)
    grad_wide = extend(cotangent, padded)
    totals = cycle_totals(widened, lon_count)
    grad_totals = cycle_totals(grad_wide, lon_count)

    def rows_of(table, begin, count):
        return lax.dynamic_slice_in_dim(table, begin, count, 0)

    f_tables = (
        rows_of(src_rows, first_row, row_count) - first_row + REACH,
        rows_of(lon_start, first_row, row_count),
        rows_of(lon_span, first_row, row_count),
        rows_of(basis_idx, first_row, row_count),
        rows_of(weighting, first_row, row_count),
    )
    flattened = run_filter(f_tables, widened, totals, lon_count, lon_total, False)
    w_fwd = weight.reshape(BASIS * channels, channels)
    response = jnp.einsum("brwq,qo->brwo", flattened, w_fwd, preferred_element_type=jnp.float32)

    pad_pair = ((REACH, REACH), (0, 0))
    b_src = rows_of(jnp.pad(src_rows, pad_pair, constant_values=-1), first_row, window)
    b_start = rows_of(jnp.pad(lon_start, pad_pair, constant_values=0), first_row, window)
    b_span = rows_of(jnp.pad(lon_span, pad_pair, constant_values=1), first_row, window)
    b_basis = rows_of(jnp.pad(basis_idx, pad_pair, constant_values=0), first_row, window)
    b_scale = rows_of(jnp.pad(weighting, pad_pair, constant_values=0.0), first_row, window)
    targets = first_row + jnp.arange(row_count, dtype=jnp.int32)
    b_hit = b_src[None, :, :] == targets[:, None, None]
    b_weights = jnp.where(b_hit, b_scale[None], 0.0).reshape(row_count, -1)
    b_tables = (b_src, b_start, b_span, b_basis, b_weights)
    back_filtered = run_filter(b_tables, grad_wide, grad_totals, lon_count, lon_total, True)
    w_back = jnp.transpose(weight, (0, 2, 1)).reshape(BASIS * channels, channels)
    grad_input = jnp.einsum(
        "bpwq,qc->bpwc", back_filtered, w_back, preferred_element_type=jnp.float32
    )
    partial_value = jnp.einsum(
        "brwq,brwo->qo", flattened, cotangent, preferred_element_type=jnp.float32
    )
    partial_value = partial_value.reshape(BASIS, channels, channels)
    reduced = lax.psum_scatter(partial_value, "lon", scatter_dimension=2, tiled=True)
    reduced = lax.psum_scatter(reduced, "lat", scatter_dimension=1, tiled=True)
    grad_weight = reduced / jnp.sqrt(jnp.float32(members * height * lon_total))
    return (response, grad_input, grad_weight)


def solution(mesh):
    placed = (
        P("grp", "lat", "lon", None),
        P("grp", "lat", "lon", None),
        P(),
        P(),
        P(),
        P(),
        P(),
        P(),
    )
    return jax.shard_map(
        on_device,
        mesh=mesh,
        in_specs=placed,
        out_specs=(
            P("grp", "lat", "lon", None),
            P("grp", "lat", "lon", None),
            P("grp", "lat", "lon"),
        ),
        check_vma=False,
    )
```

```python
import functools

import jax
import jax.numpy as jnp
from jax import lax
from jax.experimental import pallas as pl
from jax.experimental.pallas import tpu as pltpu
from jax.sharding import PartitionSpec as P

BASIS = 9
REACH = 2
RIM = 16


def with_halo(block, sides, width, periodic):
    for axis, dim in sides:
        count = lax.axis_size(axis)
        forward = [(i, i + 1) for i in range(count - 1)]
        if periodic:
            forward.append((count - 1, 0))
        backward = [(target, source) for source, target in forward]
        low = lax.ppermute(
            lax.slice_in_dim(block, block.shape[dim] - width, None, axis=dim), axis, forward
        )
        high = lax.ppermute(lax.slice_in_dim(block, 0, width, axis=dim), axis, backward)
        block = jnp.concatenate([low, block, high], axis=dim)
    return block


def extend(grid_field, padded):
    grid_field = with_halo(grid_field, (("lat", 1),), REACH, False)
    grid_field = with_halo(grid_field, (("lon", 2),), RIM, True)
    extra = padded - grid_field.shape[2]
    return jnp.pad(grid_field, ((0, 0), (0, 0), (0, extra), (0, 0)))


def filter_kernel(
    rows_ref, start_ref, span_ref, basis_ref, scale_ref, field_ref, total_ref, out_ref, acc_ref,
    *, slots, window_rows, lon_count, lon_total, backward,
):
    r = pl.program_id(1)
    padded = field_ref.shape[2]
    channels = field_ref.shape[3]
    acc_ref[...] = jnp.zeros(acc_ref.shape, jnp.float32)
    out_col = lax.broadcasted_iota(jnp.int32, (lon_count, padded), 0)
    in_col = lax.broadcasted_iota(jnp.int32, (lon_count, padded), 1) - RIM
    offset = out_col - in_col if backward else in_col - out_col

    def add_slot(row, table_row, slot, scale):
        start = start_ref[table_row, slot]
        span = span_ref[table_row, slot]
        basis = basis_ref[table_row, slot]
        narrow = span < lon_total
        band = ((offset >= start) & (offset < start + span) & narrow).astype(jnp.bfloat16)
        boxed = jnp.dot(band, field_ref[0, row], preferred_element_type=jnp.float32)
        full = jnp.where(narrow, 0.0, 1.0).astype(jnp.float32)
        boxed = boxed + full * total_ref[0, row]
        acc_ref[basis] = acc_ref[basis] + scale * boxed

    if backward:
        for e in range(window_rows):
            row = r + e
            for slot in range(slots):
                scale = scale_ref[r, row * slots + slot]

                @pl.when(scale != 0.0)
                def _():
                    add_slot(row, row, slot, scale)
    else:
        for slot in range(slots):
            add_slot(rows_ref[r, slot], r, slot, scale_ref[r, slot])

    for k in range(BASIS):
        out_ref[0, 0, :, k * channels:(k + 1) * channels] = acc_ref[k].astype(jnp.bfloat16)


def run_filter(tables, field, totals, lon_count, lon_total, backward):
    members, window, padded, channels = field.shape
    row_count = window - 2 * REACH
    slots = tables[1].shape[1]
    smem = pl.BlockSpec(memory_space=pltpu.SMEM)
    kernel = functools.partial(
        filter_kernel,
        slots=slots,
        window_rows=2 * REACH + 1,
        lon_count=lon_count,
        lon_total=lon_total,
        backward=backward,
    )
    return pl.pallas_call(
        kernel,
        grid=(members, row_count),
        in_specs=[smem] * 5
        + [
            pl.BlockSpec((1, window, padded, channels), lambda b, r: (b, 0, 0, 0)),
            pl.BlockSpec((1, window, 1, channels), lambda b, r: (b, 0, 0, 0)),
        ],
        out_specs=pl.BlockSpec(
            (1, 1, lon_count, BASIS * channels), lambda b, r: (b, r, 0, 0)
        ),
        out_shape=jax.ShapeDtypeStruct(
            (members, row_count, lon_count, BASIS * channels), jnp.bfloat16
        ),
        scratch_shapes=[pltpu.VMEM((BASIS, lon_count, channels), jnp.float32)],
    )(*tables, field, totals[:, :, None, :])


def on_device(inputs, cotangent, weight, src_rows, lon_start, lon_span, basis_idx, quad_weight):
    members, row_count, lon_count, channels = inputs.shape
    lon_total = lon_count * lax.axis_size("lon")
    height = row_count * lax.axis_size("lat")
    first_row = lax.axis_index("lat") * row_count
    window = row_count + 2 * REACH
    padded = -(-(lon_count + 2 * RIM) // 128) * 128
    weighting = quad_weight / jnp.sqrt(lon_span.astype(jnp.float32))

    widened = extend(inputs, padded)
    grad_wide = extend(cotangent, padded)
    row_sums = jnp.stack(
        [jnp.sum(inputs, axis=2, dtype=jnp.float32), jnp.sum(cotangent, axis=2, dtype=jnp.float32)]
    )
    gathered = lax.all_gather(row_sums, ("lat", "lon"), tiled=False)
    lat_count = lax.axis_size("lat")
    gathered = gathered.reshape((lat_count, lax.axis_size("lon")) + row_sums.shape)
    whole = jnp.sum(gathered, axis=1)
    whole = jnp.moveaxis(whole, 0, 2).reshape(2, members, height, channels)
    whole = jnp.pad(whole, ((0, 0), (0, 0), (REACH, REACH), (0, 0)))
    totals, grad_totals = lax.dynamic_slice_in_dim(whole, first_row, window, 2)

    def rows_of(table, begin, count):
        return lax.dynamic_slice_in_dim(table, begin, count, 0)

    f_tables = (
        rows_of(src_rows, first_row, row_count) - first_row + REACH,
        rows_of(lon_start, first_row, row_count),
        rows_of(lon_span, first_row, row_count),
        rows_of(basis_idx, first_row, row_count),
        rows_of(weighting, first_row, row_count),
    )
    flattened = run_filter(f_tables, widened, totals, lon_count, lon_total, False)
    w_fwd = weight.reshape(BASIS * channels, channels)
    response = jnp.einsum("brwq,qo->brwo", flattened, w_fwd, preferred_element_type=jnp.float32)

    pad_pair = ((REACH, REACH), (0, 0))
    b_src = rows_of(jnp.pad(src_rows, pad_pair, constant_values=-1), first_row, window)
    b_start = rows_of(jnp.pad(lon_start, pad_pair, constant_values=0), first_row, window)
    b_span = rows_of(jnp.pad(lon_span, pad_pair, constant_values=1), first_row, window)
    b_basis = rows_of(jnp.pad(basis_idx, pad_pair, constant_values=0), first_row, window)
    b_scale = rows_of(jnp.pad(weighting, pad_pair, constant_values=0.0), first_row, window)
    targets = first_row + jnp.arange(row_count, dtype=jnp.int32)
    b_hit = b_src[None, :, :] == targets[:, None, None]
    b_weights = jnp.where(b_hit, b_scale[None], 0.0).reshape(row_count, -1)
    b_tables = (b_src, b_start, b_span, b_basis, b_weights)
    back_filtered = run_filter(b_tables, grad_wide, grad_totals, lon_count, lon_total, True)
    w_back = jnp.transpose(weight, (0, 2, 1)).reshape(BASIS * channels, channels)
    grad_input = jnp.einsum(
        "bpwq,qc->bpwc", back_filtered, w_back, preferred_element_type=jnp.float32
    )
    lon_parts = lax.axis_size("lon")
    lat_parts = lax.axis_size("lat")
    left = flattened.reshape(
        members, row_count, lon_count, BASIS, lat_parts, channels // lat_parts
    )
    right = cotangent.reshape(members, row_count, lon_count, lon_parts, channels // lon_parts)
    partial_value = jnp.einsum(
        "brwkic,brwjo->ijkco", left, right, preferred_element_type=jnp.float32
    )
    partial_value = partial_value.reshape(
        (lat_parts * lon_parts, BASIS, channels // lat_parts, channels // lon_parts)
    )
    reduced = lax.psum_scatter(partial_value, ("lat", "lon"), scatter_dimension=0, tiled=True)
    reduced = reduced.reshape(BASIS, channels // lat_parts, channels // lon_parts)
    grad_weight = reduced / jnp.sqrt(jnp.float32(members * height * lon_total))
    return (response, grad_input, grad_weight)


def solution(mesh):
    placed = (
        P("grp", "lat", "lon", None),
        P("grp", "lat", "lon", None),
        P(),
        P(),
        P(),
        P(),
        P(),
        P(),
    )
    return jax.shard_map(
        on_device,
        mesh=mesh,
        in_specs=placed,
        out_specs=(
            P("grp", "lat", "lon", None),
            P("grp", "lat", "lon", None),
            P("grp", "lat", "lon"),
        ),
        check_vma=False,
    )
```

```python
import functools

import jax
import jax.numpy as jnp
from jax import lax
from jax.experimental import pallas as pl
from jax.experimental.pallas import tpu as pltpu
from jax.sharding import PartitionSpec as P

BASIS = 9
REACH = 2
RIM = 16


def with_halo(block, sides, width, periodic):
    for axis, dim in sides:
        count = lax.axis_size(axis)
        forward = [(i, i + 1) for i in range(count - 1)]
        if periodic:
            forward.append((count - 1, 0))
        backward = [(target, source) for source, target in forward]
        low = lax.ppermute(
            lax.slice_in_dim(block, block.shape[dim] - width, None, axis=dim), axis, forward
        )
        high = lax.ppermute(lax.slice_in_dim(block, 0, width, axis=dim), axis, backward)
        block = jnp.concatenate([low, block, high], axis=dim)
    return block


def extend(grid_field, padded):
    grid_field = with_halo(grid_field, (("lat", 1),), REACH, False)
    grid_field = with_halo(grid_field, (("lon", 2),), RIM, True)
    extra = padded - grid_field.shape[2]
    return jnp.pad(grid_field, ((0, 0), (0, 0), (0, extra), (0, 0)))


def ring_sum(value, axis):
    count = lax.axis_size(axis)
    total = value
    for shift in range(1, count):
        pairs = [(i, (i + shift) % count) for i in range(count)]
        total = total + lax.ppermute(value, axis, pairs)
    return total


def cycle_totals(widened, lon_count):
    interior = lax.slice_in_dim(widened, RIM, RIM + lon_count, axis=2)
    return ring_sum(jnp.sum(interior, axis=2, dtype=jnp.float32), "lon")


def ring_scatter(value, axis, dim):
    count = lax.axis_size(axis)
    own = lax.axis_index(axis)
    block = value.shape[dim] // count
    total = lax.dynamic_slice_in_dim(value, own * block, block, dim)
    for shift in range(1, count):
        pairs = [(i, (i + shift) % count) for i in range(count)]
        piece = lax.dynamic_slice_in_dim(value, ((own + shift) % count) * block, block, dim)
        total = total + lax.ppermute(piece, axis, pairs)
    return total


def filter_kernel(
    rows_ref, start_ref, span_ref, basis_ref, scale_ref, field_ref, total_ref, out_ref, acc_ref,
    *, slots, window_rows, lon_count, lon_total, backward,
):
    r = pl.program_id(1)
    padded = field_ref.shape[2]
    channels = field_ref.shape[3]
    acc_ref[...] = jnp.zeros(acc_ref.shape, jnp.float32)
    out_col = lax.broadcasted_iota(jnp.int32, (lon_count, padded), 0)
    in_col = lax.broadcasted_iota(jnp.int32, (lon_count, padded), 1) - RIM
    offset = out_col - in_col if backward else in_col - out_col

    def add_slot(row, table_row, slot, scale):
        start = start_ref[table_row, slot]
        span = span_ref[table_row, slot]
        basis = basis_ref[table_row, slot]
        narrow = span < lon_total
        band = ((offset >= start) & (offset < start + span) & narrow).astype(jnp.bfloat16)
        boxed = jnp.dot(band, field_ref[0, row], preferred_element_type=jnp.float32)
        full = jnp.where(narrow, 0.0, 1.0).astype(jnp.float32)
        boxed = boxed + full * total_ref[0, row]
        acc_ref[basis] = acc_ref[basis] + scale * boxed

    if backward:
        for e in range(window_rows):
            row = r + e
            for slot in range(slots):
                scale = scale_ref[r, row * slots + slot]

                @pl.when(scale != 0.0)
                def _():
                    add_slot(row, row, slot, scale)
    else:
        for slot in range(slots):
            add_slot(rows_ref[r, slot], r, slot, scale_ref[r, slot])

    for k in range(BASIS):
        out_ref[0, 0, :, k * channels:(k + 1) * channels] = acc_ref[k].astype(jnp.bfloat16)


def run_filter(tables, field, totals, lon_count, lon_total, backward):
    members, window, padded, channels = field.shape
    row_count = window - 2 * REACH
    slots = tables[1].shape[1]
    smem = pl.BlockSpec(memory_space=pltpu.SMEM)
    kernel = functools.partial(
        filter_kernel,
        slots=slots,
        window_rows=2 * REACH + 1,
        lon_count=lon_count,
        lon_total=lon_total,
        backward=backward,
    )
    return pl.pallas_call(
        kernel,
        grid=(members, row_count),
        in_specs=[smem] * 5
        + [
            pl.BlockSpec((1, window, padded, channels), lambda b, r: (b, 0, 0, 0)),
            pl.BlockSpec((1, window, 1, channels), lambda b, r: (b, 0, 0, 0)),
        ],
        out_specs=pl.BlockSpec(
            (1, 1, lon_count, BASIS * channels), lambda b, r: (b, r, 0, 0)
        ),
        out_shape=jax.ShapeDtypeStruct(
            (members, row_count, lon_count, BASIS * channels), jnp.bfloat16
        ),
        scratch_shapes=[pltpu.VMEM((BASIS, lon_count, channels), jnp.float32)],
    )(*tables, field, totals[:, :, None, :])


def on_device(inputs, cotangent, weight, src_rows, lon_start, lon_span, basis_idx, quad_weight):
    members, row_count, lon_count, channels = inputs.shape
    lon_total = lon_count * lax.axis_size("lon")
    height = row_count * lax.axis_size("lat")
    first_row = lax.axis_index("lat") * row_count
    window = row_count + 2 * REACH
    padded = -(-(lon_count + 2 * RIM) // 128) * 128
    weighting = quad_weight / jnp.sqrt(lon_span.astype(jnp.float32))

    widened = extend(inputs, padded)
    grad_wide = extend(cotangent, padded)
    totals = cycle_totals(widened, lon_count)
    grad_totals = cycle_totals(grad_wide, lon_count)

    def rows_of(table, begin, count):
        return lax.dynamic_slice_in_dim(table, begin, count, 0)

    f_tables = (
        rows_of(src_rows, first_row, row_count) - first_row + REACH,
        rows_of(lon_start, first_row, row_count),
        rows_of(lon_span, first_row, row_count),
        rows_of(basis_idx, first_row, row_count),
        rows_of(weighting, first_row, row_count),
    )
    flattened = run_filter(f_tables, widened, totals, lon_count, lon_total, False)
    w_fwd = weight.reshape(BASIS * channels, channels)
    response = jnp.einsum("brwq,qo->brwo", flattened, w_fwd, preferred_element_type=jnp.float32)

    pad_pair = ((REACH, REACH), (0, 0))
    b_src = rows_of(jnp.pad(src_rows, pad_pair, constant_values=-1), first_row, window)
    b_start = rows_of(jnp.pad(lon_start, pad_pair, constant_values=0), first_row, window)
    b_span = rows_of(jnp.pad(lon_span, pad_pair, constant_values=1), first_row, window)
    b_basis = rows_of(jnp.pad(basis_idx, pad_pair, constant_values=0), first_row, window)
    b_scale = rows_of(jnp.pad(weighting, pad_pair, constant_values=0.0), first_row, window)
    targets = first_row + jnp.arange(row_count, dtype=jnp.int32)
    b_hit = b_src[None, :, :] == targets[:, None, None]
    b_weights = jnp.where(b_hit, b_scale[None], 0.0).reshape(row_count, -1)
    b_tables = (b_src, b_start, b_span, b_basis, b_weights)
    back_filtered = run_filter(b_tables, grad_wide, grad_totals, lon_count, lon_total, True)
    w_back = jnp.transpose(weight, (0, 2, 1)).reshape(BASIS * channels, channels)
    grad_input = jnp.einsum(
        "bpwq,qc->bpwc", back_filtered, w_back, preferred_element_type=jnp.float32
    )
    partial_value = jnp.einsum(
        "brwq,brwo->qo", flattened, cotangent, preferred_element_type=jnp.float32
    )
    partial_value = partial_value.reshape(BASIS, channels, channels)
    reduced = lax.psum_scatter(partial_value, "lon", scatter_dimension=2, tiled=True)
    reduced = ring_scatter(reduced, "lat", 1)
    grad_weight = reduced / jnp.sqrt(jnp.float32(members * height * lon_total))
    return (response, grad_input, grad_weight)


def solution(mesh):
    placed = (
        P("grp", "lat", "lon", None),
        P("grp", "lat", "lon", None),
        P(),
        P(),
        P(),
        P(),
        P(),
        P(),
    )
    return jax.shard_map(
        on_device,
        mesh=mesh,
        in_specs=placed,
        out_specs=(
            P("grp", "lat", "lon", None),
            P("grp", "lat", "lon", None),
            P("grp", "lat", "lon"),
        ),
        check_vma=False,
    )
```

```python
import functools

import jax
import jax.numpy as jnp
from jax import lax
from jax.experimental import pallas as pl
from jax.experimental.pallas import tpu as pltpu
from jax.sharding import PartitionSpec as P

BASIS = 9
REACH = 2
RIM = 16


def with_halo(block, sides, width, periodic):
    for axis, dim in sides:
        count = lax.axis_size(axis)
        forward = [(i, i + 1) for i in range(count - 1)]
        if periodic:
            forward.append((count - 1, 0))
        backward = [(target, source) for source, target in forward]
        low = lax.ppermute(
            lax.slice_in_dim(block, block.shape[dim] - width, None, axis=dim), axis, forward
        )
        high = lax.ppermute(lax.slice_in_dim(block, 0, width, axis=dim), axis, backward)
        block = jnp.concatenate([low, block, high], axis=dim)
    return block


def extend(grid_field, padded):
    grid_field = with_halo(grid_field, (("lat", 1),), REACH, False)
    grid_field = with_halo(grid_field, (("lon", 2),), RIM, True)
    extra = padded - grid_field.shape[2]
    return jnp.pad(grid_field, ((0, 0), (0, 0), (0, extra), (0, 0)))


def ring_sum(value, axis):
    count = lax.axis_size(axis)
    total = value
    for shift in range(1, count):
        pairs = [(i, (i + shift) % count) for i in range(count)]
        total = total + lax.ppermute(value, axis, pairs)
    return total


def cycle_totals(widened, lon_count):
    interior = lax.slice_in_dim(widened, RIM, RIM + lon_count, axis=2)
    return ring_sum(jnp.sum(interior, axis=2, dtype=jnp.float32), "lon")


def filter_kernel(
    rows_ref, start_ref, span_ref, basis_ref, scale_ref, field_ref, total_ref, out_ref, acc_ref,
    *, slots, window_rows, lon_count, lon_total, backward,
):
    r = pl.program_id(1)
    padded = field_ref.shape[2]
    channels = field_ref.shape[3]
    acc_ref[...] = jnp.zeros(acc_ref.shape, jnp.float32)
    out_col = lax.broadcasted_iota(jnp.int32, (lon_count, padded), 0)
    in_col = lax.broadcasted_iota(jnp.int32, (lon_count, padded), 1) - RIM
    offset = out_col - in_col if backward else in_col - out_col

    def add_slot(row, table_row, slot, scale):
        start = start_ref[table_row, slot]
        span = span_ref[table_row, slot]
        basis = basis_ref[table_row, slot]
        narrow = span < lon_total
        band = ((offset >= start) & (offset < start + span) & narrow).astype(jnp.bfloat16)
        boxed = jnp.dot(band, field_ref[0, row], preferred_element_type=jnp.float32)
        full = jnp.where(narrow, 0.0, 1.0).astype(jnp.float32)
        boxed = boxed + full * total_ref[0, row]
        acc_ref[basis] = acc_ref[basis] + scale * boxed

    if backward:
        for e in range(window_rows):
            row = r + e
            for slot in range(slots):
                scale = scale_ref[r, row * slots + slot]

                @pl.when(scale != 0.0)
                def _():
                    add_slot(row, row, slot, scale)
    else:
        for slot in range(slots):
            add_slot(rows_ref[r, slot], r, slot, scale_ref[r, slot])

    for k in range(BASIS):
        out_ref[0, 0, :, k * channels:(k + 1) * channels] = acc_ref[k].astype(jnp.bfloat16)


def run_filter(tables, field, totals, row_count, lon_count, lon_total, backward):
    members, window, padded, channels = field.shape
    slots = tables[1].shape[1]
    smem = pl.BlockSpec(memory_space=pltpu.SMEM)
    kernel = functools.partial(
        filter_kernel,
        slots=slots,
        window_rows=2 * REACH + 1,
        lon_count=lon_count,
        lon_total=lon_total,
        backward=backward,
    )
    return pl.pallas_call(
        kernel,
        grid=(members, row_count),
        in_specs=[smem] * 5
        + [
            pl.BlockSpec((1, window, padded, channels), lambda b, r: (b, 0, 0, 0)),
            pl.BlockSpec((1, window, 1, channels), lambda b, r: (b, 0, 0, 0)),
        ],
        out_specs=pl.BlockSpec(
            (1, 1, lon_count, BASIS * channels), lambda b, r: (b, r, 0, 0)
        ),
        out_shape=jax.ShapeDtypeStruct(
            (members, row_count, lon_count, BASIS * channels), jnp.bfloat16
        ),
        scratch_shapes=[pltpu.VMEM((BASIS, lon_count, channels), jnp.float32)],
    )(*tables, field, totals[:, :, None, :])


def on_device(inputs, cotangent, weight, src_rows, lon_start, lon_span, basis_idx, quad_weight):
    members, row_count, lon_count, channels = inputs.shape
    lon_total = lon_count * lax.axis_size("lon")
    height = row_count * lax.axis_size("lat")
    first_row = lax.axis_index("lat") * row_count
    window = row_count + 2 * REACH
    padded = -(-(lon_count + 2 * RIM) // 128) * 128
    weighting = quad_weight / jnp.sqrt(lon_span.astype(jnp.float32))

    widened = extend(inputs, padded)
    grad_wide = extend(cotangent, padded)
    totals = cycle_totals(widened, lon_count)
    grad_totals = cycle_totals(grad_wide, lon_count)

    def rows_of(table, begin, count):
        return lax.dynamic_slice_in_dim(table, begin, count, 0)

    f_tables = (
        rows_of(src_rows, first_row, row_count) - first_row + REACH,
        rows_of(lon_start, first_row, row_count),
        rows_of(lon_span, first_row, row_count),
        rows_of(basis_idx, first_row, row_count),
        rows_of(weighting, first_row, row_count),
    )
    flattened = run_filter(f_tables, widened, totals, row_count, lon_count, lon_total, False)
    w_fwd = weight.reshape(BASIS * channels, channels)
    response = jnp.einsum("brwq,qo->brwo", flattened, w_fwd, preferred_element_type=jnp.float32)

    pad_pair = ((REACH, REACH), (0, 0))
    b_src = rows_of(jnp.pad(src_rows, pad_pair, constant_values=-1), first_row, window)
    b_start = rows_of(jnp.pad(lon_start, pad_pair, constant_values=0), first_row, window)
    b_span = rows_of(jnp.pad(lon_span, pad_pair, constant_values=1), first_row, window)
    b_basis = rows_of(jnp.pad(basis_idx, pad_pair, constant_values=0), first_row, window)
    b_scale = rows_of(jnp.pad(weighting, pad_pair, constant_values=0.0), first_row, window)
    targets = first_row + jnp.arange(row_count, dtype=jnp.int32)
    b_hit = b_src[None, :, :] == targets[:, None, None]
    b_weights = jnp.where(b_hit, b_scale[None], 0.0).reshape(row_count, -1)
    b_tables = (b_src, b_start, b_span, b_basis, b_weights)
    back_filtered = run_filter(
        b_tables, grad_wide, grad_totals, row_count, lon_count, lon_total, True
    )
    w_back = jnp.transpose(weight, (0, 2, 1)).reshape(BASIS * channels, channels)
    grad_input = jnp.einsum(
        "bpwq,qc->bpwc", back_filtered, w_back, preferred_element_type=jnp.float32
    )
    lat_parts = lax.axis_size("lat")
    lon_parts = lax.axis_size("lon")
    in_block = lax.all_to_all(inputs, "lat", 3, 1, tiled=True)
    in_block = lax.all_gather(in_block, "lon", axis=2, tiled=True)
    out_block = lax.all_to_all(cotangent, "lon", 3, 2, tiled=True)
    out_block = lax.all_gather(out_block, "lat", axis=1, tiled=True)
    c_part = channels // lat_parts
    o_part = channels // lon_parts
    ring = jnp.concatenate(
        [in_block[:, :, lon_total - RIM:], in_block, in_block[:, :, :RIM]], axis=2
    )
    span_wide = lon_count + 2 * RIM
    stacked = jnp.concatenate(
        [
            jnp.pad(
                ring[:, :, q * lon_count:q * lon_count + span_wide],
                ((0, 0), (0, 0), (0, padded - span_wide), (0, 0)),
            )
            for q in range(lon_parts)
        ],
        axis=3,
    )
    ring_totals = jnp.tile(jnp.sum(in_block, axis=2, dtype=jnp.float32), (1, 1, lon_parts))
    g_tables = (src_rows, lon_start, lon_span, basis_idx, weighting)
    every = run_filter(g_tables, stacked, ring_totals, height, lon_count, lon_total, False)
    every = every.reshape(members, height, lon_count, BASIS, lon_parts, c_part)
    right = out_block.reshape(members, height, lon_parts, lon_count, o_part)
    block_value = jnp.einsum(
        "bhwkqc,bhqwo->kco", every, right, preferred_element_type=jnp.float32
    )
    grad_weight = block_value / jnp.sqrt(jnp.float32(members * height * lon_total))
    return (response, grad_input, grad_weight)


def solution(mesh):
    placed = (
        P("grp", "lat", "lon", None),
        P("grp", "lat", "lon", None),
        P(),
        P(),
        P(),
        P(),
        P(),
        P(),
    )
    return jax.shard_map(
        on_device,
        mesh=mesh,
        in_specs=placed,
        out_specs=(
            P("grp", "lat", "lon", None),
            P("grp", "lat", "lon", None),
            P("grp", "lat", "lon"),
        ),
        check_vma=False,
    )
```

```python
import functools

import jax
import jax.numpy as jnp
from jax import lax
from jax.experimental import pallas as pl
from jax.experimental.pallas import tpu as pltpu
from jax.sharding import PartitionSpec as P

BASIS = 9
REACH = 2
RIM = 16


def with_halo(block, sides, width, periodic):
    for axis, dim in sides:
        count = lax.axis_size(axis)
        forward = [(i, i + 1) for i in range(count - 1)]
        if periodic:
            forward.append((count - 1, 0))
        backward = [(target, source) for source, target in forward]
        low = lax.ppermute(
            lax.slice_in_dim(block, block.shape[dim] - width, None, axis=dim), axis, forward
        )
        high = lax.ppermute(lax.slice_in_dim(block, 0, width, axis=dim), axis, backward)
        block = jnp.concatenate([low, block, high], axis=dim)
    return block


def extend(grid_field, padded):
    grid_field = with_halo(grid_field, (("lat", 1),), REACH, False)
    grid_field = with_halo(grid_field, (("lon", 2),), RIM, True)
    extra = padded - grid_field.shape[2]
    return jnp.pad(grid_field, ((0, 0), (0, 0), (0, extra), (0, 0)))


def ring_sum(value, axis):
    count = lax.axis_size(axis)
    total = value
    for shift in range(1, count):
        pairs = [(i, (i + shift) % count) for i in range(count)]
        total = total + lax.ppermute(value, axis, pairs)
    return total


def cycle_totals(widened, lon_count):
    interior = lax.slice_in_dim(widened, RIM, RIM + lon_count, axis=2)
    return ring_sum(jnp.sum(interior, axis=2, dtype=jnp.float32), "lon")


def ring_scatter(value, axis, dim):
    count = lax.axis_size(axis)
    own = lax.axis_index(axis)
    block = value.shape[dim] // count
    total = lax.dynamic_slice_in_dim(value, own * block, block, dim)
    for shift in range(1, count):
        pairs = [(i, (i + shift) % count) for i in range(count)]
        piece = lax.dynamic_slice_in_dim(value, ((own + shift) % count) * block, block, dim)
        sent = lax.ppermute(piece.astype(jnp.bfloat16), axis, pairs)
        total = total + sent.astype(jnp.float32)
    return total


def filter_kernel(
    rows_ref, start_ref, span_ref, basis_ref, scale_ref, field_ref, total_ref, out_ref, acc_ref,
    *, slots, window_rows, lon_count, lon_total, backward,
):
    r = pl.program_id(1)
    padded = field_ref.shape[2]
    channels = field_ref.shape[3]
    acc_ref[...] = jnp.zeros(acc_ref.shape, jnp.float32)
    out_col = lax.broadcasted_iota(jnp.int32, (lon_count, padded), 0)
    in_col = lax.broadcasted_iota(jnp.int32, (lon_count, padded), 1) - RIM
    offset = out_col - in_col if backward else in_col - out_col

    def add_slot(row, table_row, slot, scale):
        start = start_ref[table_row, slot]
        span = span_ref[table_row, slot]
        basis = basis_ref[table_row, slot]
        narrow = span < lon_total
        band = ((offset >= start) & (offset < start + span) & narrow).astype(jnp.bfloat16)
        boxed = jnp.dot(band, field_ref[0, row], preferred_element_type=jnp.float32)
        full = jnp.where(narrow, 0.0, 1.0).astype(jnp.float32)
        boxed = boxed + full * total_ref[0, row]
        acc_ref[basis] = acc_ref[basis] + scale * boxed

    if backward:
        for e in range(window_rows):
            row = r + e
            for slot in range(slots):
                scale = scale_ref[r, row * slots + slot]

                @pl.when(scale != 0.0)
                def _():
                    add_slot(row, row, slot, scale)
    else:
        for slot in range(slots):
            add_slot(rows_ref[r, slot], r, slot, scale_ref[r, slot])

    for k in range(BASIS):
        out_ref[0, 0, :, k * channels:(k + 1) * channels] = acc_ref[k].astype(jnp.bfloat16)


def run_filter(tables, field, totals, lon_count, lon_total, backward):
    members, window, padded, channels = field.shape
    row_count = window - 2 * REACH
    slots = tables[1].shape[1]
    smem = pl.BlockSpec(memory_space=pltpu.SMEM)
    kernel = functools.partial(
        filter_kernel,
        slots=slots,
        window_rows=2 * REACH + 1,
        lon_count=lon_count,
        lon_total=lon_total,
        backward=backward,
    )
    return pl.pallas_call(
        kernel,
        grid=(members, row_count),
        in_specs=[smem] * 5
        + [
            pl.BlockSpec((1, window, padded, channels), lambda b, r: (b, 0, 0, 0)),
            pl.BlockSpec((1, window, 1, channels), lambda b, r: (b, 0, 0, 0)),
        ],
        out_specs=pl.BlockSpec(
            (1, 1, lon_count, BASIS * channels), lambda b, r: (b, r, 0, 0)
        ),
        out_shape=jax.ShapeDtypeStruct(
            (members, row_count, lon_count, BASIS * channels), jnp.bfloat16
        ),
        scratch_shapes=[pltpu.VMEM((BASIS, lon_count, channels), jnp.float32)],
    )(*tables, field, totals[:, :, None, :])


def on_device(inputs, cotangent, weight, src_rows, lon_start, lon_span, basis_idx, quad_weight):
    members, row_count, lon_count, channels = inputs.shape
    lon_total = lon_count * lax.axis_size("lon")
    height = row_count * lax.axis_size("lat")
    first_row = lax.axis_index("lat") * row_count
    window = row_count + 2 * REACH
    padded = -(-(lon_count + 2 * RIM) // 128) * 128
    weighting = quad_weight / jnp.sqrt(lon_span.astype(jnp.float32))

    widened = extend(inputs, padded)
    grad_wide = extend(cotangent, padded)
    totals = cycle_totals(widened, lon_count)
    grad_totals = cycle_totals(grad_wide, lon_count)

    def rows_of(table, begin, count):
        return lax.dynamic_slice_in_dim(table, begin, count, 0)

    f_tables = (
        rows_of(src_rows, first_row, row_count) - first_row + REACH,
        rows_of(lon_start, first_row, row_count),
        rows_of(lon_span, first_row, row_count),
        rows_of(basis_idx, first_row, row_count),
        rows_of(weighting, first_row, row_count),
    )
    flattened = run_filter(f_tables, widened, totals, lon_count, lon_total, False)
    w_fwd = weight.reshape(BASIS * channels, channels)
    response = jnp.einsum("brwq,qo->brwo", flattened, w_fwd, preferred_element_type=jnp.float32)

    pad_pair = ((REACH, REACH), (0, 0))
    b_src = rows_of(jnp.pad(src_rows, pad_pair, constant_values=-1), first_row, window)
    b_start = rows_of(jnp.pad(lon_start, pad_pair, constant_values=0), first_row, window)
    b_span = rows_of(jnp.pad(lon_span, pad_pair, constant_values=1), first_row, window)
    b_basis = rows_of(jnp.pad(basis_idx, pad_pair, constant_values=0), first_row, window)
    b_scale = rows_of(jnp.pad(weighting, pad_pair, constant_values=0.0), first_row, window)
    targets = first_row + jnp.arange(row_count, dtype=jnp.int32)
    b_hit = b_src[None, :, :] == targets[:, None, None]
    b_weights = jnp.where(b_hit, b_scale[None], 0.0).reshape(row_count, -1)
    b_tables = (b_src, b_start, b_span, b_basis, b_weights)
    back_filtered = run_filter(b_tables, grad_wide, grad_totals, lon_count, lon_total, True)
    w_back = jnp.transpose(weight, (0, 2, 1)).reshape(BASIS * channels, channels)
    grad_input = jnp.einsum(
        "bpwq,qc->bpwc", back_filtered, w_back, preferred_element_type=jnp.float32
    )
    partial_value = jnp.einsum(
        "brwq,brwo->qo", flattened, cotangent, preferred_element_type=jnp.float32
    )
    partial_value = partial_value.reshape(BASIS, channels, channels)
    reduced = ring_scatter(partial_value, "lon", 2)
    reduced = ring_scatter(reduced, "lat", 1)
    grad_weight = reduced / jnp.sqrt(jnp.float32(members * height * lon_total))
    return (response, grad_input, grad_weight)


def solution(mesh):
    placed = (
        P("grp", "lat", "lon", None),
        P("grp", "lat", "lon", None),
        P(),
        P(),
        P(),
        P(),
        P(),
        P(),
    )
    return jax.shard_map(
        on_device,
        mesh=mesh,
        in_specs=placed,
        out_specs=(
            P("grp", "lat", "lon", None),
            P("grp", "lat", "lon", None),
            P("grp", "lat", "lon"),
        ),
        check_vma=False,
    )
```

```python
import functools

import jax
import jax.numpy as jnp
from jax import lax
from jax.experimental import pallas as pl
from jax.experimental.pallas import tpu as pltpu
from jax.sharding import PartitionSpec as P

BASIS = 9
REACH = 2
RIM = 16
POLAR = 2


def extend(block, padded):
    lat_count = lax.axis_size("lat")
    lon_count = lax.axis_size("lon")
    rows = block.shape[1]
    cols = block.shape[2]

    def fetch(piece, d_lat, d_lon):
        pairs = []
        for lat in range(lat_count):
            source = lat - d_lat
            if 0 <= source < lat_count:
                for lon in range(lon_count):
                    pairs.append(
                        (source * lon_count + (lon - d_lon) % lon_count, lat * lon_count + lon)
                    )
        return lax.ppermute(piece, ("lat", "lon"), pairs)

    top = block[:, rows - REACH:]
    bottom = block[:, :REACH]
    bands = []
    for d_lat, part in ((1, top), (0, block), (-1, bottom)):
        left = fetch(part[:, :, cols - RIM:], d_lat, 1)
        right = fetch(part[:, :, :RIM], d_lat, -1)
        middle = part if d_lat == 0 else fetch(part, d_lat, 0)
        bands.append(jnp.concatenate([left, middle, right], axis=2))
    field = jnp.concatenate(bands, axis=1)
    extra = padded - field.shape[2]
    return jnp.pad(field, ((0, 0), (0, 0), (0, extra), (0, 0)))


def ring_sum(value, axis):
    count = lax.axis_size(axis)
    total = value
    for shift in range(1, count):
        pairs = [(i, (i + shift) % count) for i in range(count)]
        total = total + lax.ppermute(value, axis, pairs)
    return total


def with_lat_halo(value):
    count = lax.axis_size("lat")
    forward = [(i, i + 1) for i in range(count - 1)]
    backward = [(t, f) for f, t in forward]
    rows = value.shape[2]
    low = lax.ppermute(value[:, :, rows - REACH:], "lat", forward)
    high = lax.ppermute(value[:, :, :REACH], "lat", backward)
    return jnp.concatenate([low, value, high], axis=2)


def ring_scatter(value, axis, dim):
    count = lax.axis_size(axis)
    own = lax.axis_index(axis)
    block = value.shape[dim] // count
    total = lax.dynamic_slice_in_dim(value, own * block, block, dim)
    for shift in range(1, count):
        pairs = [(i, (i + shift) % count) for i in range(count)]
        piece = lax.dynamic_slice_in_dim(value, ((own + shift) % count) * block, block, dim)
        sent = lax.ppermute(piece.astype(jnp.bfloat16), axis, pairs)
        total = total + sent.astype(jnp.float32)
    return total


def filter_kernel(
    rows_ref, start_ref, span_ref, basis_ref, scale_ref, field_ref, total_ref, out_ref, acc_ref,
    *, slots, window_rows, lon_count, lon_total, backward,
):
    r = pl.program_id(1)
    padded = field_ref.shape[2]
    channels = field_ref.shape[3]
    acc_ref[...] = jnp.zeros(acc_ref.shape, jnp.float32)
    out_col = lax.broadcasted_iota(jnp.int32, (lon_count, padded), 0)
    in_col = lax.broadcasted_iota(jnp.int32, (lon_count, padded), 1) - RIM
    offset = out_col - in_col if backward else in_col - out_col

    def add_slot(row, table_row, slot, scale):
        start = start_ref[table_row, slot]
        span = span_ref[table_row, slot]
        basis = basis_ref[table_row, slot]
        narrow = span < lon_total
        band = ((offset >= start) & (offset < start + span) & narrow).astype(jnp.bfloat16)
        boxed = jnp.dot(band, field_ref[0, row], preferred_element_type=jnp.float32)
        full = jnp.where(narrow, 0.0, 1.0).astype(jnp.float32)
        boxed = boxed + full * total_ref[0, row]
        acc_ref[basis] = acc_ref[basis] + scale * boxed

    if backward:
        for e in range(window_rows):
            row = r + e
            for slot in range(slots):
                scale = scale_ref[r, row * slots + slot]

                @pl.when(scale != 0.0)
                def _():
                    add_slot(row, row, slot, scale)
    else:
        for slot in range(slots):
            add_slot(rows_ref[r, slot], r, slot, scale_ref[r, slot])

    for k in range(BASIS):
        out_ref[0, 0, :, k * channels:(k + 1) * channels] = acc_ref[k].astype(jnp.bfloat16)


def run_filter(tables, field, totals, lon_count, lon_total, backward):
    members, window, padded, channels = field.shape
    row_count = window - 2 * REACH
    slots = tables[1].shape[1]
    smem = pl.BlockSpec(memory_space=pltpu.SMEM)
    kernel = functools.partial(
        filter_kernel,
        slots=slots,
        window_rows=2 * REACH + 1,
        lon_count=lon_count,
        lon_total=lon_total,
        backward=backward,
    )
    return pl.pallas_call(
        kernel,
        grid=(members, row_count),
        in_specs=[smem] * 5
        + [
            pl.BlockSpec((1, window, padded, channels), lambda b, r: (b, 0, 0, 0)),
            pl.BlockSpec((1, window, 1, channels), lambda b, r: (b, 0, 0, 0)),
        ],
        out_specs=pl.BlockSpec(
            (1, 1, lon_count, BASIS * channels), lambda b, r: (b, r, 0, 0)
        ),
        out_shape=jax.ShapeDtypeStruct(
            (members, row_count, lon_count, BASIS * channels), jnp.bfloat16
        ),
        scratch_shapes=[pltpu.VMEM((BASIS, lon_count, channels), jnp.float32)],
    )(*tables, field, totals[:, :, None, :])


def on_device(inputs, cotangent, weight, src_rows, lon_start, lon_span, basis_idx, quad_weight):
    members, row_count, lon_count, channels = inputs.shape
    lon_total = lon_count * lax.axis_size("lon")
    height = row_count * lax.axis_size("lat")
    first_row = lax.axis_index("lat") * row_count
    window = row_count + 2 * REACH
    padded = -(-(lon_count + 2 * RIM) // 128) * 128
    weighting = quad_weight / jnp.sqrt(lon_span.astype(jnp.float32))

    widened = extend(inputs, padded)
    grad_wide = extend(cotangent, padded)
    row_sums = jnp.stack(
        [jnp.sum(inputs, axis=2, dtype=jnp.float32), jnp.sum(cotangent, axis=2, dtype=jnp.float32)]
    )
    local_totals = ring_sum(row_sums, "lon")
    if row_count >= POLAR + REACH:
        framed = jnp.pad(local_totals, ((0, 0), (0, 0), (REACH, REACH), (0, 0)))
    else:
        framed = with_lat_halo(local_totals)
    totals, grad_totals = framed[0], framed[1]

    def rows_of(table, begin, count):
        return lax.dynamic_slice_in_dim(table, begin, count, 0)

    f_tables = (
        rows_of(src_rows, first_row, row_count) - first_row + REACH,
        rows_of(lon_start, first_row, row_count),
        rows_of(lon_span, first_row, row_count),
        rows_of(basis_idx, first_row, row_count),
        rows_of(weighting, first_row, row_count),
    )
    flattened = run_filter(f_tables, widened, totals, lon_count, lon_total, False)
    w_fwd = weight.reshape(BASIS * channels, channels)
    response = jnp.einsum("brwq,qo->brwo", flattened, w_fwd, preferred_element_type=jnp.float32)

    pad_pair = ((REACH, REACH), (0, 0))
    b_src = rows_of(jnp.pad(src_rows, pad_pair, constant_values=-1), first_row, window)
    b_start = rows_of(jnp.pad(lon_start, pad_pair, constant_values=0), first_row, window)
    b_span = rows_of(jnp.pad(lon_span, pad_pair, constant_values=1), first_row, window)
    b_basis = rows_of(jnp.pad(basis_idx, pad_pair, constant_values=0), first_row, window)
    b_scale = rows_of(jnp.pad(weighting, pad_pair, constant_values=0.0), first_row, window)
    targets = first_row + jnp.arange(row_count, dtype=jnp.int32)
    b_hit = b_src[None, :, :] == targets[:, None, None]
    b_weights = jnp.where(b_hit, b_scale[None], 0.0).reshape(row_count, -1)
    b_tables = (b_src, b_start, b_span, b_basis, b_weights)
    back_filtered = run_filter(b_tables, grad_wide, grad_totals, lon_count, lon_total, True)
    w_back = jnp.transpose(weight, (0, 2, 1)).reshape(BASIS * channels, channels)
    grad_input = jnp.einsum(
        "bpwq,qc->bpwc", back_filtered, w_back, preferred_element_type=jnp.float32
    )
    partial_value = jnp.einsum(
        "brwq,brwo->qo", flattened, cotangent, preferred_element_type=jnp.float32
    )
    partial_value = partial_value.reshape(BASIS, channels, channels)
    reduced = ring_scatter(partial_value, "lon", 2)
    reduced = ring_scatter(reduced, "lat", 1)
    grad_weight = reduced / jnp.sqrt(jnp.float32(members * height * lon_total))
    return (response, grad_input, grad_weight)


def solution(mesh):
    placed = (
        P("grp", "lat", "lon", None),
        P("grp", "lat", "lon", None),
        P(),
        P(),
        P(),
        P(),
        P(),
        P(),
    )
    return jax.shard_map(
        on_device,
        mesh=mesh,
        in_specs=placed,
        out_specs=(
            P("grp", "lat", "lon", None),
            P("grp", "lat", "lon", None),
            P("grp", "lat", "lon"),
        ),
        check_vma=False,
    )
```

```python
import functools

import jax
import jax.numpy as jnp
from jax import lax
from jax.experimental import pallas as pl
from jax.experimental.pallas import tpu as pltpu
from jax.sharding import PartitionSpec as P

BASIS = 9
REACH = 2
RIM = 16
POLAR = 2


def with_halo(block, sides, width, periodic):
    for axis, dim in sides:
        count = lax.axis_size(axis)
        forward = [(i, i + 1) for i in range(count - 1)]
        if periodic:
            forward.append((count - 1, 0))
        backward = [(target, source) for source, target in forward]
        low = lax.ppermute(
            lax.slice_in_dim(block, block.shape[dim] - width, None, axis=dim), axis, forward
        )
        high = lax.ppermute(lax.slice_in_dim(block, 0, width, axis=dim), axis, backward)
        block = jnp.concatenate([low, block, high], axis=dim)
    return block


def extend(grid_field, padded):
    grid_field = with_halo(grid_field, (("lat", 1),), REACH, False)
    grid_field = with_halo(grid_field, (("lon", 2),), RIM, True)
    extra = padded - grid_field.shape[2]
    return jnp.pad(grid_field, ((0, 0), (0, 0), (0, extra), (0, 0)))


def ring_sum(value, axis):
    count = lax.axis_size(axis)
    total = value
    for shift in range(1, count):
        pairs = [(i, (i + shift) % count) for i in range(count)]
        total = total + lax.ppermute(value, axis, pairs)
    return total


def ring_scatter(value, axis, dim):
    count = lax.axis_size(axis)
    own = lax.axis_index(axis)
    block = value.shape[dim] // count
    total = lax.dynamic_slice_in_dim(value, own * block, block, dim)
    for shift in range(1, count):
        pairs = [(i, (i + shift) % count) for i in range(count)]
        piece = lax.dynamic_slice_in_dim(value, ((own + shift) % count) * block, block, dim)
        sent = lax.ppermute(piece.astype(jnp.bfloat16), axis, pairs)
        total = total + sent.astype(jnp.float32)
    return total


def filter_kernel(
    first_ref, src_ref, start_ref, span_ref, basis_ref, scale_ref, field_ref, total_ref,
    out_ref, acc_ref, *, slots, height, lon_count, lon_total, backward,
):
    r = pl.program_id(1)
    first_row = first_ref[0]
    padded = field_ref.shape[2]
    channels = field_ref.shape[3]
    acc_ref[...] = jnp.zeros(acc_ref.shape, jnp.float32)
    out_col = lax.broadcasted_iota(jnp.int32, (lon_count, padded), 0)
    in_col = lax.broadcasted_iota(jnp.int32, (lon_count, padded), 1) - RIM
    offset = out_col - in_col if backward else in_col - out_col

    def add_slot(row, table_row, slot, scale):
        start = start_ref[table_row, slot]
        span = span_ref[table_row, slot]
        basis = basis_ref[table_row, slot]
        narrow = span < lon_total
        band = ((offset >= start) & (offset < start + span) & narrow).astype(jnp.bfloat16)
        boxed = jnp.dot(band, field_ref[0, row], preferred_element_type=jnp.float32)
        full = jnp.where(narrow, 0.0, 1.0).astype(jnp.float32)
        boxed = boxed + full * total_ref[0, row]
        acc_ref[basis] = acc_ref[basis] + scale * boxed

    if backward:
        target = first_row + r
        for e in range(2 * REACH + 1):
            row = r + e
            global_row = target + e - REACH
            inside = (global_row >= 0) & (global_row < height)
            table_row = jnp.clip(global_row, 0, height - 1)
            for slot in range(slots):
                scale = scale_ref[table_row, slot]
                hit = inside & (src_ref[table_row, slot] == target) & (scale != 0.0)

                @pl.when(hit)
                def _():
                    add_slot(row, table_row, slot, scale)
    else:
        table_row = first_row + r
        for slot in range(slots):
            row = src_ref[table_row, slot] - first_row + REACH
            add_slot(row, table_row, slot, scale_ref[table_row, slot])

    for k in range(BASIS):
        out_ref[0, 0, :, k * channels:(k + 1) * channels] = acc_ref[k].astype(jnp.bfloat16)


def run_filter(first, tables, field, totals, row_count, lon_count, lon_total, backward):
    members, window, padded, channels = field.shape
    height, slots = tables[0].shape
    smem = pl.BlockSpec(memory_space=pltpu.SMEM)
    kernel = functools.partial(
        filter_kernel,
        slots=slots,
        height=height,
        lon_count=lon_count,
        lon_total=lon_total,
        backward=backward,
    )
    return pl.pallas_call(
        kernel,
        grid=(members, row_count),
        in_specs=[smem] * 6
        + [
            pl.BlockSpec((1, window, padded, channels), lambda b, r: (b, 0, 0, 0)),
            pl.BlockSpec((1, window, 1, channels), lambda b, r: (b, 0, 0, 0)),
        ],
        out_specs=pl.BlockSpec(
            (1, 1, lon_count, BASIS * channels), lambda b, r: (b, r, 0, 0)
        ),
        out_shape=jax.ShapeDtypeStruct(
            (members, row_count, lon_count, BASIS * channels), jnp.bfloat16
        ),
        scratch_shapes=[pltpu.VMEM((BASIS, lon_count, channels), jnp.float32)],
    )(first, *tables, field, totals[:, :, None, :])


def on_device(inputs, cotangent, weight, src_rows, lon_start, lon_span, basis_idx, quad_weight):
    members, row_count, lon_count, channels = inputs.shape
    lon_total = lon_count * lax.axis_size("lon")
    height = row_count * lax.axis_size("lat")
    first_row = lax.axis_index("lat") * row_count
    padded = -(-(lon_count + 2 * RIM) // 128) * 128
    weighting = quad_weight / jnp.sqrt(lon_span.astype(jnp.float32))
    first = jnp.reshape(first_row, (1,)).astype(jnp.int32)
    tables = (src_rows, lon_start, lon_span, basis_idx, weighting)

    both = extend(jnp.concatenate([inputs, cotangent], axis=3), padded)
    widened = both[..., :channels]
    grad_wide = both[..., channels:]
    row_sums = jnp.stack(
        [jnp.sum(inputs, axis=2, dtype=jnp.float32), jnp.sum(cotangent, axis=2, dtype=jnp.float32)]
    )
    local_totals = ring_sum(row_sums, "lon")
    if row_count >= POLAR + REACH:
        framed = jnp.pad(local_totals, ((0, 0), (0, 0), (REACH, REACH), (0, 0)))
    else:
        framed = with_halo(local_totals, (("lat", 2),), REACH, False)
    totals, grad_totals = framed[0], framed[1]

    flattened = run_filter(first, tables, widened, totals, row_count, lon_count, lon_total, False)
    w_fwd = weight.reshape(BASIS * channels, channels)
    response = jnp.einsum("brwq,qo->brwo", flattened, w_fwd, preferred_element_type=jnp.float32)

    back_filtered = run_filter(
        first, tables, grad_wide, grad_totals, row_count, lon_count, lon_total, True
    )
    w_back = jnp.transpose(weight, (0, 2, 1)).reshape(BASIS * channels, channels)
    grad_input = jnp.einsum(
        "bpwq,qc->bpwc", back_filtered, w_back, preferred_element_type=jnp.float32
    )
    partial_value = jnp.einsum(
        "brwq,brwo->qo", flattened, cotangent, preferred_element_type=jnp.float32
    )
    partial_value = partial_value.reshape(BASIS, channels, channels)
    reduced = ring_scatter(partial_value, "lon", 2)
    reduced = ring_scatter(reduced, "lat", 1)
    grad_weight = reduced / jnp.sqrt(jnp.float32(members * height * lon_total))
    return (response, grad_input, grad_weight)


def solution(mesh):
    placed = (
        P("grp", "lat", "lon", None),
        P("grp", "lat", "lon", None),
        P(),
        P(),
        P(),
        P(),
        P(),
        P(),
    )
    return jax.shard_map(
        on_device,
        mesh=mesh,
        in_specs=placed,
        out_specs=(
            P("grp", "lat", "lon", None),
            P("grp", "lat", "lon", None),
            P("grp", "lat", "lon"),
        ),
        check_vma=False,
    )
```

```python
import functools

import jax
import jax.numpy as jnp
from jax import lax
from jax.experimental import pallas as pl
from jax.experimental.pallas import tpu as pltpu
from jax.sharding import PartitionSpec as P

BASIS = 9
REACH = 2
RIM = 16
POLAR = 2


def with_halo(block, sides, width, periodic):
    for axis, dim in sides:
        count = lax.axis_size(axis)
        forward = [(i, i + 1) for i in range(count - 1)]
        if periodic:
            forward.append((count - 1, 0))
        backward = [(target, source) for source, target in forward]
        low = lax.ppermute(
            lax.slice_in_dim(block, block.shape[dim] - width, None, axis=dim), axis, forward
        )
        high = lax.ppermute(lax.slice_in_dim(block, 0, width, axis=dim), axis, backward)
        block = jnp.concatenate([low, block, high], axis=dim)
    return block


def extend(grid_field, padded):
    grid_field = with_halo(grid_field, (("lat", 1),), REACH, False)
    grid_field = with_halo(grid_field, (("lon", 2),), RIM, True)
    extra = padded - grid_field.shape[2]
    return jnp.pad(grid_field, ((0, 0), (0, 0), (0, extra), (0, 0)))


def ring_sum(value, axis):
    count = lax.axis_size(axis)
    total = value
    for shift in range(1, count):
        pairs = [(i, (i + shift) % count) for i in range(count)]
        total = total + lax.ppermute(value, axis, pairs)
    return total


def ring_scatter(value, axis, dim):
    count = lax.axis_size(axis)
    own = lax.axis_index(axis)
    block = value.shape[dim] // count
    total = lax.dynamic_slice_in_dim(value, own * block, block, dim)
    for shift in range(1, count):
        pairs = [(i, (i + shift) % count) for i in range(count)]
        piece = lax.dynamic_slice_in_dim(value, ((own + shift) % count) * block, block, dim)
        sent = lax.ppermute(piece.astype(jnp.bfloat16), axis, pairs)
        total = total + sent.astype(jnp.float32)
    return total


def paired_scatter(value, axis, dim):
    count = lax.axis_size(axis)
    if count % 2:
        return ring_scatter(value, axis, dim)
    own = lax.axis_index(axis)
    parity = own % 2
    group = own // 2
    groups = count // 2
    block = value.shape[dim] // count
    shape = value.shape[:dim] + (groups, 2, block) + value.shape[dim + 1:]
    split = value.reshape(shape)
    keep = lax.dynamic_index_in_dim(split, parity, dim + 1, keepdims=False)
    give = lax.dynamic_index_in_dim(split, 1 - parity, dim + 1, keepdims=False)
    swap = [(i, i ^ 1) for i in range(count)]
    merged = keep + lax.ppermute(give, axis, swap)
    total = lax.dynamic_index_in_dim(merged, group, dim, keepdims=False)
    for shift in range(1, groups):
        pairs = [
            (2 * g + p, 2 * ((g + shift) % groups) + p) for g in range(groups) for p in range(2)
        ]
        piece = lax.dynamic_index_in_dim(merged, (group + shift) % groups, dim, keepdims=False)
        sent = lax.ppermute(piece.astype(jnp.bfloat16), axis, pairs)
        total = total + sent.astype(jnp.float32)
    return total


def filter_kernel(
    first_ref, src_ref, start_ref, span_ref, basis_ref, scale_ref, field_ref, total_ref,
    out_ref, acc_ref, *, slots, height, lon_count, lon_total, backward,
):
    r = pl.program_id(1)
    first_row = first_ref[0]
    padded = field_ref.shape[2]
    channels = field_ref.shape[3]
    acc_ref[...] = jnp.zeros(acc_ref.shape, jnp.float32)
    out_col = lax.broadcasted_iota(jnp.int32, (lon_count, padded), 0)
    in_col = lax.broadcasted_iota(jnp.int32, (lon_count, padded), 1) - RIM
    offset = out_col - in_col if backward else in_col - out_col

    def add_slot(row, table_row, slot, scale):
        start = start_ref[table_row, slot]
        span = span_ref[table_row, slot]
        basis = basis_ref[table_row, slot]
        narrow = span < lon_total
        band = ((offset >= start) & (offset < start + span) & narrow).astype(jnp.bfloat16)
        boxed = jnp.dot(band, field_ref[0, row], preferred_element_type=jnp.float32)
        full = jnp.where(narrow, 0.0, 1.0).astype(jnp.float32)
        boxed = boxed + full * total_ref[0, row]
        acc_ref[basis] = acc_ref[basis] + scale * boxed

    if backward:
        target = first_row + r
        for e in range(2 * REACH + 1):
            row = r + e
            global_row = target + e - REACH
            inside = (global_row >= 0) & (global_row < height)
            table_row = jnp.clip(global_row, 0, height - 1)
            for slot in range(slots):
                scale = scale_ref[table_row, slot]
                hit = inside & (src_ref[table_row, slot] == target) & (scale != 0.0)

                @pl.when(hit)
                def _():
                    add_slot(row, table_row, slot, scale)
    else:
        table_row = first_row + r
        for slot in range(slots):
            row = src_ref[table_row, slot] - first_row + REACH
            add_slot(row, table_row, slot, scale_ref[table_row, slot])

    for k in range(BASIS):
        out_ref[0, 0, :, k * channels:(k + 1) * channels] = acc_ref[k].astype(jnp.bfloat16)


def run_filter(first, tables, field, totals, row_count, lon_count, lon_total, backward):
    members, window, padded, channels = field.shape
    height, slots = tables[0].shape
    smem = pl.BlockSpec(memory_space=pltpu.SMEM)
    kernel = functools.partial(
        filter_kernel,
        slots=slots,
        height=height,
        lon_count=lon_count,
        lon_total=lon_total,
        backward=backward,
    )
    return pl.pallas_call(
        kernel,
        grid=(members, row_count),
        in_specs=[smem] * 6
        + [
            pl.BlockSpec((1, window, padded, channels), lambda b, r: (b, 0, 0, 0)),
            pl.BlockSpec((1, window, 1, channels), lambda b, r: (b, 0, 0, 0)),
        ],
        out_specs=pl.BlockSpec(
            (1, 1, lon_count, BASIS * channels), lambda b, r: (b, r, 0, 0)
        ),
        out_shape=jax.ShapeDtypeStruct(
            (members, row_count, lon_count, BASIS * channels), jnp.bfloat16
        ),
        scratch_shapes=[pltpu.VMEM((BASIS, lon_count, channels), jnp.float32)],
    )(first, *tables, field, totals[:, :, None, :])


def on_device(inputs, cotangent, weight, src_rows, lon_start, lon_span, basis_idx, quad_weight):
    members, row_count, lon_count, channels = inputs.shape
    lon_total = lon_count * lax.axis_size("lon")
    height = row_count * lax.axis_size("lat")
    first_row = lax.axis_index("lat") * row_count
    padded = -(-(lon_count + 2 * RIM) // 128) * 128
    weighting = quad_weight / jnp.sqrt(lon_span.astype(jnp.float32))
    first = jnp.reshape(first_row, (1,)).astype(jnp.int32)
    tables = (src_rows, lon_start, lon_span, basis_idx, weighting)

    both = extend(jnp.concatenate([inputs, cotangent], axis=3), padded)
    widened = both[..., :channels]
    grad_wide = both[..., channels:]
    row_sums = jnp.stack(
        [jnp.sum(inputs, axis=2, dtype=jnp.float32), jnp.sum(cotangent, axis=2, dtype=jnp.float32)]
    )
    local_totals = ring_sum(row_sums, "lon")
    if row_count >= POLAR + REACH:
        framed = jnp.pad(local_totals, ((0, 0), (0, 0), (REACH, REACH), (0, 0)))
    else:
        framed = with_halo(local_totals, (("lat", 2),), REACH, False)
    totals, grad_totals = framed[0], framed[1]

    flattened = run_filter(first, tables, widened, totals, row_count, lon_count, lon_total, False)
    w_fwd = weight.reshape(BASIS * channels, channels)
    response = jnp.einsum("brwq,qo->brwo", flattened, w_fwd, preferred_element_type=jnp.float32)

    back_filtered = run_filter(
        first, tables, grad_wide, grad_totals, row_count, lon_count, lon_total, True
    )
    w_back = jnp.transpose(weight, (0, 2, 1)).reshape(BASIS * channels, channels)
    grad_input = jnp.einsum(
        "bpwq,qc->bpwc", back_filtered, w_back, preferred_element_type=jnp.float32
    )
    partial_value = jnp.einsum(
        "brwq,brwo->qo", flattened, cotangent, preferred_element_type=jnp.float32
    )
    partial_value = partial_value.reshape(BASIS, channels, channels)
    reduced = paired_scatter(partial_value, "lon", 2)
    reduced = ring_scatter(reduced, "lat", 1)
    grad_weight = reduced / jnp.sqrt(jnp.float32(members * height * lon_total))
    return (response, grad_input, grad_weight)


def solution(mesh):
    placed = (
        P("grp", "lat", "lon", None),
        P("grp", "lat", "lon", None),
        P(),
        P(),
        P(),
        P(),
        P(),
        P(),
    )
    return jax.shard_map(
        on_device,
        mesh=mesh,
        in_specs=placed,
        out_specs=(
            P("grp", "lat", "lon", None),
            P("grp", "lat", "lon", None),
            P("grp", "lat", "lon"),
        ),
        check_vma=False,
    )
```

```python
import functools

import jax
import jax.numpy as jnp
from jax import lax
from jax.experimental import pallas as pl
from jax.experimental.pallas import tpu as pltpu
from jax.sharding import PartitionSpec as P

BASIS = 9
REACH = 2
RIM = 16
POLAR = 2


def with_halo(block, sides, width, periodic):
    for axis, dim in sides:
        count = lax.axis_size(axis)
        forward = [(i, i + 1) for i in range(count - 1)]
        if periodic:
            forward.append((count - 1, 0))
        backward = [(target, source) for source, target in forward]
        low = lax.ppermute(
            lax.slice_in_dim(block, block.shape[dim] - width, None, axis=dim), axis, forward
        )
        high = lax.ppermute(lax.slice_in_dim(block, 0, width, axis=dim), axis, backward)
        block = jnp.concatenate([low, block, high], axis=dim)
    return block


def extend(grid_field, padded):
    grid_field = with_halo(grid_field, (("lat", 1),), REACH, False)
    grid_field = with_halo(grid_field, (("lon", 2),), RIM, True)
    extra = padded - grid_field.shape[2]
    return jnp.pad(grid_field, ((0, 0), (0, 0), (0, extra), (0, 0)))


def ring_sum(value, axis):
    count = lax.axis_size(axis)
    total = value
    for shift in range(1, count):
        pairs = [(i, (i + shift) % count) for i in range(count)]
        total = total + lax.ppermute(value, axis, pairs)
    return total


def ring_scatter(value, axis, dim):
    count = lax.axis_size(axis)
    own = lax.axis_index(axis)
    block = value.shape[dim] // count
    total = lax.dynamic_slice_in_dim(value, own * block, block, dim)
    for shift in range(1, count):
        pairs = [(i, (i + shift) % count) for i in range(count)]
        piece = lax.dynamic_slice_in_dim(value, ((own + shift) % count) * block, block, dim)
        sent = lax.ppermute(piece.astype(jnp.bfloat16), axis, pairs)
        total = total + sent.astype(jnp.float32)
    return total


def filter_kernel(
    first_ref, src_ref, start_ref, span_ref, basis_ref, scale_ref, field_ref, total_ref,
    out_ref, acc_ref, *hits_ref, slots, height, lon_count, lon_total, backward,
):
    r = pl.program_id(1)
    first_row = first_ref[0]
    padded = field_ref.shape[2]
    channels = field_ref.shape[3]
    acc_ref[...] = jnp.zeros(acc_ref.shape, jnp.float32)
    out_col = lax.broadcasted_iota(jnp.int32, (lon_count, padded), 0)
    in_col = lax.broadcasted_iota(jnp.int32, (lon_count, padded), 1) - RIM
    offset = out_col - in_col if backward else in_col - out_col

    def add_slot(row, table_row, slot, scale):
        start = start_ref[table_row, slot]
        span = span_ref[table_row, slot]
        basis = basis_ref[table_row, slot]
        narrow = span < lon_total
        band = ((offset >= start) & (offset < start + span) & narrow).astype(jnp.bfloat16)
        boxed = jnp.dot(band, field_ref[0, row], preferred_element_type=jnp.float32)
        full = jnp.where(narrow, 0.0, 1.0).astype(jnp.float32)
        boxed = boxed + full * total_ref[0, row]
        acc_ref[basis] = acc_ref[basis] + scale * boxed

    if backward:
        target = first_row + r
        list_ref = hits_ref[0]

        def collect(i, count):
            e = i // slots
            slot = i % slots
            global_row = target + e - REACH
            inside = (global_row >= 0) & (global_row < height)
            table_row = jnp.clip(global_row, 0, height - 1)
            scale = scale_ref[table_row, slot]
            hit = inside & (src_ref[table_row, slot] == target) & (scale != 0.0)
            list_ref[count] = i
            return count + hit.astype(jnp.int32)

        count = lax.fori_loop(0, (2 * REACH + 1) * slots, collect, jnp.int32(0))

        def accumulate(j, carry):
            i = list_ref[j]
            e = i // slots
            slot = i % slots
            table_row = target + e - REACH
            add_slot(r + e, table_row, slot, scale_ref[table_row, slot])
            return carry

        lax.fori_loop(0, count, accumulate, jnp.int32(0))
    else:
        table_row = first_row + r
        for slot in range(slots):
            row = src_ref[table_row, slot] - first_row + REACH
            add_slot(row, table_row, slot, scale_ref[table_row, slot])

    for k in range(BASIS):
        out_ref[0, 0, :, k * channels:(k + 1) * channels] = acc_ref[k].astype(jnp.bfloat16)


def run_filter(first, tables, field, totals, row_count, lon_count, lon_total, backward):
    members, window, padded, channels = field.shape
    height, slots = tables[0].shape
    smem = pl.BlockSpec(memory_space=pltpu.SMEM)
    kernel = functools.partial(
        filter_kernel,
        slots=slots,
        height=height,
        lon_count=lon_count,
        lon_total=lon_total,
        backward=backward,
    )
    return pl.pallas_call(
        kernel,
        grid=(members, row_count),
        in_specs=[smem] * 6
        + [
            pl.BlockSpec((1, window, padded, channels), lambda b, r: (b, 0, 0, 0)),
            pl.BlockSpec((1, window, 1, channels), lambda b, r: (b, 0, 0, 0)),
        ],
        out_specs=pl.BlockSpec(
            (1, 1, lon_count, BASIS * channels), lambda b, r: (b, r, 0, 0)
        ),
        out_shape=jax.ShapeDtypeStruct(
            (members, row_count, lon_count, BASIS * channels), jnp.bfloat16
        ),
        scratch_shapes=[pltpu.VMEM((BASIS, lon_count, channels), jnp.float32)]
        + ([pltpu.SMEM(((2 * REACH + 1) * slots,), jnp.int32)] if backward else []),
    )(first, *tables, field, totals[:, :, None, :])


def on_device(inputs, cotangent, weight, src_rows, lon_start, lon_span, basis_idx, quad_weight):
    members, row_count, lon_count, channels = inputs.shape
    lon_total = lon_count * lax.axis_size("lon")
    height = row_count * lax.axis_size("lat")
    first_row = lax.axis_index("lat") * row_count
    padded = -(-(lon_count + 2 * RIM) // 128) * 128
    weighting = quad_weight / jnp.sqrt(lon_span.astype(jnp.float32))
    first = jnp.reshape(first_row, (1,)).astype(jnp.int32)
    tables = (src_rows, lon_start, lon_span, basis_idx, weighting)

    both = extend(jnp.concatenate([inputs, cotangent], axis=3), padded)
    widened = both[..., :channels]
    grad_wide = both[..., channels:]
    row_sums = jnp.stack(
        [jnp.sum(inputs, axis=2, dtype=jnp.float32), jnp.sum(cotangent, axis=2, dtype=jnp.float32)]
    )
    local_totals = ring_sum(row_sums, "lon")
    if row_count >= POLAR + REACH:
        framed = jnp.pad(local_totals, ((0, 0), (0, 0), (REACH, REACH), (0, 0)))
    else:
        framed = with_halo(local_totals, (("lat", 2),), REACH, False)
    totals, grad_totals = framed[0], framed[1]

    flattened = run_filter(first, tables, widened, totals, row_count, lon_count, lon_total, False)
    w_fwd = weight.reshape(BASIS * channels, channels)
    response = jnp.einsum("brwq,qo->brwo", flattened, w_fwd, preferred_element_type=jnp.float32)

    back_filtered = run_filter(
        first, tables, grad_wide, grad_totals, row_count, lon_count, lon_total, True
    )
    w_back = jnp.transpose(weight, (0, 2, 1)).reshape(BASIS * channels, channels)
    grad_input = jnp.einsum(
        "bpwq,qc->bpwc", back_filtered, w_back, preferred_element_type=jnp.float32
    )
    partial_value = jnp.einsum(
        "brwq,brwo->qo", flattened, cotangent, preferred_element_type=jnp.float32
    )
    partial_value = partial_value.reshape(BASIS, channels, channels)
    reduced = ring_scatter(partial_value, "lon", 2)
    reduced = ring_scatter(reduced, "lat", 1)
    grad_weight = reduced / jnp.sqrt(jnp.float32(members * height * lon_total))
    return (response, grad_input, grad_weight)


def solution(mesh):
    placed = (
        P("grp", "lat", "lon", None),
        P("grp", "lat", "lon", None),
        P(),
        P(),
        P(),
        P(),
        P(),
        P(),
    )
    return jax.shard_map(
        on_device,
        mesh=mesh,
        in_specs=placed,
        out_specs=(
            P("grp", "lat", "lon", None),
            P("grp", "lat", "lon", None),
            P("grp", "lat", "lon"),
        ),
        check_vma=False,
    )
```

```python
import functools

import jax
import jax.numpy as jnp
from jax import lax
from jax.experimental import pallas as pl
from jax.experimental.pallas import tpu as pltpu
from jax.sharding import PartitionSpec as P

BASIS = 9
REACH = 2
RIM = 16
POLAR = 2


def with_halo(block, sides, width, periodic):
    for axis, dim in sides:
        count = lax.axis_size(axis)
        forward = [(i, i + 1) for i in range(count - 1)]
        if periodic:
            forward.append((count - 1, 0))
        backward = [(target, source) for source, target in forward]
        low = lax.ppermute(
            lax.slice_in_dim(block, block.shape[dim] - width, None, axis=dim), axis, forward
        )
        high = lax.ppermute(lax.slice_in_dim(block, 0, width, axis=dim), axis, backward)
        block = jnp.concatenate([low, block, high], axis=dim)
    return block


def extend(grid_field, padded):
    grid_field = with_halo(grid_field, (("lat", 1),), REACH, False)
    grid_field = with_halo(grid_field, (("lon", 2),), RIM, True)
    extra = padded - grid_field.shape[2]
    return jnp.pad(grid_field, ((0, 0), (0, 0), (0, extra), (0, 0)))


def ring_sum(value, axis):
    count = lax.axis_size(axis)
    total = value
    for shift in range(1, count):
        pairs = [(i, (i + shift) % count) for i in range(count)]
        total = total + lax.ppermute(value, axis, pairs)
    return total


def ring_scatter(value, axis, dim):
    count = lax.axis_size(axis)
    own = lax.axis_index(axis)
    block = value.shape[dim] // count
    total = lax.dynamic_slice_in_dim(value, own * block, block, dim)
    for shift in range(1, count):
        pairs = [(i, (i + shift) % count) for i in range(count)]
        piece = lax.dynamic_slice_in_dim(value, ((own + shift) % count) * block, block, dim)
        sent = lax.ppermute(piece.astype(jnp.bfloat16), axis, pairs)
        total = total + sent.astype(jnp.float32)
    return total


def filter_kernel(
    first_ref, src_ref, start_ref, span_ref, basis_ref, scale_ref, field_ref, total_ref,
    out_ref, acc_ref, *, slots, height, lon_count, lon_total, backward,
):
    r = pl.program_id(1)
    first_row = first_ref[0]
    padded = field_ref.shape[2]
    channels = field_ref.shape[3]
    acc_ref[...] = jnp.zeros(acc_ref.shape, jnp.float32)
    out_col = lax.broadcasted_iota(jnp.int32, (lon_count, padded), 0)
    in_col = lax.broadcasted_iota(jnp.int32, (lon_count, padded), 1) - RIM
    offset = out_col - in_col if backward else in_col - out_col

    def add_slot(row, table_row, slot, scale):
        start = start_ref[table_row, slot]
        span = span_ref[table_row, slot]
        basis = basis_ref[table_row, slot]
        narrow = span < lon_total
        band = ((offset >= start) & (offset < start + span) & narrow).astype(jnp.bfloat16)
        boxed = jnp.dot(band, field_ref[0, row], preferred_element_type=jnp.float32)
        full = jnp.where(narrow, 0.0, 1.0).astype(jnp.float32)
        boxed = boxed + full * total_ref[0, row]
        acc_ref[basis] = acc_ref[basis] + scale * boxed

    if backward:
        target = first_row + r
        for e in range(2 * REACH + 1):
            row = r + e
            global_row = target + e - REACH
            inside = (global_row >= 0) & (global_row < height)
            table_row = jnp.clip(global_row, 0, height - 1)
            for slot in range(slots):
                scale = scale_ref[table_row, slot]
                hit = inside & (src_ref[table_row, slot] == target) & (scale != 0.0)

                @pl.when(hit)
                def _():
                    add_slot(row, table_row, slot, scale)
    else:
        table_row = first_row + r
        for slot in range(slots):
            row = src_ref[table_row, slot] - first_row + REACH
            add_slot(row, table_row, slot, scale_ref[table_row, slot])

    for k in range(BASIS):
        out_ref[0, 0, :, k * channels:(k + 1) * channels] = acc_ref[k].astype(jnp.bfloat16)


def run_filter(first, tables, field, totals, row_count, lon_count, lon_total, backward):
    members, window, padded, channels = field.shape
    height, slots = tables[0].shape
    smem = pl.BlockSpec(memory_space=pltpu.SMEM)
    kernel = functools.partial(
        filter_kernel,
        slots=slots,
        height=height,
        lon_count=lon_count,
        lon_total=lon_total,
        backward=backward,
    )
    return pl.pallas_call(
        kernel,
        grid=(members, row_count),
        in_specs=[smem] * 6
        + [
            pl.BlockSpec((1, window, padded, channels), lambda b, r: (b, 0, 0, 0)),
            pl.BlockSpec((1, window, 1, channels), lambda b, r: (b, 0, 0, 0)),
        ],
        out_specs=pl.BlockSpec(
            (1, 1, lon_count, BASIS * channels), lambda b, r: (b, r, 0, 0)
        ),
        out_shape=jax.ShapeDtypeStruct(
            (members, row_count, lon_count, BASIS * channels), jnp.bfloat16
        ),
        scratch_shapes=[pltpu.VMEM((BASIS, lon_count, channels), jnp.float32)],
    )(first, *tables, field, totals[:, :, None, :])


def on_device(inputs, cotangent, weight, src_rows, lon_start, lon_span, basis_idx, quad_weight):
    members, row_count, lon_count, channels = inputs.shape
    lon_total = lon_count * lax.axis_size("lon")
    height = row_count * lax.axis_size("lat")
    first_row = lax.axis_index("lat") * row_count
    padded = -(-(lon_count + 2 * RIM) // 128) * 128
    weighting = quad_weight / jnp.sqrt(lon_span.astype(jnp.float32))
    first = jnp.reshape(first_row, (1,)).astype(jnp.int32)
    tables = (src_rows, lon_start, lon_span, basis_idx, weighting)

    both = extend(jnp.concatenate([inputs, cotangent], axis=3), padded)
    widened = both[..., :channels]
    grad_wide = both[..., channels:]
    row_sums = jnp.stack(
        [jnp.sum(inputs, axis=2, dtype=jnp.float32), jnp.sum(cotangent, axis=2, dtype=jnp.float32)]
    )
    local_totals = ring_sum(row_sums, "lon")
    if row_count >= POLAR + REACH:
        framed = jnp.pad(local_totals, ((0, 0), (0, 0), (REACH, REACH), (0, 0)))
    else:
        framed = with_halo(local_totals, (("lat", 2),), REACH, False)
    totals, grad_totals = framed[0], framed[1]

    flattened = run_filter(first, tables, widened, totals, row_count, lon_count, lon_total, False)
    w_fwd = weight.reshape(BASIS * channels, channels)
    response = jnp.einsum("brwq,qo->brwo", flattened, w_fwd, preferred_element_type=jnp.float32)

    partial_value = jnp.einsum(
        "brwq,brwo->qo", flattened, cotangent, preferred_element_type=jnp.float32
    )
    partial_value = partial_value.reshape(BASIS, channels, channels)
    reduced = ring_scatter(partial_value, "lon", 2)
    grad_wide, grad_totals, reduced = lax.optimization_barrier((grad_wide, grad_totals, reduced))
    reduced = ring_scatter(reduced, "lat", 1)
    back_filtered = run_filter(
        first, tables, grad_wide, grad_totals, row_count, lon_count, lon_total, True
    )
    w_back = jnp.transpose(weight, (0, 2, 1)).reshape(BASIS * channels, channels)
    grad_input = jnp.einsum(
        "bpwq,qc->bpwc", back_filtered, w_back, preferred_element_type=jnp.float32
    )
    grad_weight = reduced / jnp.sqrt(jnp.float32(members * height * lon_total))
    return (response, grad_input, grad_weight)


def solution(mesh):
    placed = (
        P("grp", "lat", "lon", None),
        P("grp", "lat", "lon", None),
        P(),
        P(),
        P(),
        P(),
        P(),
        P(),
    )
    return jax.shard_map(
        on_device,
        mesh=mesh,
        in_specs=placed,
        out_specs=(
            P("grp", "lat", "lon", None),
            P("grp", "lat", "lon", None),
            P("grp", "lat", "lon"),
        ),
        check_vma=False,
    )
```

```python
import functools

import jax
import jax.numpy as jnp
from jax import lax
from jax.experimental import pallas as pl
from jax.experimental.pallas import tpu as pltpu
from jax.sharding import PartitionSpec as P

BASIS = 9
REACH = 2
RIM = 16
POLAR = 2


def with_halo(block, sides, width, periodic):
    for axis, dim in sides:
        count = lax.axis_size(axis)
        forward = [(i, i + 1) for i in range(count - 1)]
        if periodic:
            forward.append((count - 1, 0))
        backward = [(target, source) for source, target in forward]
        low = lax.ppermute(
            lax.slice_in_dim(block, block.shape[dim] - width, None, axis=dim), axis, forward
        )
        high = lax.ppermute(lax.slice_in_dim(block, 0, width, axis=dim), axis, backward)
        block = jnp.concatenate([low, block, high], axis=dim)
    return block


def extend(grid_field, padded):
    grid_field = with_halo(grid_field, (("lat", 1),), REACH, False)
    grid_field = with_halo(grid_field, (("lon", 2),), RIM, True)
    extra = padded - grid_field.shape[2]
    return jnp.pad(grid_field, ((0, 0), (0, 0), (0, extra), (0, 0)))


def ring_sum(value, axis):
    count = lax.axis_size(axis)
    total = value
    for shift in range(1, count):
        pairs = [(i, (i + shift) % count) for i in range(count)]
        total = total + lax.ppermute(value, axis, pairs)
    return total


def ring_scatter(value, axis, dim):
    count = lax.axis_size(axis)
    own = lax.axis_index(axis)
    block = value.shape[dim] // count
    total = lax.dynamic_slice_in_dim(value, own * block, block, dim)
    for shift in range(1, count):
        pairs = [(i, (i + shift) % count) for i in range(count)]
        piece = lax.dynamic_slice_in_dim(value, ((own + shift) % count) * block, block, dim)
        sent = lax.ppermute(piece.astype(jnp.bfloat16), axis, pairs)
        total = total + sent.astype(jnp.float32)
    return total


def paired_scatter(value, axis, dim):
    count = lax.axis_size(axis)
    own = lax.axis_index(axis)
    parity = own % 2
    group = own // 2
    groups = count // 2
    half = value.shape[dim] // 2
    block = half // groups
    keep = lax.dynamic_slice_in_dim(value, parity * half, half, dim)
    give = lax.dynamic_slice_in_dim(value, (1 - parity) * half, half, dim)
    swap = [(i, i ^ 1) for i in range(count)]
    merged = keep + lax.ppermute(give.astype(jnp.bfloat16), axis, swap).astype(jnp.float32)
    total = lax.dynamic_slice_in_dim(merged, group * block, block, dim)
    for shift in range(1, groups):
        pairs = [
            (2 * g + p, 2 * ((g + shift) % groups) + p) for g in range(groups) for p in range(2)
        ]
        piece = lax.dynamic_slice_in_dim(merged, ((group + shift) % groups) * block, block, dim)
        sent = lax.ppermute(piece.astype(jnp.bfloat16), axis, pairs)
        total = total + sent.astype(jnp.float32)
    return total


def filter_kernel(
    first_ref, src_ref, start_ref, span_ref, basis_ref, scale_ref, field_ref, total_ref,
    out_ref, acc_ref, *, slots, height, lon_count, lon_total, backward,
):
    r = pl.program_id(1)
    first_row = first_ref[0]
    padded = field_ref.shape[2]
    channels = field_ref.shape[3]
    acc_ref[...] = jnp.zeros(acc_ref.shape, jnp.float32)
    out_col = lax.broadcasted_iota(jnp.int32, (lon_count, padded), 0)
    in_col = lax.broadcasted_iota(jnp.int32, (lon_count, padded), 1) - RIM
    offset = out_col - in_col if backward else in_col - out_col

    def add_slot(row, table_row, slot, scale):
        start = start_ref[table_row, slot]
        span = span_ref[table_row, slot]
        basis = basis_ref[table_row, slot]
        narrow = span < lon_total
        band = ((offset >= start) & (offset < start + span) & narrow).astype(jnp.bfloat16)
        boxed = jnp.dot(band, field_ref[0, row], preferred_element_type=jnp.float32)
        full = jnp.where(narrow, 0.0, 1.0).astype(jnp.float32)
        boxed = boxed + full * total_ref[0, row]
        acc_ref[basis] = acc_ref[basis] + scale * boxed

    if backward:
        target = first_row + r
        for e in range(2 * REACH + 1):
            row = r + e
            global_row = target + e - REACH
            inside = (global_row >= 0) & (global_row < height)
            table_row = jnp.clip(global_row, 0, height - 1)
            for slot in range(slots):
                scale = scale_ref[table_row, slot]
                hit = inside & (src_ref[table_row, slot] == target) & (scale != 0.0)

                @pl.when(hit)
                def _():
                    add_slot(row, table_row, slot, scale)
    else:
        table_row = first_row + r
        for slot in range(slots):
            row = src_ref[table_row, slot] - first_row + REACH
            add_slot(row, table_row, slot, scale_ref[table_row, slot])

    for k in range(BASIS):
        out_ref[0, 0, :, k * channels:(k + 1) * channels] = acc_ref[k].astype(jnp.bfloat16)


def run_filter(first, tables, field, totals, row_count, lon_count, lon_total, backward):
    members, window, padded, channels = field.shape
    height, slots = tables[0].shape
    smem = pl.BlockSpec(memory_space=pltpu.SMEM)
    kernel = functools.partial(
        filter_kernel,
        slots=slots,
        height=height,
        lon_count=lon_count,
        lon_total=lon_total,
        backward=backward,
    )
    return pl.pallas_call(
        kernel,
        grid=(members, row_count),
        in_specs=[smem] * 6
        + [
            pl.BlockSpec((1, window, padded, channels), lambda b, r: (b, 0, 0, 0)),
            pl.BlockSpec((1, window, 1, channels), lambda b, r: (b, 0, 0, 0)),
        ],
        out_specs=pl.BlockSpec(
            (1, 1, lon_count, BASIS * channels), lambda b, r: (b, r, 0, 0)
        ),
        out_shape=jax.ShapeDtypeStruct(
            (members, row_count, lon_count, BASIS * channels), jnp.bfloat16
        ),
        scratch_shapes=[pltpu.VMEM((BASIS, lon_count, channels), jnp.float32)],
    )(first, *tables, field, totals[:, :, None, :])


def on_device(inputs, cotangent, weight, src_rows, lon_start, lon_span, basis_idx, quad_weight):
    members, row_count, lon_count, channels = inputs.shape
    lon_total = lon_count * lax.axis_size("lon")
    height = row_count * lax.axis_size("lat")
    first_row = lax.axis_index("lat") * row_count
    padded = -(-(lon_count + 2 * RIM) // 128) * 128
    weighting = quad_weight / jnp.sqrt(lon_span.astype(jnp.float32))
    first = jnp.reshape(first_row, (1,)).astype(jnp.int32)
    tables = (src_rows, lon_start, lon_span, basis_idx, weighting)

    both = extend(jnp.concatenate([inputs, cotangent], axis=3), padded)
    widened = both[..., :channels]
    grad_wide = both[..., channels:]
    row_sums = jnp.stack(
        [jnp.sum(inputs, axis=2, dtype=jnp.float32), jnp.sum(cotangent, axis=2, dtype=jnp.float32)]
    )
    local_totals = ring_sum(row_sums, "lon")
    if row_count >= POLAR + REACH:
        framed = jnp.pad(local_totals, ((0, 0), (0, 0), (REACH, REACH), (0, 0)))
    else:
        framed = with_halo(local_totals, (("lat", 2),), REACH, False)
    totals, grad_totals = framed[0], framed[1]

    flattened = run_filter(first, tables, widened, totals, row_count, lon_count, lon_total, False)
    w_fwd = weight.reshape(BASIS * channels, channels)
    response = jnp.einsum("brwq,qo->brwo", flattened, w_fwd, preferred_element_type=jnp.float32)

    lon_parts = lax.axis_size("lon")
    if lon_parts % 2 == 0:
        o_block = channels // lon_parts
        mixed = cotangent.reshape(members, row_count, lon_count, lon_parts // 2, 2, o_block)
        mixed = jnp.swapaxes(mixed, 3, 4).reshape(cotangent.shape)
    else:
        mixed = cotangent
    partial_value = jnp.einsum(
        "brwq,brwo->qo", flattened, mixed, preferred_element_type=jnp.float32
    )
    partial_value = partial_value.reshape(BASIS, channels, channels)
    if lon_parts % 2 == 0:
        reduced = paired_scatter(partial_value, "lon", 2)
    else:
        reduced = ring_scatter(partial_value, "lon", 2)
    grad_wide, grad_totals, reduced = lax.optimization_barrier((grad_wide, grad_totals, reduced))
    reduced = ring_scatter(reduced, "lat", 1)
    back_filtered = run_filter(
        first, tables, grad_wide, grad_totals, row_count, lon_count, lon_total, True
    )
    w_back = jnp.transpose(weight, (0, 2, 1)).reshape(BASIS * channels, channels)
    grad_input = jnp.einsum(
        "bpwq,qc->bpwc", back_filtered, w_back, preferred_element_type=jnp.float32
    )
    grad_weight = reduced / jnp.sqrt(jnp.float32(members * height * lon_total))
    return (response, grad_input, grad_weight)


def solution(mesh):
    placed = (
        P("grp", "lat", "lon", None),
        P("grp", "lat", "lon", None),
        P(),
        P(),
        P(),
        P(),
        P(),
        P(),
    )
    return jax.shard_map(
        on_device,
        mesh=mesh,
        in_specs=placed,
        out_specs=(
            P("grp", "lat", "lon", None),
            P("grp", "lat", "lon", None),
            P("grp", "lat", "lon"),
        ),
        check_vma=False,
    )
```

```python
import functools

import jax
import jax.numpy as jnp
from jax import lax
from jax.experimental import pallas as pl
from jax.experimental.pallas import tpu as pltpu
from jax.sharding import PartitionSpec as P

BASIS = 9
REACH = 2
RIM = 16
POLAR = 2


def with_halo(block, sides, width, periodic):
    for axis, dim in sides:
        count = lax.axis_size(axis)
        forward = [(i, i + 1) for i in range(count - 1)]
        if periodic:
            forward.append((count - 1, 0))
        backward = [(target, source) for source, target in forward]
        low = lax.ppermute(
            lax.slice_in_dim(block, block.shape[dim] - width, None, axis=dim), axis, forward
        )
        high = lax.ppermute(lax.slice_in_dim(block, 0, width, axis=dim), axis, backward)
        block = jnp.concatenate([low, block, high], axis=dim)
    return block


def extend(grid_field, padded):
    grid_field = with_halo(grid_field, (("lat", 1),), REACH, False)
    grid_field = with_halo(grid_field, (("lon", 2),), RIM, True)
    extra = padded - grid_field.shape[2]
    return jnp.pad(grid_field, ((0, 0), (0, 0), (0, extra), (0, 0)))


def ring_sum(value, axis):
    count = lax.axis_size(axis)
    total = value
    for shift in range(1, count):
        pairs = [(i, (i + shift) % count) for i in range(count)]
        total = total + lax.ppermute(value, axis, pairs)
    return total


def ring_scatter(value, axis, dim):
    count = lax.axis_size(axis)
    own = lax.axis_index(axis)
    block = value.shape[dim] // count
    total = lax.dynamic_slice_in_dim(value, own * block, block, dim)
    for shift in range(1, count):
        pairs = [(i, (i + shift) % count) for i in range(count)]
        piece = lax.dynamic_slice_in_dim(value, ((own + shift) % count) * block, block, dim)
        sent = lax.ppermute(piece.astype(jnp.bfloat16), axis, pairs)
        total = total + sent.astype(jnp.float32)
    return total


def filter_kernel(
    first_ref, src_ref, start_ref, span_ref, basis_ref, scale_ref, field_ref, total_ref,
    out_ref, acc_ref, *, slots, height, lon_count, lon_total, backward, row_offset,
):
    r = pl.program_id(1) + row_offset
    first_row = first_ref[0]
    padded = field_ref.shape[2]
    channels = field_ref.shape[3]
    acc_ref[...] = jnp.zeros(acc_ref.shape, jnp.float32)
    out_col = lax.broadcasted_iota(jnp.int32, (lon_count, padded), 0)
    in_col = lax.broadcasted_iota(jnp.int32, (lon_count, padded), 1) - RIM
    offset = out_col - in_col if backward else in_col - out_col

    def add_slot(row, table_row, slot, scale):
        start = start_ref[table_row, slot]
        span = span_ref[table_row, slot]
        basis = basis_ref[table_row, slot]
        narrow = span < lon_total
        band = ((offset >= start) & (offset < start + span) & narrow).astype(jnp.bfloat16)
        boxed = jnp.dot(band, field_ref[0, row], preferred_element_type=jnp.float32)
        full = jnp.where(narrow, 0.0, 1.0).astype(jnp.float32)
        boxed = boxed + full * total_ref[0, row]
        acc_ref[basis] = acc_ref[basis] + scale * boxed

    if backward:
        target = first_row + r
        for e in range(2 * REACH + 1):
            row = r + e
            global_row = target + e - REACH
            inside = (global_row >= 0) & (global_row < height)
            table_row = jnp.clip(global_row, 0, height - 1)
            for slot in range(slots):
                scale = scale_ref[table_row, slot]
                hit = inside & (src_ref[table_row, slot] == target) & (scale != 0.0)

                @pl.when(hit)
                def _():
                    add_slot(row, table_row, slot, scale)
    else:
        table_row = first_row + r
        for slot in range(slots):
            row = src_ref[table_row, slot] - first_row + REACH
            add_slot(row, table_row, slot, scale_ref[table_row, slot])

    for k in range(BASIS):
        out_ref[0, 0, :, k * channels:(k + 1) * channels] = acc_ref[k].astype(jnp.bfloat16)


def run_filter(
    first, tables, field, totals, row_count, lon_count, lon_total, backward, row_offset=0
):
    members, window, padded, channels = field.shape
    height, slots = tables[0].shape
    smem = pl.BlockSpec(memory_space=pltpu.SMEM)
    kernel = functools.partial(
        filter_kernel,
        slots=slots,
        height=height,
        lon_count=lon_count,
        lon_total=lon_total,
        backward=backward,
        row_offset=row_offset,
    )
    return pl.pallas_call(
        kernel,
        grid=(members, row_count),
        in_specs=[smem] * 6
        + [
            pl.BlockSpec((1, window, padded, channels), lambda b, r: (b, 0, 0, 0)),
            pl.BlockSpec((1, window, 1, channels), lambda b, r: (b, 0, 0, 0)),
        ],
        out_specs=pl.BlockSpec(
            (1, 1, lon_count, BASIS * channels), lambda b, r: (b, r, 0, 0)
        ),
        out_shape=jax.ShapeDtypeStruct(
            (members, row_count, lon_count, BASIS * channels), jnp.bfloat16
        ),
        scratch_shapes=[pltpu.VMEM((BASIS, lon_count, channels), jnp.float32)],
    )(first, *tables, field, totals[:, :, None, :])


def on_device(inputs, cotangent, weight, src_rows, lon_start, lon_span, basis_idx, quad_weight):
    members, row_count, lon_count, channels = inputs.shape
    lon_total = lon_count * lax.axis_size("lon")
    height = row_count * lax.axis_size("lat")
    first_row = lax.axis_index("lat") * row_count
    padded = -(-(lon_count + 2 * RIM) // 128) * 128
    weighting = quad_weight / jnp.sqrt(lon_span.astype(jnp.float32))
    first = jnp.reshape(first_row, (1,)).astype(jnp.int32)
    tables = (src_rows, lon_start, lon_span, basis_idx, weighting)

    both = extend(jnp.concatenate([inputs, cotangent], axis=3), padded)
    widened = both[..., :channels]
    grad_wide = both[..., channels:]
    row_sums = jnp.stack(
        [jnp.sum(inputs, axis=2, dtype=jnp.float32), jnp.sum(cotangent, axis=2, dtype=jnp.float32)]
    )
    local_totals = ring_sum(row_sums, "lon")
    if row_count >= POLAR + REACH:
        framed = jnp.pad(local_totals, ((0, 0), (0, 0), (REACH, REACH), (0, 0)))
    else:
        framed = with_halo(local_totals, (("lat", 2),), REACH, False)
    totals, grad_totals = framed[0], framed[1]

    flattened = run_filter(first, tables, widened, totals, row_count, lon_count, lon_total, False)
    w_fwd = weight.reshape(BASIS * channels, channels)
    response = jnp.einsum("brwq,qo->brwo", flattened, w_fwd, preferred_element_type=jnp.float32)

    partial_value = jnp.einsum(
        "brwq,brwo->qo", flattened, cotangent, preferred_element_type=jnp.float32
    )
    partial_value = partial_value.reshape(BASIS, channels, channels)
    w_back = jnp.transpose(weight, (0, 2, 1)).reshape(BASIS * channels, channels)

    def backward_rows(field, field_totals, begin, count):
        back_filtered = run_filter(
            first, tables, field, field_totals, count, lon_count, lon_total, True, begin
        )
        return jnp.einsum(
            "bpwq,qc->bpwc", back_filtered, w_back, preferred_element_type=jnp.float32
        )

    early_rows = row_count // 2
    early_wide, early_totals, partial_value = lax.optimization_barrier(
        (grad_wide, grad_totals, partial_value)
    )
    early_input = backward_rows(early_wide, early_totals, 0, early_rows)
    reduced = ring_scatter(partial_value, "lon", 2)
    grad_wide, grad_totals, reduced = lax.optimization_barrier((grad_wide, grad_totals, reduced))
    reduced = ring_scatter(reduced, "lat", 1)
    late_input = backward_rows(grad_wide, grad_totals, early_rows, row_count - early_rows)
    grad_input = jnp.concatenate([early_input, late_input], axis=1)
    grad_weight = reduced / jnp.sqrt(jnp.float32(members * height * lon_total))
    return (response, grad_input, grad_weight)


def solution(mesh):
    placed = (
        P("grp", "lat", "lon", None),
        P("grp", "lat", "lon", None),
        P(),
        P(),
        P(),
        P(),
        P(),
        P(),
    )
    return jax.shard_map(
        on_device,
        mesh=mesh,
        in_specs=placed,
        out_specs=(
            P("grp", "lat", "lon", None),
            P("grp", "lat", "lon", None),
            P("grp", "lat", "lon"),
        ),
        check_vma=False,
    )
```

```python
import functools

import jax
import jax.numpy as jnp
from jax import lax
from jax.experimental import pallas as pl
from jax.experimental.pallas import tpu as pltpu
from jax.sharding import PartitionSpec as P

BASIS = 9
REACH = 2
RIM = 16
POLAR = 2


def with_halo(block, sides, width, periodic):
    for axis, dim in sides:
        count = lax.axis_size(axis)
        forward = [(i, i + 1) for i in range(count - 1)]
        if periodic:
            forward.append((count - 1, 0))
        backward = [(target, source) for source, target in forward]
        low = lax.ppermute(
            lax.slice_in_dim(block, block.shape[dim] - width, None, axis=dim), axis, forward
        )
        high = lax.ppermute(lax.slice_in_dim(block, 0, width, axis=dim), axis, backward)
        block = jnp.concatenate([low, block, high], axis=dim)
    return block


def extend(grid_field, padded):
    grid_field = with_halo(grid_field, (("lat", 1),), REACH, False)
    grid_field = with_halo(grid_field, (("lon", 2),), RIM, True)
    extra = padded - grid_field.shape[2]
    return jnp.pad(grid_field, ((0, 0), (0, 0), (0, extra), (0, 0)))


def ring_sum(value, axis):
    count = lax.axis_size(axis)
    total = value
    for shift in range(1, count):
        pairs = [(i, (i + shift) % count) for i in range(count)]
        total = total + lax.ppermute(value, axis, pairs)
    return total


def ring_scatter(value, axis, dim):
    count = lax.axis_size(axis)
    own = lax.axis_index(axis)
    block = value.shape[dim] // count
    total = lax.dynamic_slice_in_dim(value, own * block, block, dim)
    for shift in range(1, count):
        pairs = [(i, (i + shift) % count) for i in range(count)]
        piece = lax.dynamic_slice_in_dim(value, ((own + shift) % count) * block, block, dim)
        sent = lax.ppermute(piece.astype(jnp.bfloat16), axis, pairs)
        total = total + sent.astype(jnp.float32)
    return total


def filter_kernel(
    first_ref, src_ref, start_ref, span_ref, basis_ref, scale_ref, field_ref, total_ref,
    out_ref, acc_ref, *, slots, height, lon_count, lon_total, backward,
):
    r = pl.program_id(1)
    first_row = first_ref[0]
    padded = field_ref.shape[2]
    channels = field_ref.shape[3]
    acc_ref[...] = jnp.zeros(acc_ref.shape, jnp.float32)
    out_col = lax.broadcasted_iota(jnp.int32, (lon_count, padded), 0)
    in_col = lax.broadcasted_iota(jnp.int32, (lon_count, padded), 1) - RIM
    offset = out_col - in_col if backward else in_col - out_col

    def add_slot(row, table_row, slot, scale):
        start = start_ref[table_row, slot]
        span = span_ref[table_row, slot]
        basis = basis_ref[table_row, slot]
        narrow = span < lon_total
        band = ((offset >= start) & (offset < start + span) & narrow).astype(jnp.bfloat16)
        boxed = jnp.dot(band, field_ref[0, row], preferred_element_type=jnp.float32)
        full = jnp.where(narrow, 0.0, 1.0).astype(jnp.float32)
        boxed = boxed + full * total_ref[0, row]
        acc_ref[basis] = acc_ref[basis] + scale * boxed

    if backward:
        target = first_row + r
        for e in range(2 * REACH + 1):
            row = r + e
            global_row = target + e - REACH
            inside = (global_row >= 0) & (global_row < height)
            table_row = jnp.clip(global_row, 0, height - 1)
            for slot in range(slots):
                scale = scale_ref[table_row, slot]
                hit = inside & (src_ref[table_row, slot] == target) & (scale != 0.0)

                @pl.when(hit)
                def _():
                    add_slot(row, table_row, slot, scale)
    else:
        table_row = first_row + r
        for slot in range(slots):
            row = src_ref[table_row, slot] - first_row + REACH
            add_slot(row, table_row, slot, scale_ref[table_row, slot])

    for k in range(BASIS):
        out_ref[0, 0, :, k * channels:(k + 1) * channels] = acc_ref[k].astype(jnp.bfloat16)


def scatter_kernel(
    first_ref, src_ref, start_ref, span_ref, basis_ref, scale_ref, field_ref, total_ref,
    out_ref, acc_ref, *, slots, height, lon_count, lon_total,
):
    first_row = first_ref[0]
    rows = out_ref.shape[1]
    window = field_ref.shape[1]
    padded = field_ref.shape[2]
    channels = field_ref.shape[3]
    acc_ref[...] = jnp.zeros(acc_ref.shape, jnp.float32)
    out_col = lax.broadcasted_iota(jnp.int32, (lon_count, padded), 0)
    in_col = lax.broadcasted_iota(jnp.int32, (lon_count, padded), 1) - RIM
    offset = out_col - in_col
    for row in range(window):
        global_row = first_row + row - REACH
        inside = (global_row >= 0) & (global_row < height)
        table_row = jnp.clip(global_row, 0, height - 1)
        for slot in range(slots):
            target = src_ref[table_row, slot] - first_row
            scale = scale_ref[table_row, slot]
            hit = inside & (target >= 0) & (target < rows) & (scale != 0.0)

            @pl.when(hit)
            def _():
                start = start_ref[table_row, slot]
                span = span_ref[table_row, slot]
                basis = basis_ref[table_row, slot]
                narrow = span < lon_total
                band = ((offset >= start) & (offset < start + span) & narrow).astype(
                    jnp.bfloat16
                )
                boxed = jnp.dot(band, field_ref[0, row], preferred_element_type=jnp.float32)
                full = jnp.where(narrow, 0.0, 1.0).astype(jnp.float32)
                boxed = boxed + full * total_ref[0, row]
                acc_ref[target, basis] = acc_ref[target, basis] + scale * boxed

    for p in range(rows):
        for k in range(BASIS):
            out_ref[0, p, :, k * channels:(k + 1) * channels] = acc_ref[p, k].astype(
                jnp.bfloat16
            )


def run_scatter(first, tables, field, totals, row_count, lon_count, lon_total):
    members, window, padded, channels = field.shape
    height, slots = tables[0].shape
    smem = pl.BlockSpec(memory_space=pltpu.SMEM)
    kernel = functools.partial(
        scatter_kernel, slots=slots, height=height, lon_count=lon_count, lon_total=lon_total
    )
    return pl.pallas_call(
        kernel,
        grid=(members,),
        in_specs=[smem] * 6
        + [
            pl.BlockSpec((1, window, padded, channels), lambda b: (b, 0, 0, 0)),
            pl.BlockSpec((1, window, 1, channels), lambda b: (b, 0, 0, 0)),
        ],
        out_specs=pl.BlockSpec(
            (1, row_count, lon_count, BASIS * channels), lambda b: (b, 0, 0, 0)
        ),
        out_shape=jax.ShapeDtypeStruct(
            (members, row_count, lon_count, BASIS * channels), jnp.bfloat16
        ),
        scratch_shapes=[pltpu.VMEM((row_count, BASIS, lon_count, channels), jnp.float32)],
    )(first, *tables, field, totals[:, :, None, :])


def run_filter(first, tables, field, totals, row_count, lon_count, lon_total, backward):
    members, window, padded, channels = field.shape
    height, slots = tables[0].shape
    smem = pl.BlockSpec(memory_space=pltpu.SMEM)
    kernel = functools.partial(
        filter_kernel,
        slots=slots,
        height=height,
        lon_count=lon_count,
        lon_total=lon_total,
        backward=backward,
    )
    return pl.pallas_call(
        kernel,
        grid=(members, row_count),
        in_specs=[smem] * 6
        + [
            pl.BlockSpec((1, window, padded, channels), lambda b, r: (b, 0, 0, 0)),
            pl.BlockSpec((1, window, 1, channels), lambda b, r: (b, 0, 0, 0)),
        ],
        out_specs=pl.BlockSpec(
            (1, 1, lon_count, BASIS * channels), lambda b, r: (b, r, 0, 0)
        ),
        out_shape=jax.ShapeDtypeStruct(
            (members, row_count, lon_count, BASIS * channels), jnp.bfloat16
        ),
        scratch_shapes=[pltpu.VMEM((BASIS, lon_count, channels), jnp.float32)],
    )(first, *tables, field, totals[:, :, None, :])


def on_device(inputs, cotangent, weight, src_rows, lon_start, lon_span, basis_idx, quad_weight):
    members, row_count, lon_count, channels = inputs.shape
    lon_total = lon_count * lax.axis_size("lon")
    height = row_count * lax.axis_size("lat")
    first_row = lax.axis_index("lat") * row_count
    padded = -(-(lon_count + 2 * RIM) // 128) * 128
    weighting = quad_weight / jnp.sqrt(lon_span.astype(jnp.float32))
    first = jnp.reshape(first_row, (1,)).astype(jnp.int32)
    tables = (src_rows, lon_start, lon_span, basis_idx, weighting)

    both = extend(jnp.concatenate([inputs, cotangent], axis=3), padded)
    widened = both[..., :channels]
    grad_wide = both[..., channels:]
    row_sums = jnp.stack(
        [jnp.sum(inputs, axis=2, dtype=jnp.float32), jnp.sum(cotangent, axis=2, dtype=jnp.float32)]
    )
    local_totals = ring_sum(row_sums, "lon")
    if row_count >= POLAR + REACH:
        framed = jnp.pad(local_totals, ((0, 0), (0, 0), (REACH, REACH), (0, 0)))
    else:
        framed = with_halo(local_totals, (("lat", 2),), REACH, False)
    totals, grad_totals = framed[0], framed[1]

    flattened = run_filter(first, tables, widened, totals, row_count, lon_count, lon_total, False)
    w_fwd = weight.reshape(BASIS * channels, channels)
    response = jnp.einsum("brwq,qo->brwo", flattened, w_fwd, preferred_element_type=jnp.float32)

    partial_value = jnp.einsum(
        "brwq,brwo->qo", flattened, cotangent, preferred_element_type=jnp.float32
    )
    partial_value = partial_value.reshape(BASIS, channels, channels)
    reduced = ring_scatter(partial_value, "lon", 2)
    grad_wide, grad_totals, reduced = lax.optimization_barrier((grad_wide, grad_totals, reduced))
    reduced = ring_scatter(reduced, "lat", 1)
    back_filtered = run_scatter(
        first, tables, grad_wide, grad_totals, row_count, lon_count, lon_total
    )
    w_back = jnp.transpose(weight, (0, 2, 1)).reshape(BASIS * channels, channels)
    grad_input = jnp.einsum(
        "bpwq,qc->bpwc", back_filtered, w_back, preferred_element_type=jnp.float32
    )
    grad_weight = reduced / jnp.sqrt(jnp.float32(members * height * lon_total))
    return (response, grad_input, grad_weight)


def solution(mesh):
    placed = (
        P("grp", "lat", "lon", None),
        P("grp", "lat", "lon", None),
        P(),
        P(),
        P(),
        P(),
        P(),
        P(),
    )
    return jax.shard_map(
        on_device,
        mesh=mesh,
        in_specs=placed,
        out_specs=(
            P("grp", "lat", "lon", None),
            P("grp", "lat", "lon", None),
            P("grp", "lat", "lon"),
        ),
        check_vma=False,
    )
```

```python
import functools

import jax
import jax.numpy as jnp
from jax import lax
from jax.experimental import pallas as pl
from jax.experimental.pallas import tpu as pltpu
from jax.sharding import PartitionSpec as P

BASIS = 9
REACH = 2
RIM = 16
POLAR = 2


def with_halo(block, sides, width, periodic):
    for axis, dim in sides:
        count = lax.axis_size(axis)
        forward = [(i, i + 1) for i in range(count - 1)]
        if periodic:
            forward.append((count - 1, 0))
        backward = [(target, source) for source, target in forward]
        low = lax.ppermute(
            lax.slice_in_dim(block, block.shape[dim] - width, None, axis=dim), axis, forward
        )
        high = lax.ppermute(lax.slice_in_dim(block, 0, width, axis=dim), axis, backward)
        block = jnp.concatenate([low, block, high], axis=dim)
    return block


def extend(grid_field, padded):
    grid_field = with_halo(grid_field, (("lat", 1),), REACH, False)
    grid_field = with_halo(grid_field, (("lon", 2),), RIM, True)
    extra = padded - grid_field.shape[2]
    return jnp.pad(grid_field, ((0, 0), (0, 0), (0, extra), (0, 0)))


def ring_sum(value, axis):
    count = lax.axis_size(axis)
    total = value
    for shift in range(1, count):
        pairs = [(i, (i + shift) % count) for i in range(count)]
        total = total + lax.ppermute(value, axis, pairs)
    return total


def ring_scatter(value, axis, dim):
    count = lax.axis_size(axis)
    own = lax.axis_index(axis)
    block = value.shape[dim] // count
    total = lax.dynamic_slice_in_dim(value, own * block, block, dim)
    for shift in range(1, count):
        pairs = [(i, (i + shift) % count) for i in range(count)]
        piece = lax.dynamic_slice_in_dim(value, ((own + shift) % count) * block, block, dim)
        sent = lax.ppermute(piece.astype(jnp.bfloat16), axis, pairs)
        total = total + sent.astype(jnp.float32)
    return total


def filter_kernel(
    first_ref, src_ref, start_ref, span_ref, basis_ref, scale_ref, field_ref, total_ref,
    out_ref, acc_ref, *, slots, height, lon_count, lon_total, backward,
):
    r = pl.program_id(1)
    first_row = first_ref[0]
    padded = field_ref.shape[2]
    channels = field_ref.shape[3]
    acc_ref[...] = jnp.zeros(acc_ref.shape, jnp.float32)
    out_col = lax.broadcasted_iota(jnp.int32, (lon_count, padded), 0)
    in_col = lax.broadcasted_iota(jnp.int32, (lon_count, padded), 1) - RIM
    offset = out_col - in_col if backward else in_col - out_col

    def add_slot(row, table_row, slot, scale):
        start = start_ref[table_row, slot]
        span = span_ref[table_row, slot]
        basis = basis_ref[table_row, slot]
        narrow = span < lon_total
        band = ((offset >= start) & (offset < start + span) & narrow).astype(jnp.bfloat16)
        boxed = jnp.dot(band, field_ref[0, row], preferred_element_type=jnp.float32)
        full = jnp.where(narrow, 0.0, 1.0).astype(jnp.float32)
        boxed = boxed + full * total_ref[0, row]
        acc_ref[basis] = acc_ref[basis] + scale * boxed

    if backward:
        target = first_row + r
        for e in range(2 * REACH + 1):
            row = r + e
            global_row = target + e - REACH
            inside = (global_row >= 0) & (global_row < height)
            table_row = jnp.clip(global_row, 0, height - 1)
            for slot in range(slots):
                scale = scale_ref[table_row, slot]
                hit = inside & (src_ref[table_row, slot] == target) & (scale != 0.0)

                @pl.when(hit)
                def _():
                    add_slot(row, table_row, slot, scale)
    else:
        table_row = first_row + r
        for slot in range(slots):
            row = src_ref[table_row, slot] - first_row + REACH
            add_slot(row, table_row, slot, scale_ref[table_row, slot])

    for k in range(BASIS):
        out_ref[0, 0, :, k * channels:(k + 1) * channels] = acc_ref[k].astype(jnp.bfloat16)


def scatter_kernel(
    first_ref, src_ref, start_ref, span_ref, basis_ref, scale_ref, field_ref, total_ref,
    weight_ref, out_ref, acc_ref, *, slots, height, lon_count, lon_total,
):
    first_row = first_ref[0]
    rows = out_ref.shape[1]
    window = field_ref.shape[1]
    padded = field_ref.shape[2]
    channels = field_ref.shape[3]
    acc_ref[...] = jnp.zeros(acc_ref.shape, jnp.float32)
    out_col = lax.broadcasted_iota(jnp.int32, (lon_count, padded), 0)
    in_col = lax.broadcasted_iota(jnp.int32, (lon_count, padded), 1) - RIM
    offset = out_col - in_col
    for row in range(window):
        global_row = first_row + row - REACH
        inside = (global_row >= 0) & (global_row < height)
        table_row = jnp.clip(global_row, 0, height - 1)
        for slot in range(slots):
            target = src_ref[table_row, slot] - first_row
            scale = scale_ref[table_row, slot]
            hit = inside & (target >= 0) & (target < rows) & (scale != 0.0)

            @pl.when(hit)
            def _():
                start = start_ref[table_row, slot]
                span = span_ref[table_row, slot]
                basis = basis_ref[table_row, slot]
                narrow = span < lon_total
                band = ((offset >= start) & (offset < start + span) & narrow).astype(
                    jnp.bfloat16
                )
                boxed = jnp.dot(band, field_ref[0, row], preferred_element_type=jnp.float32)
                full = jnp.where(narrow, 0.0, 1.0).astype(jnp.float32)
                boxed = boxed + full * total_ref[0, row]
                acc_ref[target, basis] = acc_ref[target, basis] + scale * boxed

    for p in range(rows):
        mixed = jnp.zeros((lon_count, weight_ref.shape[1]), jnp.float32)
        for k in range(BASIS):
            mixed = mixed + lax.dot_general(
                acc_ref[p, k].astype(jnp.bfloat16),
                weight_ref[k],
                (((1,), (1,)), ((), ())),
                preferred_element_type=jnp.float32,
            )
        out_ref[0, p] = mixed


def run_scatter(first, tables, field, totals, weight, row_count, lon_count, lon_total):
    members, window, padded, channels = field.shape
    basis, in_channels, out_channels = weight.shape
    height, slots = tables[0].shape
    smem = pl.BlockSpec(memory_space=pltpu.SMEM)
    kernel = functools.partial(
        scatter_kernel, slots=slots, height=height, lon_count=lon_count, lon_total=lon_total
    )
    return pl.pallas_call(
        kernel,
        grid=(members,),
        in_specs=[smem] * 6
        + [
            pl.BlockSpec((1, window, padded, channels), lambda b: (b, 0, 0, 0)),
            pl.BlockSpec((1, window, 1, channels), lambda b: (b, 0, 0, 0)),
            pl.BlockSpec((basis, in_channels, out_channels), lambda b: (0, 0, 0)),
        ],
        out_specs=pl.BlockSpec(
            (1, row_count, lon_count, in_channels), lambda b: (b, 0, 0, 0)
        ),
        out_shape=jax.ShapeDtypeStruct(
            (members, row_count, lon_count, in_channels), jnp.float32
        ),
        scratch_shapes=[pltpu.VMEM((row_count, BASIS, lon_count, channels), jnp.float32)],
    )(first, *tables, field, totals[:, :, None, :], weight)


def run_filter(first, tables, field, totals, row_count, lon_count, lon_total, backward):
    members, window, padded, channels = field.shape
    height, slots = tables[0].shape
    smem = pl.BlockSpec(memory_space=pltpu.SMEM)
    kernel = functools.partial(
        filter_kernel,
        slots=slots,
        height=height,
        lon_count=lon_count,
        lon_total=lon_total,
        backward=backward,
    )
    return pl.pallas_call(
        kernel,
        grid=(members, row_count),
        in_specs=[smem] * 6
        + [
            pl.BlockSpec((1, window, padded, channels), lambda b, r: (b, 0, 0, 0)),
            pl.BlockSpec((1, window, 1, channels), lambda b, r: (b, 0, 0, 0)),
        ],
        out_specs=pl.BlockSpec(
            (1, 1, lon_count, BASIS * channels), lambda b, r: (b, r, 0, 0)
        ),
        out_shape=jax.ShapeDtypeStruct(
            (members, row_count, lon_count, BASIS * channels), jnp.bfloat16
        ),
        scratch_shapes=[pltpu.VMEM((BASIS, lon_count, channels), jnp.float32)],
    )(first, *tables, field, totals[:, :, None, :])


def on_device(inputs, cotangent, weight, src_rows, lon_start, lon_span, basis_idx, quad_weight):
    members, row_count, lon_count, channels = inputs.shape
    lon_total = lon_count * lax.axis_size("lon")
    height = row_count * lax.axis_size("lat")
    first_row = lax.axis_index("lat") * row_count
    padded = -(-(lon_count + 2 * RIM) // 128) * 128
    weighting = quad_weight / jnp.sqrt(lon_span.astype(jnp.float32))
    first = jnp.reshape(first_row, (1,)).astype(jnp.int32)
    tables = (src_rows, lon_start, lon_span, basis_idx, weighting)

    both = extend(jnp.concatenate([inputs, cotangent], axis=3), padded)
    widened = both[..., :channels]
    grad_wide = both[..., channels:]
    row_sums = jnp.stack(
        [jnp.sum(inputs, axis=2, dtype=jnp.float32), jnp.sum(cotangent, axis=2, dtype=jnp.float32)]
    )
    local_totals = ring_sum(row_sums, "lon")
    if row_count >= POLAR + REACH:
        framed = jnp.pad(local_totals, ((0, 0), (0, 0), (REACH, REACH), (0, 0)))
    else:
        framed = with_halo(local_totals, (("lat", 2),), REACH, False)
    totals, grad_totals = framed[0], framed[1]

    flattened = run_filter(first, tables, widened, totals, row_count, lon_count, lon_total, False)
    w_fwd = weight.reshape(BASIS * channels, channels)
    response = jnp.einsum("brwq,qo->brwo", flattened, w_fwd, preferred_element_type=jnp.float32)

    partial_value = jnp.einsum(
        "brwq,brwo->qo", flattened, cotangent, preferred_element_type=jnp.float32
    )
    partial_value = partial_value.reshape(BASIS, channels, channels)
    reduced = ring_scatter(partial_value, "lon", 2)
    grad_wide, grad_totals, reduced = lax.optimization_barrier((grad_wide, grad_totals, reduced))
    reduced = ring_scatter(reduced, "lat", 1)
    grad_input = run_scatter(
        first, tables, grad_wide, grad_totals, weight, row_count, lon_count, lon_total
    )
    grad_weight = reduced / jnp.sqrt(jnp.float32(members * height * lon_total))
    return (response, grad_input, grad_weight)


def solution(mesh):
    placed = (
        P("grp", "lat", "lon", None),
        P("grp", "lat", "lon", None),
        P(),
        P(),
        P(),
        P(),
        P(),
        P(),
    )
    return jax.shard_map(
        on_device,
        mesh=mesh,
        in_specs=placed,
        out_specs=(
            P("grp", "lat", "lon", None),
            P("grp", "lat", "lon", None),
            P("grp", "lat", "lon"),
        ),
        check_vma=False,
    )
```

```python
import functools

import jax
import jax.numpy as jnp
from jax import lax
from jax.experimental import pallas as pl
from jax.experimental.pallas import tpu as pltpu
from jax.sharding import PartitionSpec as P

BASIS = 9
REACH = 2
RIM = 16
POLAR = 2


def with_halo(block, sides, width, periodic):
    for axis, dim in sides:
        count = lax.axis_size(axis)
        forward = [(i, i + 1) for i in range(count - 1)]
        if periodic:
            forward.append((count - 1, 0))
        backward = [(target, source) for source, target in forward]
        low = lax.ppermute(
            lax.slice_in_dim(block, block.shape[dim] - width, None, axis=dim), axis, forward
        )
        high = lax.ppermute(lax.slice_in_dim(block, 0, width, axis=dim), axis, backward)
        block = jnp.concatenate([low, block, high], axis=dim)
    return block


def extend(grid_field, padded):
    grid_field = with_halo(grid_field, (("lat", 1),), REACH, False)
    grid_field = with_halo(grid_field, (("lon", 2),), RIM, True)
    extra = padded - grid_field.shape[2]
    return jnp.pad(grid_field, ((0, 0), (0, 0), (0, extra), (0, 0)))


def ring_sum(value, axis):
    count = lax.axis_size(axis)
    total = value
    for shift in range(1, count):
        pairs = [(i, (i + shift) % count) for i in range(count)]
        total = total + lax.ppermute(value, axis, pairs)
    return total


def ring_scatter(value, axis, dim):
    count = lax.axis_size(axis)
    own = lax.axis_index(axis)
    block = value.shape[dim] // count
    total = lax.dynamic_slice_in_dim(value, own * block, block, dim)
    for shift in range(1, count):
        pairs = [(i, (i + shift) % count) for i in range(count)]
        piece = lax.dynamic_slice_in_dim(value, ((own + shift) % count) * block, block, dim)
        sent = lax.ppermute(piece.astype(jnp.bfloat16), axis, pairs)
        total = total + sent.astype(jnp.float32)
    return total


def filter_kernel(
    first_ref, src_ref, start_ref, span_ref, basis_ref, scale_ref, field_ref, total_ref,
    out_ref, acc_ref, *, slots, height, lon_count, lon_total, backward,
):
    r = pl.program_id(1)
    first_row = first_ref[0]
    padded = field_ref.shape[2]
    channels = field_ref.shape[3]
    acc_ref[...] = jnp.zeros(acc_ref.shape, jnp.float32)
    out_col = lax.broadcasted_iota(jnp.int32, (lon_count, padded), 0)
    in_col = lax.broadcasted_iota(jnp.int32, (lon_count, padded), 1) - RIM
    offset = out_col - in_col if backward else in_col - out_col

    def add_slot(row, table_row, slot, scale):
        start = start_ref[table_row, slot]
        span = span_ref[table_row, slot]
        basis = basis_ref[table_row, slot]
        narrow = span < lon_total
        band = ((offset >= start) & (offset < start + span) & narrow).astype(jnp.bfloat16)
        boxed = jnp.dot(band, field_ref[0, row], preferred_element_type=jnp.float32)
        full = jnp.where(narrow, 0.0, 1.0).astype(jnp.float32)
        boxed = boxed + full * total_ref[0, row]
        acc_ref[basis] = acc_ref[basis] + scale * boxed

    if backward:
        target = first_row + r
        for e in range(2 * REACH + 1):
            row = r + e
            global_row = target + e - REACH
            inside = (global_row >= 0) & (global_row < height)
            table_row = jnp.clip(global_row, 0, height - 1)
            for slot in range(slots):
                scale = scale_ref[table_row, slot]
                hit = inside & (src_ref[table_row, slot] == target) & (scale != 0.0)

                @pl.when(hit)
                def _():
                    add_slot(row, table_row, slot, scale)
    else:
        table_row = first_row + r
        for slot in range(slots):
            row = src_ref[table_row, slot] - first_row + REACH
            add_slot(row, table_row, slot, scale_ref[table_row, slot])

    for k in range(BASIS):
        out_ref[0, 0, :, k * channels:(k + 1) * channels] = acc_ref[k].astype(jnp.bfloat16)


def scatter_kernel(
    first_ref, src_ref, start_ref, span_ref, basis_ref, scale_ref, field_ref, total_ref,
    out_ref, acc_ref, *, slots, height, lon_count, lon_total,
):
    first_row = first_ref[0]
    rows = out_ref.shape[1]
    window = field_ref.shape[1]
    padded = field_ref.shape[2]
    channels = field_ref.shape[3]
    acc_ref[...] = jnp.zeros(acc_ref.shape, jnp.float32)
    out_col = lax.broadcasted_iota(jnp.int32, (lon_count, padded), 0)
    in_col = lax.broadcasted_iota(jnp.int32, (lon_count, padded), 1) - RIM
    offset = out_col - in_col
    for row in range(window):
        global_row = first_row + row - REACH
        inside = (global_row >= 0) & (global_row < height)
        table_row = jnp.clip(global_row, 0, height - 1)
        for slot in range(slots):
            target = src_ref[table_row, slot] - first_row
            scale = scale_ref[table_row, slot]
            hit = inside & (target >= 0) & (target < rows) & (scale != 0.0)

            @pl.when(hit)
            def _():
                start = start_ref[table_row, slot]
                span = span_ref[table_row, slot]
                basis = basis_ref[table_row, slot]
                narrow = span < lon_total
                band = ((offset >= start) & (offset < start + span) & narrow).astype(
                    jnp.bfloat16
                )
                boxed = jnp.dot(band, field_ref[0, row], preferred_element_type=jnp.float32)
                full = jnp.where(narrow, 0.0, 1.0).astype(jnp.float32)
                boxed = boxed + full * total_ref[0, row]
                acc_ref[target, basis] = acc_ref[target, basis] + scale * boxed

    for p in range(rows):
        for k in range(BASIS):
            out_ref[0, p, :, k * channels:(k + 1) * channels] = acc_ref[p, k].astype(
                jnp.bfloat16
            )


def run_scatter(first, tables, field, totals, row_count, lon_count, lon_total, part=0):
    members, window, padded, combined = field.shape
    channels = totals.shape[-1]
    height, slots = tables[0].shape
    smem = pl.BlockSpec(memory_space=pltpu.SMEM)
    kernel = functools.partial(
        scatter_kernel, slots=slots, height=height, lon_count=lon_count, lon_total=lon_total
    )
    return pl.pallas_call(
        kernel,
        grid=(members,),
        in_specs=[smem] * 6
        + [
            pl.BlockSpec((1, window, padded, channels), lambda b: (b, 0, 0, part)),
            pl.BlockSpec((1, window, 1, channels), lambda b: (b, 0, 0, 0)),
        ],
        out_specs=pl.BlockSpec(
            (1, row_count, lon_count, BASIS * channels), lambda b: (b, 0, 0, 0)
        ),
        out_shape=jax.ShapeDtypeStruct(
            (members, row_count, lon_count, BASIS * channels), jnp.bfloat16
        ),
        scratch_shapes=[pltpu.VMEM((row_count, BASIS, lon_count, channels), jnp.float32)],
    )(first, *tables, field, totals[:, :, None, :])


def run_filter(
    first, tables, field, totals, row_count, lon_count, lon_total, backward, part=0
):
    members, window, padded, combined = field.shape
    channels = totals.shape[-1]
    height, slots = tables[0].shape
    smem = pl.BlockSpec(memory_space=pltpu.SMEM)
    kernel = functools.partial(
        filter_kernel,
        slots=slots,
        height=height,
        lon_count=lon_count,
        lon_total=lon_total,
        backward=backward,
    )
    return pl.pallas_call(
        kernel,
        grid=(members, row_count),
        in_specs=[smem] * 6
        + [
            pl.BlockSpec((1, window, padded, channels), lambda b, r: (b, 0, 0, part)),
            pl.BlockSpec((1, window, 1, channels), lambda b, r: (b, 0, 0, 0)),
        ],
        out_specs=pl.BlockSpec(
            (1, 1, lon_count, BASIS * channels), lambda b, r: (b, r, 0, 0)
        ),
        out_shape=jax.ShapeDtypeStruct(
            (members, row_count, lon_count, BASIS * channels), jnp.bfloat16
        ),
        scratch_shapes=[pltpu.VMEM((BASIS, lon_count, channels), jnp.float32)],
    )(first, *tables, field, totals[:, :, None, :])


def on_device(inputs, cotangent, weight, src_rows, lon_start, lon_span, basis_idx, quad_weight):
    members, row_count, lon_count, channels = inputs.shape
    lon_total = lon_count * lax.axis_size("lon")
    height = row_count * lax.axis_size("lat")
    first_row = lax.axis_index("lat") * row_count
    padded = -(-(lon_count + 2 * RIM) // 128) * 128
    weighting = quad_weight / jnp.sqrt(lon_span.astype(jnp.float32))
    first = jnp.reshape(first_row, (1,)).astype(jnp.int32)
    tables = (src_rows, lon_start, lon_span, basis_idx, weighting)

    both = extend(jnp.concatenate([inputs, cotangent], axis=3), padded)
    row_sums = jnp.stack(
        [jnp.sum(inputs, axis=2, dtype=jnp.float32), jnp.sum(cotangent, axis=2, dtype=jnp.float32)]
    )
    local_totals = ring_sum(row_sums, "lon")
    if row_count >= POLAR + REACH:
        framed = jnp.pad(local_totals, ((0, 0), (0, 0), (REACH, REACH), (0, 0)))
    else:
        framed = with_halo(local_totals, (("lat", 2),), REACH, False)
    totals, grad_totals = framed[0], framed[1]

    flattened = run_filter(first, tables, both, totals, row_count, lon_count, lon_total, False, 0)
    w_fwd = weight.reshape(BASIS * channels, channels)
    response = jnp.einsum("brwq,qo->brwo", flattened, w_fwd, preferred_element_type=jnp.float32)

    partial_value = jnp.einsum(
        "brwq,brwo->qo", flattened, cotangent, preferred_element_type=jnp.float32
    )
    partial_value = partial_value.reshape(BASIS, channels, channels)
    reduced = ring_scatter(partial_value, "lon", 2)
    both, grad_totals, reduced = lax.optimization_barrier((both, grad_totals, reduced))
    reduced = ring_scatter(reduced, "lat", 1)
    back_filtered = run_scatter(
        first, tables, both, grad_totals, row_count, lon_count, lon_total, 1
    )
    w_back = jnp.transpose(weight, (0, 2, 1)).reshape(BASIS * channels, channels)
    grad_input = jnp.einsum(
        "bpwq,qc->bpwc", back_filtered, w_back, preferred_element_type=jnp.float32
    )
    grad_weight = reduced / jnp.sqrt(jnp.float32(members * height * lon_total))
    return (response, grad_input, grad_weight)


def solution(mesh):
    placed = (
        P("grp", "lat", "lon", None),
        P("grp", "lat", "lon", None),
        P(),
        P(),
        P(),
        P(),
        P(),
        P(),
    )
    return jax.shard_map(
        on_device,
        mesh=mesh,
        in_specs=placed,
        out_specs=(
            P("grp", "lat", "lon", None),
            P("grp", "lat", "lon", None),
            P("grp", "lat", "lon"),
        ),
        check_vma=False,
    )
```

```python
import functools

import jax
import jax.numpy as jnp
from jax import lax
from jax.experimental import pallas as pl
from jax.experimental.pallas import tpu as pltpu
from jax.sharding import PartitionSpec as P

BASIS = 9
REACH = 2
RIM = 16
POLAR = 2


def with_halo(block, sides, width, periodic):
    for axis, dim in sides:
        count = lax.axis_size(axis)
        forward = [(i, i + 1) for i in range(count - 1)]
        if periodic:
            forward.append((count - 1, 0))
        backward = [(target, source) for source, target in forward]
        low = lax.ppermute(
            lax.slice_in_dim(block, block.shape[dim] - width, None, axis=dim), axis, forward
        )
        high = lax.ppermute(lax.slice_in_dim(block, 0, width, axis=dim), axis, backward)
        block = jnp.concatenate([low, block, high], axis=dim)
    return block


def ring_sum(value, axis):
    count = lax.axis_size(axis)
    total = value
    for shift in range(1, count):
        pairs = [(i, (i + shift) % count) for i in range(count)]
        total = total + lax.ppermute(value, axis, pairs)
    return total


def ring_scatter(value, axis, dim):
    count = lax.axis_size(axis)
    own = lax.axis_index(axis)
    block = value.shape[dim] // count
    total = lax.dynamic_slice_in_dim(value, own * block, block, dim)
    for shift in range(1, count):
        pairs = [(i, (i + shift) % count) for i in range(count)]
        piece = lax.dynamic_slice_in_dim(value, ((own + shift) % count) * block, block, dim)
        sent = lax.ppermute(piece.astype(jnp.bfloat16), axis, pairs)
        total = total + sent.astype(jnp.float32)
    return total


def filter_kernel(
    first_ref, src_ref, start_ref, span_ref, basis_ref, scale_ref, field_ref, total_ref,
    out_ref, acc_ref, *, slots, height, lon_count, lon_total, backward,
):
    r = pl.program_id(1)
    first_row = first_ref[0]
    padded = field_ref.shape[2]
    channels = field_ref.shape[3]
    acc_ref[...] = jnp.zeros(acc_ref.shape, jnp.float32)
    out_col = lax.broadcasted_iota(jnp.int32, (lon_count, padded), 0)
    in_col = lax.broadcasted_iota(jnp.int32, (lon_count, padded), 1) - RIM
    offset = out_col - in_col if backward else in_col - out_col

    def add_slot(row, table_row, slot, scale):
        start = start_ref[table_row, slot]
        span = span_ref[table_row, slot]
        basis = basis_ref[table_row, slot]
        narrow = span < lon_total
        band = ((offset >= start) & (offset < start + span) & narrow).astype(jnp.bfloat16)
        boxed = jnp.dot(band, field_ref[0, row], preferred_element_type=jnp.float32)
        full = jnp.where(narrow, 0.0, 1.0).astype(jnp.float32)
        boxed = boxed + full * total_ref[0, row]
        acc_ref[basis] = acc_ref[basis] + scale * boxed

    if backward:
        target = first_row + r
        for e in range(2 * REACH + 1):
            row = r + e
            global_row = target + e - REACH
            inside = (global_row >= 0) & (global_row < height)
            table_row = jnp.clip(global_row, 0, height - 1)
            for slot in range(slots):
                scale = scale_ref[table_row, slot]
                hit = inside & (src_ref[table_row, slot] == target) & (scale != 0.0)

                @pl.when(hit)
                def _():
                    add_slot(row, table_row, slot, scale)
    else:
        table_row = first_row + r
        for slot in range(slots):
            row = src_ref[table_row, slot] - first_row + REACH
            add_slot(row, table_row, slot, scale_ref[table_row, slot])

    for k in range(BASIS):
        out_ref[0, 0, :, k * channels:(k + 1) * channels] = acc_ref[k].astype(jnp.bfloat16)


def scatter_kernel(
    first_ref, src_ref, start_ref, span_ref, basis_ref, scale_ref, field_ref, total_ref,
    out_ref, acc_ref, *, slots, height, lon_count, lon_total,
):
    first_row = first_ref[0]
    rows = out_ref.shape[1]
    window = field_ref.shape[1]
    padded = field_ref.shape[2]
    channels = field_ref.shape[3]
    acc_ref[...] = jnp.zeros(acc_ref.shape, jnp.float32)
    out_col = lax.broadcasted_iota(jnp.int32, (lon_count, padded), 0)
    in_col = lax.broadcasted_iota(jnp.int32, (lon_count, padded), 1) - RIM
    offset = out_col - in_col
    for row in range(window):
        global_row = first_row + row - REACH
        inside = (global_row >= 0) & (global_row < height)
        table_row = jnp.clip(global_row, 0, height - 1)
        for slot in range(slots):
            target = src_ref[table_row, slot] - first_row
            scale = scale_ref[table_row, slot]
            hit = inside & (target >= 0) & (target < rows) & (scale != 0.0)

            @pl.when(hit)
            def _():
                start = start_ref[table_row, slot]
                span = span_ref[table_row, slot]
                basis = basis_ref[table_row, slot]
                narrow = span < lon_total
                band = ((offset >= start) & (offset < start + span) & narrow).astype(
                    jnp.bfloat16
                )
                boxed = jnp.dot(band, field_ref[0, row], preferred_element_type=jnp.float32)
                full = jnp.where(narrow, 0.0, 1.0).astype(jnp.float32)
                boxed = boxed + full * total_ref[0, row]
                acc_ref[target, basis] = acc_ref[target, basis] + scale * boxed

    for p in range(rows):
        for k in range(BASIS):
            out_ref[0, p, :, k * channels:(k + 1) * channels] = acc_ref[p, k].astype(
                jnp.bfloat16
            )


def run_scatter(first, tables, field, totals, row_count, lon_count, lon_total, part=0):
    members, window, padded, combined = field.shape
    channels = totals.shape[-1]
    height, slots = tables[0].shape
    smem = pl.BlockSpec(memory_space=pltpu.SMEM)
    kernel = functools.partial(
        scatter_kernel, slots=slots, height=height, lon_count=lon_count, lon_total=lon_total
    )
    return pl.pallas_call(
        kernel,
        grid=(members,),
        in_specs=[smem] * 6
        + [
            pl.BlockSpec((1, window, padded, channels), lambda b: (b, 0, 0, part)),
            pl.BlockSpec((1, window, 1, channels), lambda b: (b, 0, 0, 0)),
        ],
        out_specs=pl.BlockSpec(
            (1, row_count, lon_count, BASIS * channels), lambda b: (b, 0, 0, 0)
        ),
        out_shape=jax.ShapeDtypeStruct(
            (members, row_count, lon_count, BASIS * channels), jnp.bfloat16
        ),
        scratch_shapes=[pltpu.VMEM((row_count, BASIS, lon_count, channels), jnp.float32)],
    )(first, *tables, field, totals[:, :, None, :])


def run_filter(
    first, tables, field, totals, row_count, lon_count, lon_total, backward, part=0
):
    members, window, padded, combined = field.shape
    channels = totals.shape[-1]
    height, slots = tables[0].shape
    smem = pl.BlockSpec(memory_space=pltpu.SMEM)
    kernel = functools.partial(
        filter_kernel,
        slots=slots,
        height=height,
        lon_count=lon_count,
        lon_total=lon_total,
        backward=backward,
    )
    return pl.pallas_call(
        kernel,
        grid=(members, row_count),
        in_specs=[smem] * 6
        + [
            pl.BlockSpec((1, window, padded, channels), lambda b, r: (b, 0, 0, part)),
            pl.BlockSpec((1, window, 1, channels), lambda b, r: (b, 0, 0, 0)),
        ],
        out_specs=pl.BlockSpec(
            (1, 1, lon_count, BASIS * channels), lambda b, r: (b, r, 0, 0)
        ),
        out_shape=jax.ShapeDtypeStruct(
            (members, row_count, lon_count, BASIS * channels), jnp.bfloat16
        ),
        scratch_shapes=[pltpu.VMEM((BASIS, lon_count, channels), jnp.float32)],
    )(first, *tables, field, totals[:, :, None, :])


def on_device(inputs, cotangent, weight, src_rows, lon_start, lon_span, basis_idx, quad_weight):
    members, row_count, lon_count, channels = inputs.shape
    lon_total = lon_count * lax.axis_size("lon")
    height = row_count * lax.axis_size("lat")
    first_row = lax.axis_index("lat") * row_count
    padded = -(-(lon_count + 2 * RIM) // 128) * 128
    weighting = quad_weight / jnp.sqrt(lon_span.astype(jnp.float32))
    first = jnp.reshape(first_row, (1,)).astype(jnp.int32)
    tables = (src_rows, lon_start, lon_span, basis_idx, weighting)

    joined = jnp.concatenate([inputs, cotangent], axis=3)
    banded = with_halo(joined, (("lat", 1),), REACH, False)
    banded, source = lax.optimization_barrier((banded, joined))
    both = with_halo(banded, (("lon", 2),), RIM, True)
    both = jnp.pad(both, ((0, 0), (0, 0), (0, padded - both.shape[2]), (0, 0)))
    sums = jnp.sum(source, axis=2, dtype=jnp.float32)
    row_sums = jnp.stack([sums[..., :channels], sums[..., channels:]])
    local_totals = ring_sum(row_sums, "lon")
    if row_count >= POLAR + REACH:
        framed = jnp.pad(local_totals, ((0, 0), (0, 0), (REACH, REACH), (0, 0)))
    else:
        framed = with_halo(local_totals, (("lat", 2),), REACH, False)
    totals, grad_totals = framed[0], framed[1]

    flattened = run_filter(first, tables, both, totals, row_count, lon_count, lon_total, False, 0)
    w_fwd = weight.reshape(BASIS * channels, channels)
    response = jnp.einsum("brwq,qo->brwo", flattened, w_fwd, preferred_element_type=jnp.float32)

    partial_value = jnp.einsum(
        "brwq,brwo->qo", flattened, cotangent, preferred_element_type=jnp.float32
    )
    partial_value = partial_value.reshape(BASIS, channels, channels)
    reduced = ring_scatter(partial_value, "lon", 2)
    both, grad_totals, reduced = lax.optimization_barrier((both, grad_totals, reduced))
    reduced = ring_scatter(reduced, "lat", 1)
    back_filtered = run_scatter(
        first, tables, both, grad_totals, row_count, lon_count, lon_total, 1
    )
    w_back = jnp.transpose(weight, (0, 2, 1)).reshape(BASIS * channels, channels)
    grad_input = jnp.einsum(
        "bpwq,qc->bpwc", back_filtered, w_back, preferred_element_type=jnp.float32
    )
    grad_weight = reduced / jnp.sqrt(jnp.float32(members * height * lon_total))
    return (response, grad_input, grad_weight)


def solution(mesh):
    placed = (
        P("grp", "lat", "lon", None),
        P("grp", "lat", "lon", None),
        P(),
        P(),
        P(),
        P(),
        P(),
        P(),
    )
    return jax.shard_map(
        on_device,
        mesh=mesh,
        in_specs=placed,
        out_specs=(
            P("grp", "lat", "lon", None),
            P("grp", "lat", "lon", None),
            P("grp", "lat", "lon"),
        ),
        check_vma=False,
    )
```

```python
import functools

import jax
import jax.numpy as jnp
from jax import lax
from jax.experimental import pallas as pl
from jax.experimental.pallas import tpu as pltpu
from jax.sharding import PartitionSpec as P

BASIS = 9
REACH = 2
RIM = 16
POLAR = 2


def with_halo(block, sides, width, periodic):
    for axis, dim in sides:
        count = lax.axis_size(axis)
        forward = [(i, i + 1) for i in range(count - 1)]
        if periodic:
            forward.append((count - 1, 0))
        backward = [(target, source) for source, target in forward]
        low = lax.ppermute(
            lax.slice_in_dim(block, block.shape[dim] - width, None, axis=dim), axis, forward
        )
        high = lax.ppermute(lax.slice_in_dim(block, 0, width, axis=dim), axis, backward)
        block = jnp.concatenate([low, block, high], axis=dim)
    return block


def ring_sum(value, axis):
    count = lax.axis_size(axis)
    total = value
    for shift in range(1, count):
        pairs = [(i, (i + shift) % count) for i in range(count)]
        total = total + lax.ppermute(value, axis, pairs)
    return total


def ring_scatter(value, axis, dim):
    count = lax.axis_size(axis)
    own = lax.axis_index(axis)
    block = value.shape[dim] // count
    total = lax.dynamic_slice_in_dim(value, own * block, block, dim)
    for shift in range(1, count):
        pairs = [(i, (i + shift) % count) for i in range(count)]
        piece = lax.dynamic_slice_in_dim(value, ((own + shift) % count) * block, block, dim)
        sent = lax.ppermute(piece.astype(jnp.bfloat16), axis, pairs)
        total = total + sent.astype(jnp.float32)
    return total


def exchange_scatter(value, axis, dim):
    count = lax.axis_size(axis)
    own = lax.axis_index(axis)
    block = value.shape[dim] // count
    pieces = jnp.stack(jnp.split(value, count, axis=dim))
    mine = lax.dynamic_index_in_dim(pieces, own, 0, keepdims=False)
    moved = lax.all_to_all(pieces.astype(jnp.bfloat16), axis, 0, 0, tiled=True)
    others = moved.astype(jnp.float32)
    total = mine
    for source in range(count):
        other = lax.dynamic_index_in_dim(others, (own + source + 1) % count, 0, keepdims=False)
        total = total + jnp.where(source + 1 < count, other, 0.0)
    return total


def filter_kernel(
    first_ref, src_ref, start_ref, span_ref, basis_ref, scale_ref, field_ref, total_ref,
    out_ref, acc_ref, *, slots, height, lon_count, lon_total, backward,
):
    r = pl.program_id(1)
    first_row = first_ref[0]
    padded = field_ref.shape[2]
    channels = field_ref.shape[3]
    acc_ref[...] = jnp.zeros(acc_ref.shape, jnp.float32)
    out_col = lax.broadcasted_iota(jnp.int32, (lon_count, padded), 0)
    in_col = lax.broadcasted_iota(jnp.int32, (lon_count, padded), 1) - RIM
    offset = out_col - in_col if backward else in_col - out_col

    def add_slot(row, table_row, slot, scale):
        start = start_ref[table_row, slot]
        span = span_ref[table_row, slot]
        basis = basis_ref[table_row, slot]
        narrow = span < lon_total
        band = ((offset >= start) & (offset < start + span) & narrow).astype(jnp.bfloat16)
        boxed = jnp.dot(band, field_ref[0, row], preferred_element_type=jnp.float32)
        full = jnp.where(narrow, 0.0, 1.0).astype(jnp.float32)
        boxed = boxed + full * total_ref[0, row]
        acc_ref[basis] = acc_ref[basis] + scale * boxed

    if backward:
        target = first_row + r
        for e in range(2 * REACH + 1):
            row = r + e
            global_row = target + e - REACH
            inside = (global_row >= 0) & (global_row < height)
            table_row = jnp.clip(global_row, 0, height - 1)
            for slot in range(slots):
                scale = scale_ref[table_row, slot]
                hit = inside & (src_ref[table_row, slot] == target) & (scale != 0.0)

                @pl.when(hit)
                def _():
                    add_slot(row, table_row, slot, scale)
    else:
        table_row = first_row + r
        for slot in range(slots):
            row = src_ref[table_row, slot] - first_row + REACH
            add_slot(row, table_row, slot, scale_ref[table_row, slot])

    for k in range(BASIS):
        out_ref[0, 0, :, k * channels:(k + 1) * channels] = acc_ref[k].astype(jnp.bfloat16)


def scatter_kernel(
    first_ref, src_ref, start_ref, span_ref, basis_ref, scale_ref, field_ref, total_ref,
    out_ref, acc_ref, *, slots, height, lon_count, lon_total,
):
    first_row = first_ref[0]
    rows = out_ref.shape[1]
    window = field_ref.shape[1]
    padded = field_ref.shape[2]
    channels = field_ref.shape[3]
    acc_ref[...] = jnp.zeros(acc_ref.shape, jnp.float32)
    out_col = lax.broadcasted_iota(jnp.int32, (lon_count, padded), 0)
    in_col = lax.broadcasted_iota(jnp.int32, (lon_count, padded), 1) - RIM
    offset = out_col - in_col
    for row in range(window):
        global_row = first_row + row - REACH
        inside = (global_row >= 0) & (global_row < height)
        table_row = jnp.clip(global_row, 0, height - 1)
        for slot in range(slots):
            target = src_ref[table_row, slot] - first_row
            scale = scale_ref[table_row, slot]
            hit = inside & (target >= 0) & (target < rows) & (scale != 0.0)

            @pl.when(hit)
            def _():
                start = start_ref[table_row, slot]
                span = span_ref[table_row, slot]
                basis = basis_ref[table_row, slot]
                narrow = span < lon_total
                band = ((offset >= start) & (offset < start + span) & narrow).astype(
                    jnp.bfloat16
                )
                boxed = jnp.dot(band, field_ref[0, row], preferred_element_type=jnp.float32)
                full = jnp.where(narrow, 0.0, 1.0).astype(jnp.float32)
                boxed = boxed + full * total_ref[0, row]
                acc_ref[target, basis] = acc_ref[target, basis] + scale * boxed

    for p in range(rows):
        for k in range(BASIS):
            out_ref[0, p, :, k * channels:(k + 1) * channels] = acc_ref[p, k].astype(
                jnp.bfloat16
            )


def run_scatter(first, tables, field, totals, row_count, lon_count, lon_total, part=0):
    members, window, padded, combined = field.shape
    channels = totals.shape[-1]
    height, slots = tables[0].shape
    smem = pl.BlockSpec(memory_space=pltpu.SMEM)
    kernel = functools.partial(
        scatter_kernel, slots=slots, height=height, lon_count=lon_count, lon_total=lon_total
    )
    return pl.pallas_call(
        kernel,
        grid=(members,),
        in_specs=[smem] * 6
        + [
            pl.BlockSpec((1, window, padded, channels), lambda b: (b, 0, 0, part)),
            pl.BlockSpec((1, window, 1, channels), lambda b: (b, 0, 0, 0)),
        ],
        out_specs=pl.BlockSpec(
            (1, row_count, lon_count, BASIS * channels), lambda b: (b, 0, 0, 0)
        ),
        out_shape=jax.ShapeDtypeStruct(
            (members, row_count, lon_count, BASIS * channels), jnp.bfloat16
        ),
        scratch_shapes=[pltpu.VMEM((row_count, BASIS, lon_count, channels), jnp.float32)],
    )(first, *tables, field, totals[:, :, None, :])


def run_filter(
    first, tables, field, totals, row_count, lon_count, lon_total, backward, part=0
):
    members, window, padded, combined = field.shape
    channels = totals.shape[-1]
    height, slots = tables[0].shape
    smem = pl.BlockSpec(memory_space=pltpu.SMEM)
    kernel = functools.partial(
        filter_kernel,
        slots=slots,
        height=height,
        lon_count=lon_count,
        lon_total=lon_total,
        backward=backward,
    )
    return pl.pallas_call(
        kernel,
        grid=(members, row_count),
        in_specs=[smem] * 6
        + [
            pl.BlockSpec((1, window, padded, channels), lambda b, r: (b, 0, 0, part)),
            pl.BlockSpec((1, window, 1, channels), lambda b, r: (b, 0, 0, 0)),
        ],
        out_specs=pl.BlockSpec(
            (1, 1, lon_count, BASIS * channels), lambda b, r: (b, r, 0, 0)
        ),
        out_shape=jax.ShapeDtypeStruct(
            (members, row_count, lon_count, BASIS * channels), jnp.bfloat16
        ),
        scratch_shapes=[pltpu.VMEM((BASIS, lon_count, channels), jnp.float32)],
    )(first, *tables, field, totals[:, :, None, :])


def on_device(inputs, cotangent, weight, src_rows, lon_start, lon_span, basis_idx, quad_weight):
    members, row_count, lon_count, channels = inputs.shape
    lon_total = lon_count * lax.axis_size("lon")
    height = row_count * lax.axis_size("lat")
    first_row = lax.axis_index("lat") * row_count
    padded = -(-(lon_count + 2 * RIM) // 128) * 128
    weighting = quad_weight / jnp.sqrt(lon_span.astype(jnp.float32))
    first = jnp.reshape(first_row, (1,)).astype(jnp.int32)
    tables = (src_rows, lon_start, lon_span, basis_idx, weighting)

    joined = jnp.concatenate([inputs, cotangent], axis=3)
    banded = with_halo(joined, (("lat", 1),), REACH, False)
    banded, source = lax.optimization_barrier((banded, joined))
    both = with_halo(banded, (("lon", 2),), RIM, True)
    both = jnp.pad(both, ((0, 0), (0, 0), (0, padded - both.shape[2]), (0, 0)))
    sums = jnp.sum(source, axis=2, dtype=jnp.float32)
    row_sums = jnp.stack([sums[..., :channels], sums[..., channels:]])
    local_totals = ring_sum(row_sums, "lon")
    if row_count >= POLAR + REACH:
        framed = jnp.pad(local_totals, ((0, 0), (0, 0), (REACH, REACH), (0, 0)))
    else:
        framed = with_halo(local_totals, (("lat", 2),), REACH, False)
    totals, grad_totals = framed[0], framed[1]

    flattened = run_filter(first, tables, both, totals, row_count, lon_count, lon_total, False, 0)
    w_fwd = weight.reshape(BASIS * channels, channels)
    response = jnp.einsum("brwq,qo->brwo", flattened, w_fwd, preferred_element_type=jnp.float32)

    partial_value = jnp.einsum(
        "brwq,brwo->qo", flattened, cotangent, preferred_element_type=jnp.float32
    )
    partial_value = partial_value.reshape(BASIS, channels, channels)
    reduced = ring_scatter(partial_value, "lon", 2)
    both, grad_totals, reduced = lax.optimization_barrier((both, grad_totals, reduced))
    reduced = exchange_scatter(reduced, "lat", 1)
    back_filtered = run_scatter(
        first, tables, both, grad_totals, row_count, lon_count, lon_total, 1
    )
    w_back = jnp.transpose(weight, (0, 2, 1)).reshape(BASIS * channels, channels)
    grad_input = jnp.einsum(
        "bpwq,qc->bpwc", back_filtered, w_back, preferred_element_type=jnp.float32
    )
    grad_weight = reduced / jnp.sqrt(jnp.float32(members * height * lon_total))
    return (response, grad_input, grad_weight)


def solution(mesh):
    placed = (
        P("grp", "lat", "lon", None),
        P("grp", "lat", "lon", None),
        P(),
        P(),
        P(),
        P(),
        P(),
        P(),
    )
    return jax.shard_map(
        on_device,
        mesh=mesh,
        in_specs=placed,
        out_specs=(
            P("grp", "lat", "lon", None),
            P("grp", "lat", "lon", None),
            P("grp", "lat", "lon"),
        ),
        check_vma=False,
    )
```

```python
import functools

import jax
import jax.numpy as jnp
from jax import lax
from jax.experimental import pallas as pl
from jax.experimental.pallas import tpu as pltpu
from jax.sharding import PartitionSpec as P

BASIS = 9
REACH = 2
RIM = 16
POLAR = 2


def with_halo(block, sides, width, periodic):
    for axis, dim in sides:
        count = lax.axis_size(axis)
        forward = [(i, i + 1) for i in range(count - 1)]
        if periodic:
            forward.append((count - 1, 0))
        backward = [(target, source) for source, target in forward]
        low = lax.ppermute(
            lax.slice_in_dim(block, block.shape[dim] - width, None, axis=dim), axis, forward
        )
        high = lax.ppermute(lax.slice_in_dim(block, 0, width, axis=dim), axis, backward)
        block = jnp.concatenate([low, block, high], axis=dim)
    return block


def ring_sum(value, axis):
    count = lax.axis_size(axis)
    total = value
    for shift in range(1, count):
        pairs = [(i, (i + shift) % count) for i in range(count)]
        total = total + lax.ppermute(value, axis, pairs)
    return total


def ring_scatter(value, axis, dim):
    count = lax.axis_size(axis)
    own = lax.axis_index(axis)
    block = value.shape[dim] // count
    total = lax.dynamic_slice_in_dim(value, own * block, block, dim)
    for shift in range(1, count):
        pairs = [(i, (i + shift) % count) for i in range(count)]
        piece = lax.dynamic_slice_in_dim(value, ((own + shift) % count) * block, block, dim)
        sent = lax.ppermute(piece.astype(jnp.bfloat16), axis, pairs)
        total = total + sent.astype(jnp.float32)
    return total


def filter_kernel(
    first_ref, src_ref, start_ref, span_ref, basis_ref, scale_ref, field_ref, total_ref,
    out_ref, acc_ref, *, slots, height, lon_count, lon_total, backward,
):
    r = pl.program_id(1)
    first_row = first_ref[0]
    padded = field_ref.shape[2]
    channels = field_ref.shape[3]
    acc_ref[...] = jnp.zeros(acc_ref.shape, jnp.float32)
    out_col = lax.broadcasted_iota(jnp.int32, (lon_count, padded), 0)
    in_col = lax.broadcasted_iota(jnp.int32, (lon_count, padded), 1) - RIM
    offset = out_col - in_col if backward else in_col - out_col

    def add_slot(row, table_row, slot, scale):
        start = start_ref[table_row, slot]
        span = span_ref[table_row, slot]
        basis = basis_ref[table_row, slot]
        narrow = span < lon_total
        band = ((offset >= start) & (offset < start + span) & narrow).astype(jnp.bfloat16)
        boxed = jnp.dot(band, field_ref[0, row], preferred_element_type=jnp.float32)
        full = jnp.where(narrow, 0.0, 1.0).astype(jnp.float32)
        boxed = boxed + full * total_ref[0, row]
        acc_ref[basis] = acc_ref[basis] + scale * boxed

    if backward:
        target = first_row + r
        for e in range(2 * REACH + 1):
            row = r + e
            global_row = target + e - REACH
            inside = (global_row >= 0) & (global_row < height)
            table_row = jnp.clip(global_row, 0, height - 1)
            for slot in range(slots):
                scale = scale_ref[table_row, slot]
                hit = inside & (src_ref[table_row, slot] == target) & (scale != 0.0)

                @pl.when(hit)
                def _():
                    add_slot(row, table_row, slot, scale)
    else:
        table_row = first_row + r
        for slot in range(slots):
            row = src_ref[table_row, slot] - first_row + REACH
            add_slot(row, table_row, slot, scale_ref[table_row, slot])

    for k in range(BASIS):
        out_ref[0, 0, :, k * channels:(k + 1) * channels] = acc_ref[k].astype(jnp.bfloat16)


def scatter_kernel(
    first_ref, src_ref, start_ref, span_ref, basis_ref, scale_ref, field_ref, total_ref,
    out_ref, acc_ref, *, slots, height, lon_count, lon_total, lowest,
):
    first_row = first_ref[0] + lowest
    rows = out_ref.shape[1]
    window = field_ref.shape[1]
    padded = field_ref.shape[2]
    channels = field_ref.shape[3]
    acc_ref[...] = jnp.zeros(acc_ref.shape, jnp.float32)
    out_col = lax.broadcasted_iota(jnp.int32, (lon_count, padded), 0)
    in_col = lax.broadcasted_iota(jnp.int32, (lon_count, padded), 1) - RIM
    offset = out_col - in_col
    for row in range(lowest, lowest + rows + 2 * REACH):
        global_row = first_ref[0] + row - REACH
        inside = (global_row >= 0) & (global_row < height)
        table_row = jnp.clip(global_row, 0, height - 1)
        for slot in range(slots):
            target = src_ref[table_row, slot] - first_row
            scale = scale_ref[table_row, slot]
            hit = inside & (target >= 0) & (target < rows) & (scale != 0.0)

            @pl.when(hit)
            def _():
                start = start_ref[table_row, slot]
                span = span_ref[table_row, slot]
                basis = basis_ref[table_row, slot]
                narrow = span < lon_total
                band = ((offset >= start) & (offset < start + span) & narrow).astype(
                    jnp.bfloat16
                )
                boxed = jnp.dot(band, field_ref[0, row], preferred_element_type=jnp.float32)
                full = jnp.where(narrow, 0.0, 1.0).astype(jnp.float32)
                boxed = boxed + full * total_ref[0, row]
                acc_ref[target, basis] = acc_ref[target, basis] + scale * boxed

    for p in range(rows):
        for k in range(BASIS):
            out_ref[0, p, :, k * channels:(k + 1) * channels] = acc_ref[p, k].astype(
                jnp.bfloat16
            )


def run_scatter(
    first, tables, field, totals, row_count, lon_count, lon_total, part=0, lowest=0
):
    members, window, padded, combined = field.shape
    channels = totals.shape[-1]
    height, slots = tables[0].shape
    smem = pl.BlockSpec(memory_space=pltpu.SMEM)
    kernel = functools.partial(
        scatter_kernel,
        slots=slots,
        height=height,
        lon_count=lon_count,
        lon_total=lon_total,
        lowest=lowest,
    )
    return pl.pallas_call(
        kernel,
        grid=(members,),
        in_specs=[smem] * 6
        + [
            pl.BlockSpec((1, window, padded, channels), lambda b: (b, 0, 0, part)),
            pl.BlockSpec((1, window, 1, channels), lambda b: (b, 0, 0, 0)),
        ],
        out_specs=pl.BlockSpec(
            (1, row_count, lon_count, BASIS * channels), lambda b: (b, 0, 0, 0)
        ),
        out_shape=jax.ShapeDtypeStruct(
            (members, row_count, lon_count, BASIS * channels), jnp.bfloat16
        ),
        scratch_shapes=[pltpu.VMEM((row_count, BASIS, lon_count, channels), jnp.float32)],
    )(first, *tables, field, totals[:, :, None, :])


def run_filter(
    first, tables, field, totals, row_count, lon_count, lon_total, backward, part=0
):
    members, window, padded, combined = field.shape
    channels = totals.shape[-1]
    height, slots = tables[0].shape
    smem = pl.BlockSpec(memory_space=pltpu.SMEM)
    kernel = functools.partial(
        filter_kernel,
        slots=slots,
        height=height,
        lon_count=lon_count,
        lon_total=lon_total,
        backward=backward,
    )
    return pl.pallas_call(
        kernel,
        grid=(members, row_count),
        in_specs=[smem] * 6
        + [
            pl.BlockSpec((1, window, padded, channels), lambda b, r: (b, 0, 0, part)),
            pl.BlockSpec((1, window, 1, channels), lambda b, r: (b, 0, 0, 0)),
        ],
        out_specs=pl.BlockSpec(
            (1, 1, lon_count, BASIS * channels), lambda b, r: (b, r, 0, 0)
        ),
        out_shape=jax.ShapeDtypeStruct(
            (members, row_count, lon_count, BASIS * channels), jnp.bfloat16
        ),
        scratch_shapes=[pltpu.VMEM((BASIS, lon_count, channels), jnp.float32)],
    )(first, *tables, field, totals[:, :, None, :])


def on_device(inputs, cotangent, weight, src_rows, lon_start, lon_span, basis_idx, quad_weight):
    members, row_count, lon_count, channels = inputs.shape
    lon_total = lon_count * lax.axis_size("lon")
    height = row_count * lax.axis_size("lat")
    first_row = lax.axis_index("lat") * row_count
    padded = -(-(lon_count + 2 * RIM) // 128) * 128
    weighting = quad_weight / jnp.sqrt(lon_span.astype(jnp.float32))
    first = jnp.reshape(first_row, (1,)).astype(jnp.int32)
    tables = (src_rows, lon_start, lon_span, basis_idx, weighting)

    joined = jnp.concatenate([inputs, cotangent], axis=3)
    banded = with_halo(joined, (("lat", 1),), REACH, False)
    banded, source = lax.optimization_barrier((banded, joined))
    both = with_halo(banded, (("lon", 2),), RIM, True)
    both = jnp.pad(both, ((0, 0), (0, 0), (0, padded - both.shape[2]), (0, 0)))
    sums = jnp.sum(source, axis=2, dtype=jnp.float32)
    row_sums = jnp.stack([sums[..., :channels], sums[..., channels:]])
    local_totals = ring_sum(row_sums, "lon")
    if row_count >= POLAR + REACH:
        framed = jnp.pad(local_totals, ((0, 0), (0, 0), (REACH, REACH), (0, 0)))
    else:
        framed = with_halo(local_totals, (("lat", 2),), REACH, False)
    totals, grad_totals = framed[0], framed[1]

    flattened = run_filter(first, tables, both, totals, row_count, lon_count, lon_total, False, 0)
    w_fwd = weight.reshape(BASIS * channels, channels)
    response = jnp.einsum("brwq,qo->brwo", flattened, w_fwd, preferred_element_type=jnp.float32)

    partial_value = jnp.einsum(
        "brwq,brwo->qo", flattened, cotangent, preferred_element_type=jnp.float32
    )
    partial_value = partial_value.reshape(BASIS, channels, channels)
    reduced = ring_scatter(partial_value, "lon", 2)
    w_back = jnp.transpose(weight, (0, 2, 1)).reshape(BASIS * channels, channels)

    def backward_rows(field, field_totals, lowest, count):
        back_filtered = run_scatter(
            first, tables, field, field_totals, count, lon_count, lon_total, 1, lowest
        )
        return jnp.einsum(
            "bpwq,qc->bpwc", back_filtered, w_back, preferred_element_type=jnp.float32
        )

    early_rows = row_count // 2
    early_input = backward_rows(both, grad_totals, 0, early_rows)
    both, grad_totals, reduced = lax.optimization_barrier((both, grad_totals, reduced))
    reduced = ring_scatter(reduced, "lat", 1)
    grad_input = jnp.concatenate(
        [
            early_input,
            backward_rows(both, grad_totals, early_rows, row_count - early_rows),
        ],
        axis=1,
    )
    grad_weight = reduced / jnp.sqrt(jnp.float32(members * height * lon_total))
    return (response, grad_input, grad_weight)


def solution(mesh):
    placed = (
        P("grp", "lat", "lon", None),
        P("grp", "lat", "lon", None),
        P(),
        P(),
        P(),
        P(),
        P(),
        P(),
    )
    return jax.shard_map(
        on_device,
        mesh=mesh,
        in_specs=placed,
        out_specs=(
            P("grp", "lat", "lon", None),
            P("grp", "lat", "lon", None),
            P("grp", "lat", "lon"),
        ),
        check_vma=False,
    )
```

```python
import functools

import jax
import jax.numpy as jnp
from jax import lax
from jax.experimental import pallas as pl
from jax.experimental.pallas import tpu as pltpu
from jax.sharding import PartitionSpec as P

BASIS = 9
REACH = 2
RIM = 16
POLAR = 2


def with_halo(block, sides, width, periodic):
    for axis, dim in sides:
        count = lax.axis_size(axis)
        forward = [(i, i + 1) for i in range(count - 1)]
        if periodic:
            forward.append((count - 1, 0))
        backward = [(target, source) for source, target in forward]
        low = lax.ppermute(
            lax.slice_in_dim(block, block.shape[dim] - width, None, axis=dim), axis, forward
        )
        high = lax.ppermute(lax.slice_in_dim(block, 0, width, axis=dim), axis, backward)
        block = jnp.concatenate([low, block, high], axis=dim)
    return block


def ring_sum(value, axis):
    count = lax.axis_size(axis)
    total = value
    for shift in range(1, count):
        pairs = [(i, (i + shift) % count) for i in range(count)]
        total = total + lax.ppermute(value, axis, pairs)
    return total


def ring_scatter(value, axis, dim):
    count = lax.axis_size(axis)
    own = lax.axis_index(axis)
    block = value.shape[dim] // count
    total = lax.dynamic_slice_in_dim(value, own * block, block, dim)
    for shift in range(1, count):
        pairs = [(i, (i + shift) % count) for i in range(count)]
        piece = lax.dynamic_slice_in_dim(value, ((own + shift) % count) * block, block, dim)
        sent = lax.ppermute(piece.astype(jnp.bfloat16), axis, pairs)
        total = total + sent.astype(jnp.float32)
    return total


def filter_kernel(
    first_ref, src_ref, start_ref, span_ref, basis_ref, scale_ref, field_ref, total_ref,
    cot_ref, out_ref, part_ref, acc_ref, *, slots, height, lon_count, lon_total, backward,
):
    r = pl.program_id(1)
    first_row = first_ref[0]
    padded = field_ref.shape[2]
    channels = field_ref.shape[3]
    acc_ref[...] = jnp.zeros(acc_ref.shape, jnp.float32)
    out_col = lax.broadcasted_iota(jnp.int32, (lon_count, padded), 0)
    in_col = lax.broadcasted_iota(jnp.int32, (lon_count, padded), 1) - RIM
    offset = out_col - in_col if backward else in_col - out_col

    def add_slot(row, table_row, slot, scale):
        start = start_ref[table_row, slot]
        span = span_ref[table_row, slot]
        basis = basis_ref[table_row, slot]
        narrow = span < lon_total
        band = ((offset >= start) & (offset < start + span) & narrow).astype(jnp.bfloat16)
        boxed = jnp.dot(band, field_ref[0, row], preferred_element_type=jnp.float32)
        full = jnp.where(narrow, 0.0, 1.0).astype(jnp.float32)
        boxed = boxed + full * total_ref[0, row]
        acc_ref[basis] = acc_ref[basis] + scale * boxed

    if backward:
        target = first_row + r
        for e in range(2 * REACH + 1):
            row = r + e
            global_row = target + e - REACH
            inside = (global_row >= 0) & (global_row < height)
            table_row = jnp.clip(global_row, 0, height - 1)
            for slot in range(slots):
                scale = scale_ref[table_row, slot]
                hit = inside & (src_ref[table_row, slot] == target) & (scale != 0.0)

                @pl.when(hit)
                def _():
                    add_slot(row, table_row, slot, scale)
    else:
        table_row = first_row + r
        for slot in range(slots):
            row = src_ref[table_row, slot] - first_row + REACH
            add_slot(row, table_row, slot, scale_ref[table_row, slot])

    @pl.when((pl.program_id(0) == 0) & (pl.program_id(1) == 0))
    def _():
        part_ref[...] = jnp.zeros(part_ref.shape, jnp.float32)

    cot = cot_ref[0, 0]
    for k in range(BASIS):
        rounded = acc_ref[k].astype(jnp.bfloat16)
        out_ref[0, 0, :, k * channels:(k + 1) * channels] = rounded
        part_ref[k] = part_ref[k] + lax.dot_general(
            rounded, cot, (((0,), (0,)), ((), ())), preferred_element_type=jnp.float32
        )


def scatter_kernel(
    first_ref, src_ref, start_ref, span_ref, basis_ref, scale_ref, field_ref, total_ref,
    out_ref, acc_ref, *, slots, height, lon_count, lon_total, lowest,
):
    first_row = first_ref[0] + lowest
    rows = out_ref.shape[1]
    window = field_ref.shape[1]
    padded = field_ref.shape[2]
    channels = field_ref.shape[3]
    acc_ref[...] = jnp.zeros(acc_ref.shape, jnp.float32)
    out_col = lax.broadcasted_iota(jnp.int32, (lon_count, padded), 0)
    in_col = lax.broadcasted_iota(jnp.int32, (lon_count, padded), 1) - RIM
    offset = out_col - in_col
    for row in range(lowest, lowest + rows + 2 * REACH):
        global_row = first_ref[0] + row - REACH
        inside = (global_row >= 0) & (global_row < height)
        table_row = jnp.clip(global_row, 0, height - 1)
        for slot in range(slots):
            target = src_ref[table_row, slot] - first_row
            scale = scale_ref[table_row, slot]
            hit = inside & (target >= 0) & (target < rows) & (scale != 0.0)

            @pl.when(hit)
            def _():
                start = start_ref[table_row, slot]
                span = span_ref[table_row, slot]
                basis = basis_ref[table_row, slot]
                narrow = span < lon_total
                band = ((offset >= start) & (offset < start + span) & narrow).astype(
                    jnp.bfloat16
                )
                boxed = jnp.dot(band, field_ref[0, row], preferred_element_type=jnp.float32)
                full = jnp.where(narrow, 0.0, 1.0).astype(jnp.float32)
                boxed = boxed + full * total_ref[0, row]
                acc_ref[target, basis] = acc_ref[target, basis] + scale * boxed

    for p in range(rows):
        for k in range(BASIS):
            out_ref[0, p, :, k * channels:(k + 1) * channels] = acc_ref[p, k].astype(
                jnp.bfloat16
            )


def run_scatter(
    first, tables, field, totals, row_count, lon_count, lon_total, part=0, lowest=0
):
    members, window, padded, combined = field.shape
    channels = totals.shape[-1]
    height, slots = tables[0].shape
    smem = pl.BlockSpec(memory_space=pltpu.SMEM)
    kernel = functools.partial(
        scatter_kernel,
        slots=slots,
        height=height,
        lon_count=lon_count,
        lon_total=lon_total,
        lowest=lowest,
    )
    return pl.pallas_call(
        kernel,
        grid=(members,),
        in_specs=[smem] * 6
        + [
            pl.BlockSpec((1, window, padded, channels), lambda b: (b, 0, 0, part)),
            pl.BlockSpec((1, window, 1, channels), lambda b: (b, 0, 0, 0)),
        ],
        out_specs=pl.BlockSpec(
            (1, row_count, lon_count, BASIS * channels), lambda b: (b, 0, 0, 0)
        ),
        out_shape=jax.ShapeDtypeStruct(
            (members, row_count, lon_count, BASIS * channels), jnp.bfloat16
        ),
        scratch_shapes=[pltpu.VMEM((row_count, BASIS, lon_count, channels), jnp.float32)],
    )(first, *tables, field, totals[:, :, None, :])


def run_filter(
    first, tables, field, totals, cot, row_count, lon_count, lon_total, backward, part=0
):
    members, window, padded, combined = field.shape
    channels = totals.shape[-1]
    out_channels = cot.shape[-1]
    height, slots = tables[0].shape
    smem = pl.BlockSpec(memory_space=pltpu.SMEM)
    kernel = functools.partial(
        filter_kernel,
        slots=slots,
        height=height,
        lon_count=lon_count,
        lon_total=lon_total,
        backward=backward,
    )
    return pl.pallas_call(
        kernel,
        grid=(members, row_count),
        in_specs=[smem] * 6
        + [
            pl.BlockSpec((1, window, padded, channels), lambda b, r: (b, 0, 0, part)),
            pl.BlockSpec((1, window, 1, channels), lambda b, r: (b, 0, 0, 0)),
            pl.BlockSpec((1, 1, lon_count, out_channels), lambda b, r: (b, r, 0, 0)),
        ],
        out_specs=[
            pl.BlockSpec((1, 1, lon_count, BASIS * channels), lambda b, r: (b, r, 0, 0)),
            pl.BlockSpec((BASIS, channels, out_channels), lambda b, r: (0, 0, 0)),
        ],
        out_shape=[
            jax.ShapeDtypeStruct((members, row_count, lon_count, BASIS * channels), jnp.bfloat16),
            jax.ShapeDtypeStruct((BASIS, channels, out_channels), jnp.float32),
        ],
        scratch_shapes=[pltpu.VMEM((BASIS, lon_count, channels), jnp.float32)],
    )(first, *tables, field, totals[:, :, None, :], cot)


def on_device(inputs, cotangent, weight, src_rows, lon_start, lon_span, basis_idx, quad_weight):
    members, row_count, lon_count, channels = inputs.shape
    lon_total = lon_count * lax.axis_size("lon")
    height = row_count * lax.axis_size("lat")
    first_row = lax.axis_index("lat") * row_count
    padded = -(-(lon_count + 2 * RIM) // 128) * 128
    weighting = quad_weight / jnp.sqrt(lon_span.astype(jnp.float32))
    first = jnp.reshape(first_row, (1,)).astype(jnp.int32)
    tables = (src_rows, lon_start, lon_span, basis_idx, weighting)

    joined = jnp.concatenate([inputs, cotangent], axis=3)
    banded = with_halo(joined, (("lat", 1),), REACH, False)
    banded, source = lax.optimization_barrier((banded, joined))
    both = with_halo(banded, (("lon", 2),), RIM, True)
    both = jnp.pad(both, ((0, 0), (0, 0), (0, padded - both.shape[2]), (0, 0)))
    sums = jnp.sum(source, axis=2, dtype=jnp.float32)
    row_sums = jnp.stack([sums[..., :channels], sums[..., channels:]])
    local_totals = ring_sum(row_sums, "lon")
    if row_count >= POLAR + REACH:
        framed = jnp.pad(local_totals, ((0, 0), (0, 0), (REACH, REACH), (0, 0)))
    else:
        framed = with_halo(local_totals, (("lat", 2),), REACH, False)
    totals, grad_totals = framed[0], framed[1]

    flattened, partial_value = run_filter(
        first, tables, both, totals, cotangent, row_count, lon_count, lon_total, False, 0
    )
    w_fwd = weight.reshape(BASIS * channels, channels)
    response = jnp.einsum("brwq,qo->brwo", flattened, w_fwd, preferred_element_type=jnp.float32)

    reduced = ring_scatter(partial_value, "lon", 2)
    w_back = jnp.transpose(weight, (0, 2, 1)).reshape(BASIS * channels, channels)

    def backward_rows(field, field_totals, lowest, count):
        back_filtered = run_scatter(
            first, tables, field, field_totals, count, lon_count, lon_total, 1, lowest
        )
        return jnp.einsum(
            "bpwq,qc->bpwc", back_filtered, w_back, preferred_element_type=jnp.float32
        )

    early_rows = row_count // 2
    early_input = backward_rows(both, grad_totals, 0, early_rows)
    both, grad_totals, reduced = lax.optimization_barrier((both, grad_totals, reduced))
    reduced = ring_scatter(reduced, "lat", 1)
    grad_input = jnp.concatenate(
        [
            early_input,
            backward_rows(both, grad_totals, early_rows, row_count - early_rows),
        ],
        axis=1,
    )
    grad_weight = reduced / jnp.sqrt(jnp.float32(members * height * lon_total))
    return (response, grad_input, grad_weight)


def solution(mesh):
    placed = (
        P("grp", "lat", "lon", None),
        P("grp", "lat", "lon", None),
        P(),
        P(),
        P(),
        P(),
        P(),
        P(),
    )
    return jax.shard_map(
        on_device,
        mesh=mesh,
        in_specs=placed,
        out_specs=(
            P("grp", "lat", "lon", None),
            P("grp", "lat", "lon", None),
            P("grp", "lat", "lon"),
        ),
        check_vma=False,
    )
```

```python
import functools

import jax
import jax.numpy as jnp
from jax import lax
from jax.experimental import pallas as pl
from jax.experimental.pallas import tpu as pltpu
from jax.sharding import PartitionSpec as P

BASIS = 9
REACH = 2
RIM = 16
POLAR = 2


def with_halo(block, sides, width, periodic):
    for axis, dim in sides:
        count = lax.axis_size(axis)
        forward = [(i, i + 1) for i in range(count - 1)]
        if periodic:
            forward.append((count - 1, 0))
        backward = [(target, source) for source, target in forward]
        low = lax.ppermute(
            lax.slice_in_dim(block, block.shape[dim] - width, None, axis=dim), axis, forward
        )
        high = lax.ppermute(lax.slice_in_dim(block, 0, width, axis=dim), axis, backward)
        block = jnp.concatenate([low, block, high], axis=dim)
    return block


def ring_sum(value, axis):
    count = lax.axis_size(axis)
    total = value
    for shift in range(1, count):
        pairs = [(i, (i + shift) % count) for i in range(count)]
        total = total + lax.ppermute(value, axis, pairs)
    return total


def ring_scatter(value, axis, dim):
    count = lax.axis_size(axis)
    own = lax.axis_index(axis)
    block = value.shape[dim] // count
    total = lax.dynamic_slice_in_dim(value, own * block, block, dim)
    for shift in [count // 2] + [t for t in range(1, count) if t != count // 2]:
        pairs = [(i, (i + shift) % count) for i in range(count)]
        piece = lax.dynamic_slice_in_dim(value, ((own + shift) % count) * block, block, dim)
        sent = lax.ppermute(piece.astype(jnp.bfloat16), axis, pairs)
        total = total + sent.astype(jnp.float32)
    return total


def filter_kernel(
    first_ref, src_ref, start_ref, span_ref, basis_ref, scale_ref, field_ref, total_ref,
    out_ref, acc_ref, *, slots, height, lon_count, lon_total, backward,
):
    r = pl.program_id(1)
    first_row = first_ref[0]
    padded = field_ref.shape[2]
    channels = field_ref.shape[3]
    acc_ref[...] = jnp.zeros(acc_ref.shape, jnp.float32)
    out_col = lax.broadcasted_iota(jnp.int32, (lon_count, padded), 0)
    in_col = lax.broadcasted_iota(jnp.int32, (lon_count, padded), 1) - RIM
    offset = out_col - in_col if backward else in_col - out_col

    def add_slot(row, table_row, slot, scale):
        start = start_ref[table_row, slot]
        span = span_ref[table_row, slot]
        basis = basis_ref[table_row, slot]
        narrow = span < lon_total
        band = ((offset >= start) & (offset < start + span) & narrow).astype(jnp.bfloat16)
        boxed = jnp.dot(band, field_ref[0, row], preferred_element_type=jnp.float32)
        full = jnp.where(narrow, 0.0, 1.0).astype(jnp.float32)
        boxed = boxed + full * total_ref[0, row]
        acc_ref[basis] = acc_ref[basis] + scale * boxed

    if backward:
        target = first_row + r
        for e in range(2 * REACH + 1):
            row = r + e
            global_row = target + e - REACH
            inside = (global_row >= 0) & (global_row < height)
            table_row = jnp.clip(global_row, 0, height - 1)
            for slot in range(slots):
                scale = scale_ref[table_row, slot]
                hit = inside & (src_ref[table_row, slot] == target) & (scale != 0.0)

                @pl.when(hit)
                def _():
                    add_slot(row, table_row, slot, scale)
    else:
        table_row = first_row + r
        for slot in range(slots):
            row = src_ref[table_row, slot] - first_row + REACH
            add_slot(row, table_row, slot, scale_ref[table_row, slot])

    for k in range(BASIS):
        out_ref[0, 0, :, k * channels:(k + 1) * channels] = acc_ref[k].astype(jnp.bfloat16)


def scatter_kernel(
    first_ref, src_ref, start_ref, span_ref, basis_ref, scale_ref, field_ref, total_ref,
    out_ref, acc_ref, *, slots, height, lon_count, lon_total, lowest,
):
    first_row = first_ref[0] + lowest
    rows = out_ref.shape[1]
    window = field_ref.shape[1]
    padded = field_ref.shape[2]
    channels = field_ref.shape[3]
    acc_ref[...] = jnp.zeros(acc_ref.shape, jnp.float32)
    out_col = lax.broadcasted_iota(jnp.int32, (lon_count, padded), 0)
    in_col = lax.broadcasted_iota(jnp.int32, (lon_count, padded), 1) - RIM
    offset = out_col - in_col
    for row in range(lowest, lowest + rows + 2 * REACH):
        global_row = first_ref[0] + row - REACH
        inside = (global_row >= 0) & (global_row < height)
        table_row = jnp.clip(global_row, 0, height - 1)
        for slot in range(slots):
            target = src_ref[table_row, slot] - first_row
            scale = scale_ref[table_row, slot]
            hit = inside & (target >= 0) & (target < rows) & (scale != 0.0)

            @pl.when(hit)
            def _():
                start = start_ref[table_row, slot]
                span = span_ref[table_row, slot]
                basis = basis_ref[table_row, slot]
                narrow = span < lon_total
                band = ((offset >= start) & (offset < start + span) & narrow).astype(
                    jnp.bfloat16
                )
                boxed = jnp.dot(band, field_ref[0, row], preferred_element_type=jnp.float32)
                full = jnp.where(narrow, 0.0, 1.0).astype(jnp.float32)
                boxed = boxed + full * total_ref[0, row]
                acc_ref[target, basis] = acc_ref[target, basis] + scale * boxed

    for p in range(rows):
        for k in range(BASIS):
            out_ref[0, p, :, k * channels:(k + 1) * channels] = acc_ref[p, k].astype(
                jnp.bfloat16
            )


def run_scatter(
    first, tables, field, totals, row_count, lon_count, lon_total, part=0, lowest=0
):
    members, window, padded, combined = field.shape
    channels = totals.shape[-1]
    height, slots = tables[0].shape
    smem = pl.BlockSpec(memory_space=pltpu.SMEM)
    kernel = functools.partial(
        scatter_kernel,
        slots=slots,
        height=height,
        lon_count=lon_count,
        lon_total=lon_total,
        lowest=lowest,
    )
    return pl.pallas_call(
        kernel,
        grid=(members,),
        in_specs=[smem] * 6
        + [
            pl.BlockSpec((1, window, padded, channels), lambda b: (b, 0, 0, part)),
            pl.BlockSpec((1, window, 1, channels), lambda b: (b, 0, 0, 0)),
        ],
        out_specs=pl.BlockSpec(
            (1, row_count, lon_count, BASIS * channels), lambda b: (b, 0, 0, 0)
        ),
        out_shape=jax.ShapeDtypeStruct(
            (members, row_count, lon_count, BASIS * channels), jnp.bfloat16
        ),
        scratch_shapes=[pltpu.VMEM((row_count, BASIS, lon_count, channels), jnp.float32)],
    )(first, *tables, field, totals[:, :, None, :])


def run_filter(
    first, tables, field, totals, row_count, lon_count, lon_total, backward, part=0
):
    members, window, padded, combined = field.shape
    channels = totals.shape[-1]
    height, slots = tables[0].shape
    smem = pl.BlockSpec(memory_space=pltpu.SMEM)
    kernel = functools.partial(
        filter_kernel,
        slots=slots,
        height=height,
        lon_count=lon_count,
        lon_total=lon_total,
        backward=backward,
    )
    return pl.pallas_call(
        kernel,
        grid=(members, row_count),
        in_specs=[smem] * 6
        + [
            pl.BlockSpec((1, window, padded, channels), lambda b, r: (b, 0, 0, part)),
            pl.BlockSpec((1, window, 1, channels), lambda b, r: (b, 0, 0, 0)),
        ],
        out_specs=pl.BlockSpec(
            (1, 1, lon_count, BASIS * channels), lambda b, r: (b, r, 0, 0)
        ),
        out_shape=jax.ShapeDtypeStruct(
            (members, row_count, lon_count, BASIS * channels), jnp.bfloat16
        ),
        scratch_shapes=[pltpu.VMEM((BASIS, lon_count, channels), jnp.float32)],
    )(first, *tables, field, totals[:, :, None, :])


def on_device(inputs, cotangent, weight, src_rows, lon_start, lon_span, basis_idx, quad_weight):
    members, row_count, lon_count, channels = inputs.shape
    lon_total = lon_count * lax.axis_size("lon")
    height = row_count * lax.axis_size("lat")
    first_row = lax.axis_index("lat") * row_count
    padded = -(-(lon_count + 2 * RIM) // 128) * 128
    weighting = quad_weight / jnp.sqrt(lon_span.astype(jnp.float32))
    first = jnp.reshape(first_row, (1,)).astype(jnp.int32)
    tables = (src_rows, lon_start, lon_span, basis_idx, weighting)

    joined = jnp.concatenate([inputs, cotangent], axis=3)
    banded = with_halo(joined, (("lat", 1),), REACH, False)
    banded, source = lax.optimization_barrier((banded, joined))
    both = with_halo(banded, (("lon", 2),), RIM, True)
    both = jnp.pad(both, ((0, 0), (0, 0), (0, padded - both.shape[2]), (0, 0)))
    sums = jnp.sum(source, axis=2, dtype=jnp.float32)
    row_sums = jnp.stack([sums[..., :channels], sums[..., channels:]])
    local_totals = ring_sum(row_sums, "lon")
    if row_count >= POLAR + REACH:
        framed = jnp.pad(local_totals, ((0, 0), (0, 0), (REACH, REACH), (0, 0)))
    else:
        framed = with_halo(local_totals, (("lat", 2),), REACH, False)
    totals, grad_totals = framed[0], framed[1]

    flattened = run_filter(first, tables, both, totals, row_count, lon_count, lon_total, False, 0)
    w_fwd = weight.reshape(BASIS * channels, channels)
    response = jnp.einsum("brwq,qo->brwo", flattened, w_fwd, preferred_element_type=jnp.float32)

    partial_value = jnp.einsum(
        "brwq,brwo->qo", flattened, cotangent, preferred_element_type=jnp.float32
    )
    partial_value = partial_value.reshape(BASIS, channels, channels)
    reduced = ring_scatter(partial_value, "lon", 2)
    w_back = jnp.transpose(weight, (0, 2, 1)).reshape(BASIS * channels, channels)

    def backward_rows(field, field_totals, lowest, count):
        back_filtered = run_scatter(
            first, tables, field, field_totals, count, lon_count, lon_total, 1, lowest
        )
        return jnp.einsum(
            "bpwq,qc->bpwc", back_filtered, w_back, preferred_element_type=jnp.float32
        )

    early_rows = row_count // 2
    early_input = backward_rows(both, grad_totals, 0, early_rows)
    both, grad_totals, reduced = lax.optimization_barrier((both, grad_totals, reduced))
    reduced = ring_scatter(reduced, "lat", 1)
    grad_input = jnp.concatenate(
        [
            early_input,
            backward_rows(both, grad_totals, early_rows, row_count - early_rows),
        ],
        axis=1,
    )
    grad_weight = reduced / jnp.sqrt(jnp.float32(members * height * lon_total))
    return (response, grad_input, grad_weight)


def solution(mesh):
    placed = (
        P("grp", "lat", "lon", None),
        P("grp", "lat", "lon", None),
        P(),
        P(),
        P(),
        P(),
        P(),
        P(),
    )
    return jax.shard_map(
        on_device,
        mesh=mesh,
        in_specs=placed,
        out_specs=(
            P("grp", "lat", "lon", None),
            P("grp", "lat", "lon", None),
            P("grp", "lat", "lon"),
        ),
        check_vma=False,
    )
```

```python
import functools

import jax
import jax.numpy as jnp
from jax import lax
from jax.experimental import pallas as pl
from jax.experimental.pallas import tpu as pltpu
from jax.sharding import PartitionSpec as P

BASIS = 9
REACH = 2
RIM = 16
POLAR = 2


def with_halo(block, sides, width, periodic):
    for axis, dim in sides:
        count = lax.axis_size(axis)
        forward = [(i, i + 1) for i in range(count - 1)]
        if periodic:
            forward.append((count - 1, 0))
        backward = [(target, source) for source, target in forward]
        low = lax.ppermute(
            lax.slice_in_dim(block, block.shape[dim] - width, None, axis=dim), axis, forward
        )
        high = lax.ppermute(lax.slice_in_dim(block, 0, width, axis=dim), axis, backward)
        block = jnp.concatenate([low, block, high], axis=dim)
    return block


def ring_sum(value, axis):
    count = lax.axis_size(axis)
    total = value
    for shift in range(1, count):
        pairs = [(i, (i + shift) % count) for i in range(count)]
        total = total + lax.ppermute(value, axis, pairs)
    return total


def ring_scatter(value, axis, dim):
    count = lax.axis_size(axis)
    own = lax.axis_index(axis)
    block = value.shape[dim] // count
    total = lax.dynamic_slice_in_dim(value, own * block, block, dim)
    for shift in range(1, count):
        pairs = [(i, (i + shift) % count) for i in range(count)]
        piece = lax.dynamic_slice_in_dim(value, ((own + shift) % count) * block, block, dim)
        sent = lax.ppermute(piece.astype(jnp.bfloat16), axis, pairs)
        total = total + sent.astype(jnp.float32)
    return total


def filter_kernel(
    first_ref, src_ref, start_ref, span_ref, basis_ref, scale_ref, field_ref, total_ref,
    out_ref, acc_ref, ring_ref, *, slots, height, lon_count, lon_total, backward,
):
    r = pl.program_id(1)
    ring_ref[...] = jnp.zeros(ring_ref.shape, jnp.float32)
    first_row = first_ref[0]
    padded = field_ref.shape[2]
    channels = field_ref.shape[3]
    acc_ref[...] = jnp.zeros(acc_ref.shape, jnp.float32)
    out_col = lax.broadcasted_iota(jnp.int32, (lon_count, padded), 0)
    in_col = lax.broadcasted_iota(jnp.int32, (lon_count, padded), 1) - RIM
    offset = out_col - in_col if backward else in_col - out_col

    def add_slot(row, table_row, slot, scale):
        start = start_ref[table_row, slot]
        span = span_ref[table_row, slot]
        basis = basis_ref[table_row, slot]
        narrow = span < lon_total
        band = ((offset >= start) & (offset < start + span) & narrow).astype(jnp.bfloat16)
        boxed = jnp.dot(band, field_ref[0, row], preferred_element_type=jnp.float32)
        full = jnp.where(narrow, 0.0, 1.0).astype(jnp.float32)
        ring_ref[basis] = ring_ref[basis] + (scale * full) * total_ref[0, row]
        acc_ref[basis] = acc_ref[basis] + scale * boxed

    if backward:
        target = first_row + r
        for e in range(2 * REACH + 1):
            row = r + e
            global_row = target + e - REACH
            inside = (global_row >= 0) & (global_row < height)
            table_row = jnp.clip(global_row, 0, height - 1)
            for slot in range(slots):
                scale = scale_ref[table_row, slot]
                hit = inside & (src_ref[table_row, slot] == target) & (scale != 0.0)

                @pl.when(hit)
                def _():
                    add_slot(row, table_row, slot, scale)
    else:
        table_row = first_row + r
        for slot in range(slots):
            row = src_ref[table_row, slot] - first_row + REACH
            add_slot(row, table_row, slot, scale_ref[table_row, slot])

    for k in range(BASIS):
        out_ref[0, 0, :, k * channels:(k + 1) * channels] = (acc_ref[k] + ring_ref[k]).astype(
            jnp.bfloat16
        )


def scatter_kernel(
    first_ref, src_ref, start_ref, span_ref, basis_ref, scale_ref, field_ref, total_ref,
    out_ref, acc_ref, *, slots, height, lon_count, lon_total, lowest,
):
    first_row = first_ref[0] + lowest
    rows = out_ref.shape[1]
    window = field_ref.shape[1]
    padded = field_ref.shape[2]
    channels = field_ref.shape[3]
    acc_ref[...] = jnp.zeros(acc_ref.shape, jnp.float32)
    out_col = lax.broadcasted_iota(jnp.int32, (lon_count, padded), 0)
    in_col = lax.broadcasted_iota(jnp.int32, (lon_count, padded), 1) - RIM
    offset = out_col - in_col
    for row in range(lowest, lowest + rows + 2 * REACH):
        global_row = first_ref[0] + row - REACH
        inside = (global_row >= 0) & (global_row < height)
        table_row = jnp.clip(global_row, 0, height - 1)
        for slot in range(slots):
            target = src_ref[table_row, slot] - first_row
            scale = scale_ref[table_row, slot]
            hit = inside & (target >= 0) & (target < rows) & (scale != 0.0)

            @pl.when(hit)
            def _():
                start = start_ref[table_row, slot]
                span = span_ref[table_row, slot]
                basis = basis_ref[table_row, slot]
                narrow = span < lon_total
                band = ((offset >= start) & (offset < start + span) & narrow).astype(
                    jnp.bfloat16
                )
                boxed = jnp.dot(band, field_ref[0, row], preferred_element_type=jnp.float32)
                full = jnp.where(narrow, 0.0, 1.0).astype(jnp.float32)
                boxed = boxed + full * total_ref[0, row]
                acc_ref[target, basis] = acc_ref[target, basis] + scale * boxed

    for p in range(rows):
        for k in range(BASIS):
            out_ref[0, p, :, k * channels:(k + 1) * channels] = acc_ref[p, k].astype(
                jnp.bfloat16
            )


def run_scatter(
    first, tables, field, totals, row_count, lon_count, lon_total, part=0, lowest=0
):
    members, window, padded, combined = field.shape
    channels = totals.shape[-1]
    height, slots = tables[0].shape
    smem = pl.BlockSpec(memory_space=pltpu.SMEM)
    kernel = functools.partial(
        scatter_kernel,
        slots=slots,
        height=height,
        lon_count=lon_count,
        lon_total=lon_total,
        lowest=lowest,
    )
    return pl.pallas_call(
        kernel,
        grid=(members,),
        in_specs=[smem] * 6
        + [
            pl.BlockSpec((1, window, padded, channels), lambda b: (b, 0, 0, part)),
            pl.BlockSpec((1, window, 1, channels), lambda b: (b, 0, 0, 0)),
        ],
        out_specs=pl.BlockSpec(
            (1, row_count, lon_count, BASIS * channels), lambda b: (b, 0, 0, 0)
        ),
        out_shape=jax.ShapeDtypeStruct(
            (members, row_count, lon_count, BASIS * channels), jnp.bfloat16
        ),
        scratch_shapes=[pltpu.VMEM((row_count, BASIS, lon_count, channels), jnp.float32)],
    )(first, *tables, field, totals[:, :, None, :])


def run_filter(
    first, tables, field, totals, row_count, lon_count, lon_total, backward, part=0
):
    members, window, padded, combined = field.shape
    channels = totals.shape[-1]
    height, slots = tables[0].shape
    smem = pl.BlockSpec(memory_space=pltpu.SMEM)
    kernel = functools.partial(
        filter_kernel,
        slots=slots,
        height=height,
        lon_count=lon_count,
        lon_total=lon_total,
        backward=backward,
    )
    return pl.pallas_call(
        kernel,
        grid=(members, row_count),
        in_specs=[smem] * 6
        + [
            pl.BlockSpec((1, window, padded, channels), lambda b, r: (b, 0, 0, part)),
            pl.BlockSpec((1, window, 1, channels), lambda b, r: (b, 0, 0, 0)),
        ],
        out_specs=pl.BlockSpec(
            (1, 1, lon_count, BASIS * channels), lambda b, r: (b, r, 0, 0)
        ),
        out_shape=jax.ShapeDtypeStruct(
            (members, row_count, lon_count, BASIS * channels), jnp.bfloat16
        ),
        scratch_shapes=[
            pltpu.VMEM((BASIS, lon_count, channels), jnp.float32),
            pltpu.VMEM((BASIS, 1, channels), jnp.float32),
        ],
    )(first, *tables, field, totals[:, :, None, :])


def on_device(inputs, cotangent, weight, src_rows, lon_start, lon_span, basis_idx, quad_weight):
    members, row_count, lon_count, channels = inputs.shape
    lon_total = lon_count * lax.axis_size("lon")
    height = row_count * lax.axis_size("lat")
    first_row = lax.axis_index("lat") * row_count
    padded = -(-(lon_count + 2 * RIM) // 128) * 128
    weighting = quad_weight / jnp.sqrt(lon_span.astype(jnp.float32))
    first = jnp.reshape(first_row, (1,)).astype(jnp.int32)
    tables = (src_rows, lon_start, lon_span, basis_idx, weighting)

    joined = jnp.concatenate([inputs, cotangent], axis=3)
    banded = with_halo(joined, (("lat", 1),), REACH, False)
    banded, source = lax.optimization_barrier((banded, joined))
    both = with_halo(banded, (("lon", 2),), RIM, True)
    both = jnp.pad(both, ((0, 0), (0, 0), (0, padded - both.shape[2]), (0, 0)))
    sums = jnp.sum(source, axis=2, dtype=jnp.float32)
    row_sums = jnp.stack([sums[..., :channels], sums[..., channels:]])
    local_totals = ring_sum(row_sums, "lon")
    if row_count >= POLAR + REACH:
        framed = jnp.pad(local_totals, ((0, 0), (0, 0), (REACH, REACH), (0, 0)))
    else:
        framed = with_halo(local_totals, (("lat", 2),), REACH, False)
    totals, grad_totals = framed[0], framed[1]

    flattened = run_filter(first, tables, both, totals, row_count, lon_count, lon_total, False, 0)
    w_fwd = weight.reshape(BASIS * channels, channels)
    response = jnp.einsum("brwq,qo->brwo", flattened, w_fwd, preferred_element_type=jnp.float32)

    partial_value = jnp.einsum(
        "brwq,brwo->qo", flattened, cotangent, preferred_element_type=jnp.float32
    )
    partial_value = partial_value.reshape(BASIS, channels, channels)
    reduced = ring_scatter(partial_value, "lon", 2)
    w_back = jnp.transpose(weight, (0, 2, 1)).reshape(BASIS * channels, channels)

    def backward_rows(field, field_totals, lowest, count):
        back_filtered = run_scatter(
            first, tables, field, field_totals, count, lon_count, lon_total, 1, lowest
        )
        return jnp.einsum(
            "bpwq,qc->bpwc", back_filtered, w_back, preferred_element_type=jnp.float32
        )

    early_rows = row_count // 2
    early_input = backward_rows(both, grad_totals, 0, early_rows)
    both, grad_totals, reduced = lax.optimization_barrier((both, grad_totals, reduced))
    reduced = ring_scatter(reduced, "lat", 1)
    grad_input = jnp.concatenate(
        [
            early_input,
            backward_rows(both, grad_totals, early_rows, row_count - early_rows),
        ],
        axis=1,
    )
    grad_weight = reduced / jnp.sqrt(jnp.float32(members * height * lon_total))
    return (response, grad_input, grad_weight)


def solution(mesh):
    placed = (
        P("grp", "lat", "lon", None),
        P("grp", "lat", "lon", None),
        P(),
        P(),
        P(),
        P(),
        P(),
        P(),
    )
    return jax.shard_map(
        on_device,
        mesh=mesh,
        in_specs=placed,
        out_specs=(
            P("grp", "lat", "lon", None),
            P("grp", "lat", "lon", None),
            P("grp", "lat", "lon"),
        ),
        check_vma=False,
    )
```

```python
import functools

import jax
import jax.numpy as jnp
from jax import lax
from jax.experimental import pallas as pl
from jax.experimental.pallas import tpu as pltpu
from jax.sharding import PartitionSpec as P

BASIS = 9
REACH = 2
RIM = 16
POLAR = 2


def with_halo(block, sides, width, periodic):
    for axis, dim in sides:
        count = lax.axis_size(axis)
        forward = [(i, i + 1) for i in range(count - 1)]
        if periodic:
            forward.append((count - 1, 0))
        backward = [(target, source) for source, target in forward]
        low = lax.ppermute(
            lax.slice_in_dim(block, block.shape[dim] - width, None, axis=dim), axis, forward
        )
        high = lax.ppermute(lax.slice_in_dim(block, 0, width, axis=dim), axis, backward)
        block = jnp.concatenate([low, block, high], axis=dim)
    return block


def ring_sum(value, axis):
    count = lax.axis_size(axis)
    total = value
    for shift in range(1, count):
        pairs = [(i, (i + shift) % count) for i in range(count)]
        total = total + lax.ppermute(value, axis, pairs)
    return total


def ring_scatter(value, axis, dim):
    count = lax.axis_size(axis)
    own = lax.axis_index(axis)
    block = value.shape[dim] // count
    total = lax.dynamic_slice_in_dim(value, own * block, block, dim)
    for shift in range(1, count):
        pairs = [(i, (i + shift) % count) for i in range(count)]
        piece = lax.dynamic_slice_in_dim(value, ((own + shift) % count) * block, block, dim)
        sent = lax.ppermute(piece.astype(jnp.bfloat16), axis, pairs)
        total = total + sent.astype(jnp.float32)
    return total


def rolled_scatter(value, axis, dim):
    count = lax.axis_size(axis)
    block = value.shape[dim] // count
    total = lax.slice_in_dim(value, 0, block, axis=dim)
    for shift in range(1, count):
        pairs = [(i, (i + shift) % count) for i in range(count)]
        piece = lax.slice_in_dim(value, shift * block, (shift + 1) * block, axis=dim)
        sent = lax.ppermute(piece.astype(jnp.bfloat16), axis, pairs)
        total = total + sent.astype(jnp.float32)
    return total


def filter_kernel(
    first_ref, src_ref, start_ref, span_ref, basis_ref, scale_ref, field_ref, total_ref,
    out_ref, acc_ref, *, slots, height, lon_count, lon_total, backward,
):
    r = pl.program_id(1)
    first_row = first_ref[0]
    padded = field_ref.shape[2]
    channels = field_ref.shape[3]
    acc_ref[...] = jnp.zeros(acc_ref.shape, jnp.float32)
    out_col = lax.broadcasted_iota(jnp.int32, (lon_count, padded), 0)
    in_col = lax.broadcasted_iota(jnp.int32, (lon_count, padded), 1) - RIM
    offset = out_col - in_col if backward else in_col - out_col

    def add_slot(row, table_row, slot, scale):
        start = start_ref[table_row, slot]
        span = span_ref[table_row, slot]
        basis = basis_ref[table_row, slot]
        narrow = span < lon_total
        band = ((offset >= start) & (offset < start + span) & narrow).astype(jnp.bfloat16)
        boxed = jnp.dot(band, field_ref[0, row], preferred_element_type=jnp.float32)
        full = jnp.where(narrow, 0.0, 1.0).astype(jnp.float32)
        boxed = boxed + full * total_ref[0, row]
        acc_ref[basis] = acc_ref[basis] + scale * boxed

    if backward:
        target = first_row + r
        for e in range(2 * REACH + 1):
            row = r + e
            global_row = target + e - REACH
            inside = (global_row >= 0) & (global_row < height)
            table_row = jnp.clip(global_row, 0, height - 1)
            for slot in range(slots):
                scale = scale_ref[table_row, slot]
                hit = inside & (src_ref[table_row, slot] == target) & (scale != 0.0)

                @pl.when(hit)
                def _():
                    add_slot(row, table_row, slot, scale)
    else:
        table_row = first_row + r
        for slot in range(slots):
            row = src_ref[table_row, slot] - first_row + REACH
            add_slot(row, table_row, slot, scale_ref[table_row, slot])

    for k in range(BASIS):
        out_ref[0, 0, :, k * channels:(k + 1) * channels] = acc_ref[k].astype(jnp.bfloat16)


def scatter_kernel(
    first_ref, src_ref, start_ref, span_ref, basis_ref, scale_ref, field_ref, total_ref,
    out_ref, acc_ref, *, slots, height, lon_count, lon_total, lowest,
):
    first_row = first_ref[0] + lowest
    rows = out_ref.shape[1]
    window = field_ref.shape[1]
    padded = field_ref.shape[2]
    channels = field_ref.shape[3]
    acc_ref[...] = jnp.zeros(acc_ref.shape, jnp.float32)
    out_col = lax.broadcasted_iota(jnp.int32, (lon_count, padded), 0)
    in_col = lax.broadcasted_iota(jnp.int32, (lon_count, padded), 1) - RIM
    offset = out_col - in_col
    for row in range(lowest, lowest + rows + 2 * REACH):
        global_row = first_ref[0] + row - REACH
        inside = (global_row >= 0) & (global_row < height)
        table_row = jnp.clip(global_row, 0, height - 1)
        for slot in range(slots):
            target = src_ref[table_row, slot] - first_row
            scale = scale_ref[table_row, slot]
            hit = inside & (target >= 0) & (target < rows) & (scale != 0.0)

            @pl.when(hit)
            def _():
                start = start_ref[table_row, slot]
                span = span_ref[table_row, slot]
                basis = basis_ref[table_row, slot]
                narrow = span < lon_total
                band = ((offset >= start) & (offset < start + span) & narrow).astype(
                    jnp.bfloat16
                )
                boxed = jnp.dot(band, field_ref[0, row], preferred_element_type=jnp.float32)
                full = jnp.where(narrow, 0.0, 1.0).astype(jnp.float32)
                boxed = boxed + full * total_ref[0, row]
                acc_ref[target, basis] = acc_ref[target, basis] + scale * boxed

    for p in range(rows):
        for k in range(BASIS):
            out_ref[0, p, :, k * channels:(k + 1) * channels] = acc_ref[p, k].astype(
                jnp.bfloat16
            )


def run_scatter(
    first, tables, field, totals, row_count, lon_count, lon_total, part=0, lowest=0
):
    members, window, padded, combined = field.shape
    channels = totals.shape[-1]
    height, slots = tables[0].shape
    smem = pl.BlockSpec(memory_space=pltpu.SMEM)
    kernel = functools.partial(
        scatter_kernel,
        slots=slots,
        height=height,
        lon_count=lon_count,
        lon_total=lon_total,
        lowest=lowest,
    )
    return pl.pallas_call(
        kernel,
        grid=(members,),
        in_specs=[smem] * 6
        + [
            pl.BlockSpec((1, window, padded, channels), lambda b: (b, 0, 0, part)),
            pl.BlockSpec((1, window, 1, channels), lambda b: (b, 0, 0, 0)),
        ],
        out_specs=pl.BlockSpec(
            (1, row_count, lon_count, BASIS * channels), lambda b: (b, 0, 0, 0)
        ),
        out_shape=jax.ShapeDtypeStruct(
            (members, row_count, lon_count, BASIS * channels), jnp.bfloat16
        ),
        scratch_shapes=[pltpu.VMEM((row_count, BASIS, lon_count, channels), jnp.float32)],
    )(first, *tables, field, totals[:, :, None, :])


def run_filter(
    first, tables, field, totals, row_count, lon_count, lon_total, backward, part=0
):
    members, window, padded, combined = field.shape
    channels = totals.shape[-1]
    height, slots = tables[0].shape
    smem = pl.BlockSpec(memory_space=pltpu.SMEM)
    kernel = functools.partial(
        filter_kernel,
        slots=slots,
        height=height,
        lon_count=lon_count,
        lon_total=lon_total,
        backward=backward,
    )
    return pl.pallas_call(
        kernel,
        grid=(members, row_count),
        in_specs=[smem] * 6
        + [
            pl.BlockSpec((1, window, padded, channels), lambda b, r: (b, 0, 0, part)),
            pl.BlockSpec((1, window, 1, channels), lambda b, r: (b, 0, 0, 0)),
        ],
        out_specs=pl.BlockSpec(
            (1, 1, lon_count, BASIS * channels), lambda b, r: (b, r, 0, 0)
        ),
        out_shape=jax.ShapeDtypeStruct(
            (members, row_count, lon_count, BASIS * channels), jnp.bfloat16
        ),
        scratch_shapes=[pltpu.VMEM((BASIS, lon_count, channels), jnp.float32)],
    )(first, *tables, field, totals[:, :, None, :])


def on_device(inputs, cotangent, weight, src_rows, lon_start, lon_span, basis_idx, quad_weight):
    members, row_count, lon_count, channels = inputs.shape
    lon_total = lon_count * lax.axis_size("lon")
    height = row_count * lax.axis_size("lat")
    first_row = lax.axis_index("lat") * row_count
    padded = -(-(lon_count + 2 * RIM) // 128) * 128
    weighting = quad_weight / jnp.sqrt(lon_span.astype(jnp.float32))
    first = jnp.reshape(first_row, (1,)).astype(jnp.int32)
    tables = (src_rows, lon_start, lon_span, basis_idx, weighting)

    joined = jnp.concatenate([inputs, cotangent], axis=3)
    banded = with_halo(joined, (("lat", 1),), REACH, False)
    banded, source = lax.optimization_barrier((banded, joined))
    both = with_halo(banded, (("lon", 2),), RIM, True)
    both = jnp.pad(both, ((0, 0), (0, 0), (0, padded - both.shape[2]), (0, 0)))
    sums = jnp.sum(source, axis=2, dtype=jnp.float32)
    row_sums = jnp.stack([sums[..., :channels], sums[..., channels:]])
    local_totals = ring_sum(row_sums, "lon")
    if row_count >= POLAR + REACH:
        framed = jnp.pad(local_totals, ((0, 0), (0, 0), (REACH, REACH), (0, 0)))
    else:
        framed = with_halo(local_totals, (("lat", 2),), REACH, False)
    totals, grad_totals = framed[0], framed[1]

    flattened = run_filter(first, tables, both, totals, row_count, lon_count, lon_total, False, 0)
    w_fwd = weight.reshape(BASIS * channels, channels)
    response = jnp.einsum("brwq,qo->brwo", flattened, w_fwd, preferred_element_type=jnp.float32)

    o_block = channels // lax.axis_size("lon")
    rolled = jnp.roll(cotangent, -lax.axis_index("lon") * o_block, axis=3)
    partial_value = jnp.einsum(
        "brwq,brwo->qo", flattened, rolled, preferred_element_type=jnp.float32
    )
    partial_value = partial_value.reshape(BASIS, channels, channels)
    reduced = rolled_scatter(partial_value, "lon", 2)
    w_back = jnp.transpose(weight, (0, 2, 1)).reshape(BASIS * channels, channels)

    def backward_rows(field, field_totals, lowest, count):
        back_filtered = run_scatter(
            first, tables, field, field_totals, count, lon_count, lon_total, 1, lowest
        )
        return jnp.einsum(
            "bpwq,qc->bpwc", back_filtered, w_back, preferred_element_type=jnp.float32
        )

    early_rows = row_count // 2
    early_input = backward_rows(both, grad_totals, 0, early_rows)
    both, grad_totals, reduced = lax.optimization_barrier((both, grad_totals, reduced))
    reduced = ring_scatter(reduced, "lat", 1)
    grad_input = jnp.concatenate(
        [
            early_input,
            backward_rows(both, grad_totals, early_rows, row_count - early_rows),
        ],
        axis=1,
    )
    grad_weight = reduced / jnp.sqrt(jnp.float32(members * height * lon_total))
    return (response, grad_input, grad_weight)


def solution(mesh):
    placed = (
        P("grp", "lat", "lon", None),
        P("grp", "lat", "lon", None),
        P(),
        P(),
        P(),
        P(),
        P(),
        P(),
    )
    return jax.shard_map(
        on_device,
        mesh=mesh,
        in_specs=placed,
        out_specs=(
            P("grp", "lat", "lon", None),
            P("grp", "lat", "lon", None),
            P("grp", "lat", "lon"),
        ),
        check_vma=False,
    )
```

```python
import functools

import jax
import jax.numpy as jnp
from jax import lax
from jax.experimental import pallas as pl
from jax.experimental.pallas import tpu as pltpu
from jax.sharding import PartitionSpec as P

BASIS = 9
REACH = 2
RIM = 16
POLAR = 2


def with_halo(block, sides, width, periodic):
    for axis, dim in sides:
        count = lax.axis_size(axis)
        forward = [(i, i + 1) for i in range(count - 1)]
        if periodic:
            forward.append((count - 1, 0))
        backward = [(target, source) for source, target in forward]
        low = lax.ppermute(
            lax.slice_in_dim(block, block.shape[dim] - width, None, axis=dim), axis, forward
        )
        high = lax.ppermute(lax.slice_in_dim(block, 0, width, axis=dim), axis, backward)
        block = jnp.concatenate([low, block, high], axis=dim)
    return block


def ring_sum(value, axis):
    count = lax.axis_size(axis)
    total = value
    for shift in range(1, count):
        pairs = [(i, (i + shift) % count) for i in range(count)]
        total = total + lax.ppermute(value, axis, pairs)
    return total


def ring_scatter(value, axis, dim):
    count = lax.axis_size(axis)
    own = lax.axis_index(axis)
    block = value.shape[dim] // count
    total = lax.dynamic_slice_in_dim(value, own * block, block, dim)
    for shift in range(1, count):
        pairs = [(i, (i + shift) % count) for i in range(count)]
        piece = lax.dynamic_slice_in_dim(value, ((own + shift) % count) * block, block, dim)
        sent = lax.ppermute(piece.astype(jnp.bfloat16), axis, pairs)
        total = total + sent.astype(jnp.float32)
    return total


def rolled_scatter(value, axis, dim):
    count = lax.axis_size(axis)
    block = value.shape[dim] // count
    total = lax.slice_in_dim(value, 0, block, axis=dim)
    for shift in range(1, count):
        pairs = [(i, (i + shift) % count) for i in range(count)]
        piece = lax.slice_in_dim(value, shift * block, (shift + 1) * block, axis=dim)
        sent = lax.ppermute(piece.astype(jnp.bfloat16), axis, pairs)
        total = total + sent.astype(jnp.float32)
    return total


def filter_kernel(
    twist_ref, first_ref, src_ref, start_ref, span_ref, basis_ref, scale_ref, field_ref, total_ref,
    out_ref, acc_ref, *, slots, height, lon_count, lon_total, backward,
):
    r = pl.program_id(1)
    first_row = first_ref[0]
    padded = field_ref.shape[2]
    channels = field_ref.shape[3]
    acc_ref[...] = jnp.zeros(acc_ref.shape, jnp.float32)
    out_col = lax.broadcasted_iota(jnp.int32, (lon_count, padded), 0)
    in_col = lax.broadcasted_iota(jnp.int32, (lon_count, padded), 1) - RIM
    offset = out_col - in_col if backward else in_col - out_col

    def add_slot(row, table_row, slot, scale):
        start = start_ref[table_row, slot]
        span = span_ref[table_row, slot]
        basis = basis_ref[table_row, slot]
        narrow = span < lon_total
        band = ((offset >= start) & (offset < start + span) & narrow).astype(jnp.bfloat16)
        boxed = jnp.dot(band, field_ref[0, row], preferred_element_type=jnp.float32)
        full = jnp.where(narrow, 0.0, 1.0).astype(jnp.float32)
        boxed = boxed + full * total_ref[0, row]
        acc_ref[basis] = acc_ref[basis] + scale * boxed

    if backward:
        target = first_row + r
        for e in range(2 * REACH + 1):
            row = r + e
            global_row = target + e - REACH
            inside = (global_row >= 0) & (global_row < height)
            table_row = jnp.clip(global_row, 0, height - 1)
            for slot in range(slots):
                scale = scale_ref[table_row, slot]
                hit = inside & (src_ref[table_row, slot] == target) & (scale != 0.0)

                @pl.when(hit)
                def _():
                    add_slot(row, table_row, slot, scale)
    else:
        table_row = first_row + r
        for slot in range(slots):
            row = src_ref[table_row, slot] - first_row + REACH
            add_slot(row, table_row, slot, scale_ref[table_row, slot])

    twist = (channels - twist_ref[0]) % channels
    for k in range(BASIS):
        out_ref[0, 0, :, k * channels:(k + 1) * channels] = pltpu.roll(
            acc_ref[k], twist, 1
        ).astype(jnp.bfloat16)


def scatter_kernel(
    first_ref, src_ref, start_ref, span_ref, basis_ref, scale_ref, field_ref, total_ref,
    out_ref, acc_ref, *, slots, height, lon_count, lon_total, lowest,
):
    first_row = first_ref[0] + lowest
    rows = out_ref.shape[1]
    window = field_ref.shape[1]
    padded = field_ref.shape[2]
    channels = field_ref.shape[3]
    acc_ref[...] = jnp.zeros(acc_ref.shape, jnp.float32)
    out_col = lax.broadcasted_iota(jnp.int32, (lon_count, padded), 0)
    in_col = lax.broadcasted_iota(jnp.int32, (lon_count, padded), 1) - RIM
    offset = out_col - in_col
    for row in range(lowest, lowest + rows + 2 * REACH):
        global_row = first_ref[0] + row - REACH
        inside = (global_row >= 0) & (global_row < height)
        table_row = jnp.clip(global_row, 0, height - 1)
        for slot in range(slots):
            target = src_ref[table_row, slot] - first_row
            scale = scale_ref[table_row, slot]
            hit = inside & (target >= 0) & (target < rows) & (scale != 0.0)

            @pl.when(hit)
            def _():
                start = start_ref[table_row, slot]
                span = span_ref[table_row, slot]
                basis = basis_ref[table_row, slot]
                narrow = span < lon_total
                band = ((offset >= start) & (offset < start + span) & narrow).astype(
                    jnp.bfloat16
                )
                boxed = jnp.dot(band, field_ref[0, row], preferred_element_type=jnp.float32)
                full = jnp.where(narrow, 0.0, 1.0).astype(jnp.float32)
                boxed = boxed + full * total_ref[0, row]
                acc_ref[target, basis] = acc_ref[target, basis] + scale * boxed

    for p in range(rows):
        for k in range(BASIS):
            out_ref[0, p, :, k * channels:(k + 1) * channels] = acc_ref[p, k].astype(
                jnp.bfloat16
            )


def run_scatter(
    first, tables, field, totals, row_count, lon_count, lon_total, part=0, lowest=0
):
    members, window, padded, combined = field.shape
    channels = totals.shape[-1]
    height, slots = tables[0].shape
    smem = pl.BlockSpec(memory_space=pltpu.SMEM)
    kernel = functools.partial(
        scatter_kernel,
        slots=slots,
        height=height,
        lon_count=lon_count,
        lon_total=lon_total,
        lowest=lowest,
    )
    return pl.pallas_call(
        kernel,
        grid=(members,),
        in_specs=[smem] * 6
        + [
            pl.BlockSpec((1, window, padded, channels), lambda b: (b, 0, 0, part)),
            pl.BlockSpec((1, window, 1, channels), lambda b: (b, 0, 0, 0)),
        ],
        out_specs=pl.BlockSpec(
            (1, row_count, lon_count, BASIS * channels), lambda b: (b, 0, 0, 0)
        ),
        out_shape=jax.ShapeDtypeStruct(
            (members, row_count, lon_count, BASIS * channels), jnp.bfloat16
        ),
        scratch_shapes=[pltpu.VMEM((row_count, BASIS, lon_count, channels), jnp.float32)],
    )(first, *tables, field, totals[:, :, None, :])


def run_filter(
    twist, first, tables, field, totals, row_count, lon_count, lon_total, backward, part=0
):
    members, window, padded, combined = field.shape
    channels = totals.shape[-1]
    height, slots = tables[0].shape
    smem = pl.BlockSpec(memory_space=pltpu.SMEM)
    kernel = functools.partial(
        filter_kernel,
        slots=slots,
        height=height,
        lon_count=lon_count,
        lon_total=lon_total,
        backward=backward,
    )
    return pl.pallas_call(
        kernel,
        grid=(members, row_count),
        in_specs=[smem] * 7
        + [
            pl.BlockSpec((1, window, padded, channels), lambda b, r: (b, 0, 0, part)),
            pl.BlockSpec((1, window, 1, channels), lambda b, r: (b, 0, 0, 0)),
        ],
        out_specs=pl.BlockSpec(
            (1, 1, lon_count, BASIS * channels), lambda b, r: (b, r, 0, 0)
        ),
        out_shape=jax.ShapeDtypeStruct(
            (members, row_count, lon_count, BASIS * channels), jnp.bfloat16
        ),
        scratch_shapes=[pltpu.VMEM((BASIS, lon_count, channels), jnp.float32)],
    )(twist, first, *tables, field, totals[:, :, None, :])


def on_device(inputs, cotangent, weight, src_rows, lon_start, lon_span, basis_idx, quad_weight):
    members, row_count, lon_count, channels = inputs.shape
    lon_total = lon_count * lax.axis_size("lon")
    height = row_count * lax.axis_size("lat")
    first_row = lax.axis_index("lat") * row_count
    padded = -(-(lon_count + 2 * RIM) // 128) * 128
    weighting = quad_weight / jnp.sqrt(lon_span.astype(jnp.float32))
    first = jnp.reshape(first_row, (1,)).astype(jnp.int32)
    tables = (src_rows, lon_start, lon_span, basis_idx, weighting)

    joined = jnp.concatenate([inputs, cotangent], axis=3)
    banded = with_halo(joined, (("lat", 1),), REACH, False)
    banded, source = lax.optimization_barrier((banded, joined))
    both = with_halo(banded, (("lon", 2),), RIM, True)
    both = jnp.pad(both, ((0, 0), (0, 0), (0, padded - both.shape[2]), (0, 0)))
    sums = jnp.sum(source, axis=2, dtype=jnp.float32)
    row_sums = jnp.stack([sums[..., :channels], sums[..., channels:]])
    local_totals = ring_sum(row_sums, "lon")
    if row_count >= POLAR + REACH:
        framed = jnp.pad(local_totals, ((0, 0), (0, 0), (REACH, REACH), (0, 0)))
    else:
        framed = with_halo(local_totals, (("lat", 2),), REACH, False)
    totals, grad_totals = framed[0], framed[1]

    c_block = channels // lax.axis_size("lat")
    offset = lax.axis_index("lat") * c_block
    twist = jnp.reshape(offset, (1,)).astype(jnp.int32)
    flattened = run_filter(
        twist, first, tables, both, totals, row_count, lon_count, lon_total, False, 0
    )
    w_fwd = jnp.roll(weight, -offset, axis=1).reshape(BASIS * channels, channels)
    response = jnp.einsum("brwq,qo->brwo", flattened, w_fwd, preferred_element_type=jnp.float32)

    o_block = channels // lax.axis_size("lon")
    rolled = jnp.roll(cotangent, -lax.axis_index("lon") * o_block, axis=3)
    partial_value = jnp.einsum(
        "brwq,brwo->qo", flattened, rolled, preferred_element_type=jnp.float32
    )
    partial_value = partial_value.reshape(BASIS, channels, channels)
    reduced = rolled_scatter(partial_value, "lon", 2)
    w_back = jnp.transpose(weight, (0, 2, 1)).reshape(BASIS * channels, channels)

    def backward_rows(field, field_totals, lowest, count):
        back_filtered = run_scatter(
            first, tables, field, field_totals, count, lon_count, lon_total, 1, lowest
        )
        return jnp.einsum(
            "bpwq,qc->bpwc", back_filtered, w_back, preferred_element_type=jnp.float32
        )

    early_rows = row_count // 2
    early_input = backward_rows(both, grad_totals, 0, early_rows)
    both, grad_totals, reduced = lax.optimization_barrier((both, grad_totals, reduced))
    reduced = rolled_scatter(reduced, "lat", 1)
    grad_input = jnp.concatenate(
        [
            early_input,
            backward_rows(both, grad_totals, early_rows, row_count - early_rows),
        ],
        axis=1,
    )
    grad_weight = reduced / jnp.sqrt(jnp.float32(members * height * lon_total))
    return (response, grad_input, grad_weight)


def solution(mesh):
    placed = (
        P("grp", "lat", "lon", None),
        P("grp", "lat", "lon", None),
        P(),
        P(),
        P(),
        P(),
        P(),
        P(),
    )
    return jax.shard_map(
        on_device,
        mesh=mesh,
        in_specs=placed,
        out_specs=(
            P("grp", "lat", "lon", None),
            P("grp", "lat", "lon", None),
            P("grp", "lat", "lon"),
        ),
        check_vma=False,
    )
```
